32 devices in a mesh: groups: 2 (over x), dp: 16 (over z, y, core).
Axes of the slice: x: 2, y: 2, z: 4, core: 2. Of those that a mesh axis runs over, the one named last changes fastest.
Arguments:
- frames: bfloat16 [128, 256, 1536], P(('groups', 'dp')), parts along dimension 0, may hold values from -6 to 6
- cotangent: bfloat16 [128, 256, 1536], P(('groups', 'dp')), parts along dimension 0, may hold values from -6 to 6
- gain: float32 [1536], replicated, may hold values from 0.25 to 1.75
- down_weight: bfloat16 [320, 1536, 256], P('groups', 'dp'), parts along dimension 0, may hold values from -0.15625 to 0.15625
- up_weight: bfloat16 [320, 1536, 256], P('groups', 'dp'), parts along dimension 0, may hold values from -0.375 to 0.375
- slot_lang: int32 [32, 2], P('groups'), parts along dimension 0, may hold values from 0 to 159
- utt_slot: int32 [128], P('groups'), parts along dimension 0, may hold values from 0 to 1
- lengths: int32 [128], P('groups'), parts along dimension 0, may hold values from 64 to 256
Outputs:
- frame_grads: bfloat16 [128, 256, 1536], P(('groups', 'dp')), parts along dimension 0
- down_grads: bfloat16 [320, 1536, 256], P('groups', 'dp'), parts along dimension 0
- up_grads: bfloat16 [320, 1536, 256], P('groups', 'dp'), parts along dimension 0
The draws below stay inside these ranges and needn't reach their ends.
There are 2 independent parts, one for each index of `groups`. The reference program is written for one: setup_inputs(seed, part) draws one part's arguments, and reference() takes and returns one part's arrays. A program takes and returns all parts, laid end to end along the dimension named above; an argument that names none is the same for every part. Nothing has to cross between parts.
All inputs are finite; a program needn't handle non-finite values.
Results may differ from the reference program's by a relative error of at most 0.0061.
Values may be sent and summed in bfloat16 or wider, within the bound.
No kernel may reach another device: no remote copies, remote signals or barrier semaphores. Data moves between devices by JAX's collectives and lax.ppermute only.
A program may use at most 128 MiB of HBM per device.

```python
import math
import jax
import jax.numpy as jnp
import numpy as np
from jax import lax

D = 1536
R = 256
LANGS = 160
SLOTS = 2
UTT_DEV = 4
FRAMES = 256
UTTS = 64
LISTS = 16


def place_ends(entries, own_key, smallest, high):
    extent = entries.shape
    index_at = [jax.random.randint(jax.random.fold_in(own_key, axis), (), 0, extent[axis]) for axis in range(len(extent))]
    entries = entries.at[tuple(index_at)].set(smallest)
    longest = extent.index(max(extent))
    index_at[longest] = (index_at[longest] + 1) % extent[longest]
    return entries.at[tuple(index_at)].set(high)


def levels(own_key, dims, split, least, top_value):
    loudness, own = 1.0, jax.random.fold_in(own_key, 6)
    for axis_at, shards_of in split:
        steps = jnp.exp(jax.random.uniform(jax.random.fold_in(own, axis_at), (shards_of,), jnp.float32, least / len(split), top_value / len(split)))
        loudness = loudness * jnp.repeat(steps, dims[axis_at] // shards_of).reshape([-1 if axis == axis_at else 1 for axis in range(len(dims))])
    return loudness


def rank_table(count, lean):
    loads = [(1 << 20) // math.isqrt(grade ** lean) + 1 for grade in range(1, count + 1)]
    scale = 1 + sum(loads) // (1 << 30)
    return np.cumsum(np.array([max(1, weight // scale) for weight in loads]))


def ranked(stream_key, extent, number_of, skew):
    grid = rank_table(number_of, skew)
    ticket = jax.random.randint(jax.random.fold_in(stream_key, 1), extent, 0, int(grid[number_of - 1]))
    standing = jnp.searchsorted(jnp.asarray(grid, jnp.int32), ticket, side="right")
    return jax.random.permutation(jax.random.fold_in(stream_key, 2), number_of)[standing].astype(jnp.int32)


def centred(key, dims, scale, bound, shards=(), kind=jnp.bfloat16):
    level = levels(key, dims, shards, -0.22, 0.18) if shards else 1.0
    result = jax.random.normal(key, dims, jnp.float32) * scale * level
    return jnp.minimum(jnp.maximum(result, -bound), bound).astype(kind)


def setup_inputs(seed: int = 0, part: int = 0) -> dict:
    key_of = jax.random.split(jax.random.key(seed), 9)
    part_splits = jax.random.split(jax.random.fold_in(key_of[8], part), 9)
    frames = centred(part_splits[0], (UTTS, FRAMES, D), 1.0, 6.0, ((0, 16),))
    cotangent = centred(part_splits[1], (UTTS, FRAMES, D), 1.0, 6.0, ((0, 16),))
    gain = jnp.clip(1.0 + 0.15 * jax.random.normal(key_of[2], (D,), jnp.float32), 0.25, 1.75)
    down_weight = centred(part_splits[3], (LANGS, D, R), D ** -0.5, 0.15625, ((1, 16),))
    up_weight = centred(part_splits[4], (LANGS, D, R), R ** -0.5, 0.375, ((1, 16),))
    slot_lang = place_ends(ranked(part_splits[5], (LISTS, SLOTS), LANGS, 2), jax.random.fold_in(part_splits[5], 3), 0, LANGS - 1).astype(jnp.int32)
    utt_slot = place_ends(jax.random.randint(part_splits[6], (UTTS,), 0, SLOTS), jax.random.fold_in(part_splits[6], 1), 0, SLOTS - 1).astype(jnp.int32)
    lengths = place_ends(jax.random.randint(part_splits[7], (UTTS,), FRAMES // 4, FRAMES + 1), jax.random.fold_in(part_splits[7], 1), FRAMES // 4, FRAMES).astype(jnp.int32)
    return {"frames": frames, "cotangent": cotangent, "gain": gain, "down_weight": down_weight, "up_weight": up_weight, "slot_lang": slot_lang, "utt_slot": utt_slot, "lengths": lengths}


def reference(frames, cotangent, gain, down_weight, up_weight, slot_lang, utt_slot, lengths):
    owners = jnp.arange(UTTS, dtype=jnp.int32) // UTT_DEV
    utt_lang = slot_lang[owners, utt_slot]
    positions = jnp.arange(FRAMES, dtype=jnp.int32)

    def accumulate(totals, inputs):
        total_down, total_up = totals
        frame_block, upstream, language, length = inputs
        live_mask = (positions < length).astype(jnp.float32)[:, None]
        values = frame_block.astype(jnp.float32)
        centre_mean = lax.optimization_barrier(jnp.mean(values, axis=1, keepdims=True))
        mean_removed = values - centre_mean
        variance = lax.optimization_barrier(jnp.mean(mean_removed * mean_removed, axis=1, keepdims=True))
        reciprocal_deviation = lax.rsqrt(variance + 1e-06)
        standardized_input = mean_removed * reciprocal_deviation
        layer_normed = (standardized_input * gain).astype(jnp.bfloat16)
        w_down = lax.dynamic_index_in_dim(down_weight, language, 0, keepdims=False)
        w_up = lax.dynamic_index_in_dim(up_weight, language, 0, keepdims=False)
        pre_act = jnp.dot(layer_normed, w_down, preferred_element_type=jnp.float32)
        sigmoid_pre = jax.nn.sigmoid(pre_act)
        hidden = (pre_act * sigmoid_pre).astype(jnp.bfloat16)
        masked_up = (upstream.astype(jnp.float32) * live_mask).astype(jnp.bfloat16)
        grad_up = jnp.dot(masked_up.T, hidden, preferred_element_type=jnp.float32)
        d_hidden = jnp.dot(masked_up, w_up, preferred_element_type=jnp.float32)
        d_pre = (d_hidden * sigmoid_pre * (1.0 + pre_act * (1.0 - sigmoid_pre))).astype(jnp.bfloat16)
        grad_down = jnp.dot(layer_normed.T, d_pre, preferred_element_type=jnp.float32)
        d_normed = jnp.dot(d_pre, w_down.T, preferred_element_type=jnp.float32)
        scaled_rows = d_normed * gain
        inner_gradient = (scaled_rows - lax.optimization_barrier(jnp.mean(scaled_rows, axis=1, keepdims=True)) - standardized_input * lax.optimization_barrier(jnp.mean(scaled_rows * standardized_input, axis=1, keepdims=True))) * reciprocal_deviation
        d_frames = (upstream.astype(jnp.float32) + inner_gradient).astype(jnp.bfloat16)
        total_down = total_down.at[language].add(grad_down)
        total_up = total_up.at[language].add(grad_up)
        return ((total_down, total_up), d_frames)
    start = (jnp.zeros((LANGS, D, R), jnp.float32), jnp.zeros((LANGS, D, R), jnp.float32))
    (total_down, total_up), frame_grads = lax.scan(accumulate, start, (frames, cotangent, utt_lang, lengths))
    matches = utt_lang[None, :] == jnp.arange(LANGS, dtype=jnp.int32)[:, None]
    counts = lax.optimization_barrier(jnp.sum(jnp.where(matches, lengths[None, :], 0), axis=1))
    scaling = lax.rsqrt(jnp.maximum(counts, 1).astype(jnp.float32))[:, None, None]
    return (frame_grads, (total_down * scaling).astype(jnp.bfloat16), (total_up * scaling).astype(jnp.bfloat16))
```

```python
import jax
import jax.numpy as jnp
from jax import lax
from jax.sharding import PartitionSpec as P


def local_pass(frames, cotangent, gain, w_down, w_up, live_mask, slot_select):
    values = frames.astype(jnp.float32)
    centre_mean = jnp.mean(values, axis=2, keepdims=True)
    mean_removed = values - centre_mean
    variance = jnp.mean(mean_removed * mean_removed, axis=2, keepdims=True)
    reciprocal_deviation = lax.rsqrt(variance + 1e-06)
    standardized_input = mean_removed * reciprocal_deviation
    layer_normed = (standardized_input * gain).astype(jnp.bfloat16)
    pre_act = jnp.einsum("ufd,udr->ufr", layer_normed, w_down, preferred_element_type=jnp.float32)
    sigmoid_pre = jax.nn.sigmoid(pre_act)
    hidden = (pre_act * sigmoid_pre).astype(jnp.bfloat16)
    masked_up = jnp.where(live_mask, cotangent, jnp.zeros_like(cotangent))
    hidden_slots = hidden[None] * slot_select[:, :, None, None]
    grad_up = jnp.einsum("ufd,sufr->sdr", masked_up, hidden_slots, preferred_element_type=jnp.float32)
    d_hidden = jnp.einsum("ufd,udr->ufr", masked_up, w_up, preferred_element_type=jnp.float32)
    d_pre = (d_hidden * sigmoid_pre * (1.0 + pre_act * (1.0 - sigmoid_pre))).astype(jnp.bfloat16)
    d_pre_slots = d_pre[None] * slot_select[:, :, None, None]
    grad_down = jnp.einsum("ufd,sufr->sdr", layer_normed, d_pre_slots, preferred_element_type=jnp.float32)
    d_normed = jnp.einsum("ufr,udr->ufd", d_pre, w_down, preferred_element_type=jnp.float32)
    scaled_rows = d_normed * gain
    inner_gradient = (
        scaled_rows
        - jnp.mean(scaled_rows, axis=2, keepdims=True)
        - standardized_input * jnp.mean(scaled_rows * standardized_input, axis=2, keepdims=True)
    ) * reciprocal_deviation
    d_frames = (cotangent.astype(jnp.float32) + inner_gradient).astype(jnp.bfloat16)
    return (d_frames, grad_down, grad_up)


def on_device(frames, cotangent, gain, down_weight, up_weight, slot_lang, utt_slot, lengths):
    devices = lax.axis_size("dp")
    self_index = lax.axis_index("dp")
    per_device = frames.shape[0]
    slots = slot_lang.shape[1]
    lang_count, row_count, bottleneck = down_weight.shape
    owners = jnp.arange(utt_slot.shape[0], dtype=jnp.int32) // per_device
    utt_lang = slot_lang[owners, utt_slot]
    own_lengths = lax.dynamic_slice_in_dim(lengths, self_index * per_device, per_device)
    own_slot = lax.dynamic_slice_in_dim(utt_slot, self_index * per_device, per_device)
    live_mask = (jnp.arange(frames.shape[1], dtype=jnp.int32)[None, :] < own_lengths[:, None])[
        :, :, None
    ]
    list_langs = slot_lang.reshape(-1)
    send_down = jnp.take(down_weight, list_langs, axis=0).reshape(
        devices, slots, row_count, bottleneck
    )
    send_up = jnp.take(up_weight, list_langs, axis=0).reshape(
        devices, slots, row_count, bottleneck
    )
    got_down = lax.all_to_all(send_down, "dp", split_axis=0, concat_axis=2, tiled=True)[0]
    got_up = lax.all_to_all(send_up, "dp", split_axis=0, concat_axis=2, tiled=True)[0]
    w_down = jnp.take(got_down, own_slot, axis=0)
    w_up = jnp.take(got_up, own_slot, axis=0)
    slot_select = (jnp.arange(slots, dtype=jnp.int32)[:, None] == own_slot[None, :]).astype(
        jnp.bfloat16
    )
    d_frames, grad_down, grad_up = local_pass(
        frames, cotangent, gain, w_down, w_up, live_mask, slot_select
    )
    back_down = lax.all_to_all(grad_down[None], "dp", split_axis=2, concat_axis=0, tiled=True)
    back_up = lax.all_to_all(grad_up[None], "dp", split_axis=2, concat_axis=0, tiled=True)
    members = devices * slots
    lang_ids = jnp.arange(lang_count, dtype=jnp.int32)
    lang_table = (lang_ids[:, None] == list_langs[None, :]).astype(jnp.float32)
    sum_down = jnp.dot(
        lang_table,
        back_down.reshape(members, row_count * bottleneck),
        precision=lax.Precision.HIGHEST,
    )
    sum_up = jnp.dot(
        lang_table,
        back_up.reshape(members, row_count * bottleneck),
        precision=lax.Precision.HIGHEST,
    )
    counts = jnp.sum(jnp.where(utt_lang[None, :] == lang_ids[:, None], lengths[None, :], 0), axis=1)
    scaling = lax.rsqrt(jnp.maximum(counts, 1).astype(jnp.float32))[:, None]
    down_grads = (
        (sum_down * scaling).reshape(lang_count, row_count, bottleneck).astype(jnp.bfloat16)
    )
    up_grads = (sum_up * scaling).reshape(lang_count, row_count, bottleneck).astype(jnp.bfloat16)
    return (d_frames, down_grads, up_grads)


def solution(mesh):
    placed = (
        P(("groups", "dp"), None, None),
        P(("groups", "dp"), None, None),
        P(),
        P("groups", "dp", None),
        P("groups", "dp", None),
        P("groups", None),
        P("groups"),
        P("groups"),
    )
    return jax.shard_map(
        on_device,
        mesh=mesh,
        in_specs=placed,
        out_specs=(
            P(("groups", "dp"), None, None),
            P("groups", "dp", None),
            P("groups", "dp", None),
        ),
        check_vma=False,
    )
```

```python
import jax
import jax.numpy as jnp
from jax import lax
from jax.sharding import PartitionSpec as P


def local_pass(frames, cotangent, gain, w_down, w_up, live_mask, slot_select):
    values = frames.astype(jnp.float32)
    centre_mean = jnp.mean(values, axis=2, keepdims=True)
    mean_removed = values - centre_mean
    variance = jnp.mean(mean_removed * mean_removed, axis=2, keepdims=True)
    reciprocal_deviation = lax.rsqrt(variance + 1e-06)
    standardized_input = mean_removed * reciprocal_deviation
    layer_normed = (standardized_input * gain).astype(jnp.bfloat16)
    pre_act = jnp.einsum("ufd,udr->ufr", layer_normed, w_down, preferred_element_type=jnp.float32)
    sigmoid_pre = jax.nn.sigmoid(pre_act)
    hidden = (pre_act * sigmoid_pre).astype(jnp.bfloat16)
    masked_up = jnp.where(live_mask, cotangent, jnp.zeros_like(cotangent))
    hidden_slots = hidden[None] * slot_select[:, :, None, None]
    grad_up = jnp.einsum("ufd,sufr->sdr", masked_up, hidden_slots, preferred_element_type=jnp.float32)
    d_hidden = jnp.einsum("ufd,udr->ufr", masked_up, w_up, preferred_element_type=jnp.float32)
    d_pre = (d_hidden * sigmoid_pre * (1.0 + pre_act * (1.0 - sigmoid_pre))).astype(jnp.bfloat16)
    d_pre_slots = d_pre[None] * slot_select[:, :, None, None]
    grad_down = jnp.einsum("ufd,sufr->sdr", layer_normed, d_pre_slots, preferred_element_type=jnp.float32)
    d_normed = jnp.einsum("ufr,udr->ufd", d_pre, w_down, preferred_element_type=jnp.float32)
    scaled_rows = d_normed * gain
    inner_gradient = (
        scaled_rows
        - jnp.mean(scaled_rows, axis=2, keepdims=True)
        - standardized_input * jnp.mean(scaled_rows * standardized_input, axis=2, keepdims=True)
    ) * reciprocal_deviation
    d_frames = (cotangent.astype(jnp.float32) + inner_gradient).astype(jnp.bfloat16)
    return (d_frames, grad_down, grad_up)


def on_device(frames, cotangent, gain, down_weight, up_weight, slot_lang, utt_slot, lengths):
    devices = lax.axis_size("dp")
    self_index = lax.axis_index("dp")
    per_device = frames.shape[0]
    slots = slot_lang.shape[1]
    lang_count, row_count, bottleneck = down_weight.shape
    owners = jnp.arange(utt_slot.shape[0], dtype=jnp.int32) // per_device
    utt_lang = slot_lang[owners, utt_slot]
    own_lengths = lax.dynamic_slice_in_dim(lengths, self_index * per_device, per_device)
    own_slot = lax.dynamic_slice_in_dim(utt_slot, self_index * per_device, per_device)
    live_mask = (jnp.arange(frames.shape[1], dtype=jnp.int32)[None, :] < own_lengths[:, None])[
        :, :, None
    ]
    lang_ids = jnp.arange(lang_count, dtype=jnp.int32)
    counts = jnp.sum(jnp.where(utt_lang[None, :] == lang_ids[:, None], lengths[None, :], 0), axis=1)
    scaling = lax.rsqrt(jnp.maximum(counts, 1).astype(jnp.float32))
    member_langs = slot_lang.T.reshape(-1)
    send_down = jnp.take(down_weight, member_langs, axis=0).reshape(
        slots, devices, row_count, bottleneck
    )
    send_up = jnp.take(up_weight, member_langs, axis=0).reshape(
        slots, devices, row_count, bottleneck
    )
    got_down = lax.all_to_all(send_down, "dp", split_axis=1, concat_axis=1, tiled=True)
    got_up = lax.all_to_all(send_up, "dp", split_axis=1, concat_axis=1, tiled=True)
    got_down = got_down.reshape(slots, devices * row_count, bottleneck)
    got_up = got_up.reshape(slots, devices * row_count, bottleneck)
    w_down = jnp.take(got_down, own_slot, axis=0)
    w_up = jnp.take(got_up, own_slot, axis=0)
    slot_select = (jnp.arange(slots, dtype=jnp.int32)[:, None] == own_slot[None, :]).astype(
        jnp.bfloat16
    )
    d_frames, grad_down, grad_up = local_pass(
        frames, cotangent, gain, w_down, w_up, live_mask, slot_select
    )
    own_scale = jnp.take(scaling, lax.dynamic_index_in_dim(slot_lang, self_index, 0, False))
    own_scale = own_scale[:, None, None]

    def exchange_back(grad):
        scaled = (grad * own_scale).astype(jnp.bfloat16)
        scaled = scaled.reshape(slots, devices, row_count, bottleneck)
        back = lax.all_to_all(scaled, "dp", split_axis=1, concat_axis=1, tiled=True)
        return back.reshape(slots * devices, row_count, bottleneck)

    back_down = exchange_back(grad_down)
    back_up = exchange_back(grad_up)
    lang_table = (lang_ids[:, None] == member_langs[None, :]).astype(jnp.bfloat16)
    down_grads = jnp.einsum(
        "lm,mkr->lkr", lang_table, back_down, preferred_element_type=jnp.float32
    ).astype(jnp.bfloat16)
    up_grads = jnp.einsum(
        "lm,mkr->lkr", lang_table, back_up, preferred_element_type=jnp.float32
    ).astype(jnp.bfloat16)
    return (d_frames, down_grads, up_grads)


def solution(mesh):
    placed = (
        P(("groups", "dp"), None, None),
        P(("groups", "dp"), None, None),
        P(),
        P("groups", "dp", None),
        P("groups", "dp", None),
        P("groups", None),
        P("groups"),
        P("groups"),
    )
    return jax.shard_map(
        on_device,
        mesh=mesh,
        in_specs=placed,
        out_specs=(
            P(("groups", "dp"), None, None),
            P("groups", "dp", None),
            P("groups", "dp", None),
        ),
        check_vma=False,
    )
```

```python
import jax
import jax.numpy as jnp
from jax import lax
from jax.sharding import PartitionSpec as P


def local_pass(frames, cotangent, gain, w_down, w_up, live_mask, slot_select):
    values = frames.astype(jnp.float32)
    centre_mean = jnp.mean(values, axis=2, keepdims=True)
    mean_removed = values - centre_mean
    variance = jnp.mean(mean_removed * mean_removed, axis=2, keepdims=True)
    reciprocal_deviation = lax.rsqrt(variance + 1e-06)
    standardized_input = mean_removed * reciprocal_deviation
    layer_normed = (standardized_input * gain).astype(jnp.bfloat16)
    pre_act = jnp.einsum("ufd,udr->ufr", layer_normed, w_down, preferred_element_type=jnp.float32)
    sigmoid_pre = jax.nn.sigmoid(pre_act)
    hidden = (pre_act * sigmoid_pre).astype(jnp.bfloat16)
    masked_up = jnp.where(live_mask, cotangent, jnp.zeros_like(cotangent))
    hidden_slots = hidden[None] * slot_select[:, :, None, None]
    grad_up = jnp.einsum("ufd,sufr->sdr", masked_up, hidden_slots, preferred_element_type=jnp.float32)
    d_hidden = jnp.einsum("ufd,udr->ufr", masked_up, w_up, preferred_element_type=jnp.float32)
    d_pre = (d_hidden * sigmoid_pre * (1.0 + pre_act * (1.0 - sigmoid_pre))).astype(jnp.bfloat16)
    d_pre_slots = d_pre[None] * slot_select[:, :, None, None]
    grad_down = jnp.einsum("ufd,sufr->sdr", layer_normed, d_pre_slots, preferred_element_type=jnp.float32)
    d_normed = jnp.einsum("ufr,udr->ufd", d_pre, w_down, preferred_element_type=jnp.float32)
    scaled_rows = d_normed * gain
    inner_gradient = (
        scaled_rows
        - jnp.mean(scaled_rows, axis=2, keepdims=True)
        - standardized_input * jnp.mean(scaled_rows * standardized_input, axis=2, keepdims=True)
    ) * reciprocal_deviation
    d_frames = (cotangent.astype(jnp.float32) + inner_gradient).astype(jnp.bfloat16)
    return (d_frames, grad_down, grad_up)


def on_device(frames, cotangent, gain, down_weight, up_weight, slot_lang, utt_slot, lengths):
    devices = lax.axis_size("dp")
    self_index = lax.axis_index("dp")
    per_device = frames.shape[0]
    slots = slot_lang.shape[1]
    lang_count, row_count, bottleneck = down_weight.shape
    owners = jnp.arange(utt_slot.shape[0], dtype=jnp.int32) // per_device
    utt_lang = slot_lang[owners, utt_slot]
    own_lengths = lax.dynamic_slice_in_dim(lengths, self_index * per_device, per_device)
    own_slot = lax.dynamic_slice_in_dim(utt_slot, self_index * per_device, per_device)
    live_mask = (jnp.arange(frames.shape[1], dtype=jnp.int32)[None, :] < own_lengths[:, None])[
        :, :, None
    ]
    lang_ids = jnp.arange(lang_count, dtype=jnp.int32)
    counts = jnp.sum(jnp.where(utt_lang[None, :] == lang_ids[:, None], lengths[None, :], 0), axis=1)
    scaling = lax.rsqrt(jnp.maximum(counts, 1).astype(jnp.float32))
    member_langs = slot_lang.reshape(-1)
    send_down = jnp.take(down_weight, member_langs, axis=0).reshape(
        devices, slots, row_count, bottleneck
    )
    send_up = jnp.take(up_weight, member_langs, axis=0).reshape(
        devices, slots, row_count, bottleneck
    )
    sent = jnp.concatenate([send_down, send_up], axis=1)
    got = lax.all_to_all(sent, "dp", split_axis=0, concat_axis=0, tiled=True)

    def own_rows(offset):
        rows = jnp.take(got, own_slot + offset, axis=1)
        return rows.transpose(1, 0, 2, 3).reshape(per_device, devices * row_count, bottleneck)

    w_down = own_rows(0)
    w_up = own_rows(slots)
    slot_select = (jnp.arange(slots, dtype=jnp.int32)[:, None] == own_slot[None, :]).astype(
        jnp.bfloat16
    )
    d_frames, grad_down, grad_up = local_pass(
        frames, cotangent, gain, w_down, w_up, live_mask, slot_select
    )
    own_scale = jnp.take(scaling, lax.dynamic_index_in_dim(slot_lang, self_index, 0, False))
    own_scale = own_scale[:, None, None]
    grads = jnp.concatenate([grad_down * own_scale, grad_up * own_scale], axis=0)
    grads = grads.astype(jnp.bfloat16).reshape(2 * slots, devices, row_count, bottleneck)
    back = lax.all_to_all(
        grads.transpose(1, 0, 2, 3), "dp", split_axis=0, concat_axis=0, tiled=True
    ).reshape(devices * 2 * slots, row_count, bottleneck)
    both_langs = jnp.concatenate([slot_lang, slot_lang], axis=1).reshape(-1)
    is_down = (jnp.arange(2 * slots, dtype=jnp.int32) < slots)[None, :]
    is_down = jnp.broadcast_to(is_down, (devices, 2 * slots)).reshape(-1)
    matches = lang_ids[:, None] == both_langs[None, :]
    down_table = (matches & is_down[None, :]).astype(jnp.bfloat16)
    up_table = (matches & ~is_down[None, :]).astype(jnp.bfloat16)
    down_grads = jnp.einsum(
        "lm,mkr->lkr", down_table, back, preferred_element_type=jnp.float32
    ).astype(jnp.bfloat16)
    up_grads = jnp.einsum(
        "lm,mkr->lkr", up_table, back, preferred_element_type=jnp.float32
    ).astype(jnp.bfloat16)
    return (d_frames, down_grads, up_grads)


def solution(mesh):
    placed = (
        P(("groups", "dp"), None, None),
        P(("groups", "dp"), None, None),
        P(),
        P("groups", "dp", None),
        P("groups", "dp", None),
        P("groups", None),
        P("groups"),
        P("groups"),
    )
    return jax.shard_map(
        on_device,
        mesh=mesh,
        in_specs=placed,
        out_specs=(
            P(("groups", "dp"), None, None),
            P("groups", "dp", None),
            P("groups", "dp", None),
        ),
        check_vma=False,
    )
```

```python
import functools

import jax
import jax.numpy as jnp
from jax import lax
from jax.experimental import pallas as pl
from jax.experimental.pallas import tpu as pltpu
from jax.sharding import PartitionSpec as P


def adapter_kernel(slot_ref, len_ref, frames_ref, cot_ref, gain_ref, wd_ref, wu_ref,
                   out_ref, gd_ref, gu_ref):
    u = pl.program_id(0)

    @pl.when(u == 0)
    def _():
        gd_ref[...] = jnp.zeros_like(gd_ref)
        gu_ref[...] = jnp.zeros_like(gu_ref)

    slot = slot_ref[u]
    length = len_ref[u]
    gain = gain_ref[...]
    values = frames_ref[0].astype(jnp.float32)
    centre_mean = jnp.mean(values, axis=1, keepdims=True)
    mean_removed = values - centre_mean
    variance = jnp.mean(mean_removed * mean_removed, axis=1, keepdims=True)
    reciprocal_deviation = lax.rsqrt(variance + 1e-06)
    standardized_input = mean_removed * reciprocal_deviation
    layer_normed = (standardized_input * gain).astype(jnp.bfloat16)
    w_down = wd_ref[0]
    w_up = wu_ref[0]
    pre_act = jnp.dot(layer_normed, w_down, preferred_element_type=jnp.float32)
    sigmoid_pre = 1.0 / (1.0 + jnp.exp(-pre_act))
    hidden = (pre_act * sigmoid_pre).astype(jnp.bfloat16)
    upstream = cot_ref[0]
    live = lax.broadcasted_iota(jnp.int32, (upstream.shape[0], 1), 0) < length
    masked_up = jnp.where(live, upstream, jnp.zeros_like(upstream))
    contract_rows = (((0,), (0,)), ((), ()))
    gu_ref[slot] += lax.dot_general(
        masked_up, hidden, contract_rows, preferred_element_type=jnp.float32
    )
    d_hidden = jnp.dot(masked_up, w_up, preferred_element_type=jnp.float32)
    d_pre = (d_hidden * sigmoid_pre * (1.0 + pre_act * (1.0 - sigmoid_pre))).astype(jnp.bfloat16)
    gd_ref[slot] += lax.dot_general(
        layer_normed, d_pre, contract_rows, preferred_element_type=jnp.float32
    )
    d_normed = lax.dot_general(
        d_pre, w_down, (((1,), (1,)), ((), ())), preferred_element_type=jnp.float32
    )
    scaled_rows = d_normed * gain
    inner_gradient = (
        scaled_rows
        - jnp.mean(scaled_rows, axis=1, keepdims=True)
        - standardized_input * jnp.mean(scaled_rows * standardized_input, axis=1, keepdims=True)
    ) * reciprocal_deviation
    out_ref[0] = (upstream.astype(jnp.float32) + inner_gradient).astype(out_ref.dtype)


def local_pass(frames, cotangent, gain, weights, own_slot, own_lengths, slots):
    utts, frame_count, width = frames.shape
    bottleneck = weights.shape[2]
    flops = 10 * utts * frame_count * width * bottleneck
    moved = 3 * frames.size * 2 + 2 * utts * width * bottleneck * 2 + 4 * slots * width * bottleneck * 4
    grid_spec = pltpu.PrefetchScalarGridSpec(
        num_scalar_prefetch=2,
        grid=(utts,),
        in_specs=[
            pl.BlockSpec((1, frame_count, width), lambda u, sl, ln: (u, 0, 0)),
            pl.BlockSpec((1, frame_count, width), lambda u, sl, ln: (u, 0, 0)),
            pl.BlockSpec((1, width), lambda u, sl, ln: (0, 0)),
            pl.BlockSpec((1, width, bottleneck), lambda u, sl, ln: (sl[u], 0, 0)),
            pl.BlockSpec((1, width, bottleneck), lambda u, sl, ln: (sl[u] + slots, 0, 0)),
        ],
        out_specs=[
            pl.BlockSpec((1, frame_count, width), lambda u, sl, ln: (u, 0, 0)),
            pl.BlockSpec((slots, width, bottleneck), lambda u, sl, ln: (0, 0, 0)),
            pl.BlockSpec((slots, width, bottleneck), lambda u, sl, ln: (0, 0, 0)),
        ],
    )
    return pl.pallas_call(
        adapter_kernel,
        grid_spec=grid_spec,
        out_shape=[
            jax.ShapeDtypeStruct(frames.shape, jnp.bfloat16),
            jax.ShapeDtypeStruct((slots, width, bottleneck), jnp.float32),
            jax.ShapeDtypeStruct((slots, width, bottleneck), jnp.float32),
        ],
        compiler_params=pltpu.CompilerParams(
            dimension_semantics=("arbitrary",), vmem_limit_bytes=60 * 1024 * 1024
        ),
        cost_estimate=pl.CostEstimate(flops=flops, bytes_accessed=moved, transcendentals=utts * frame_count * bottleneck),
    )(own_slot, own_lengths, frames, cotangent, gain.reshape(1, width), weights, weights)


def on_device(frames, cotangent, gain, down_weight, up_weight, slot_lang, utt_slot, lengths):
    devices = lax.axis_size("dp")
    self_index = lax.axis_index("dp")
    per_device = frames.shape[0]
    slots = slot_lang.shape[1]
    lang_count, row_count, bottleneck = down_weight.shape
    owners = jnp.arange(utt_slot.shape[0], dtype=jnp.int32) // per_device
    utt_lang = slot_lang[owners, utt_slot]
    own_lengths = lax.dynamic_slice_in_dim(lengths, self_index * per_device, per_device)
    own_slot = lax.dynamic_slice_in_dim(utt_slot, self_index * per_device, per_device)
    live_mask = (jnp.arange(frames.shape[1], dtype=jnp.int32)[None, :] < own_lengths[:, None])[
        :, :, None
    ]
    lang_ids = jnp.arange(lang_count, dtype=jnp.int32)
    counts = jnp.sum(jnp.where(utt_lang[None, :] == lang_ids[:, None], lengths[None, :], 0), axis=1)
    scaling = lax.rsqrt(jnp.maximum(counts, 1).astype(jnp.float32))
    member_langs = slot_lang.reshape(-1)
    send_down = jnp.take(down_weight, member_langs, axis=0).reshape(
        devices, slots, row_count, bottleneck
    )
    send_up = jnp.take(up_weight, member_langs, axis=0).reshape(
        devices, slots, row_count, bottleneck
    )
    sent = jnp.concatenate([send_down, send_up], axis=1)
    got = lax.all_to_all(sent, "dp", split_axis=0, concat_axis=0, tiled=True)

    weights = got.transpose(1, 0, 2, 3).reshape(2 * slots, devices * row_count, bottleneck)
    d_frames, grad_down, grad_up = local_pass(
        frames, cotangent, gain, weights, own_slot, own_lengths, slots
    )
    own_scale = jnp.take(scaling, lax.dynamic_index_in_dim(slot_lang, self_index, 0, False))
    own_scale = own_scale[:, None, None]
    lang_table = (lang_ids[:, None] == member_langs[None, :]).astype(jnp.bfloat16)

    def exchange_back(grad):
        scaled = (grad * own_scale).astype(jnp.bfloat16)
        scaled = scaled.reshape(slots, devices, row_count, bottleneck).transpose(1, 0, 2, 3)
        back = lax.all_to_all(scaled, "dp", split_axis=0, concat_axis=0, tiled=True)
        back = back.reshape(devices * slots, row_count, bottleneck)
        return jnp.einsum(
            "lm,mkr->lkr", lang_table, back, preferred_element_type=jnp.float32
        ).astype(jnp.bfloat16)

    down_grads = exchange_back(grad_down)
    up_grads = exchange_back(grad_up)
    return (d_frames, down_grads, up_grads)


def solution(mesh):
    placed = (
        P(("groups", "dp"), None, None),
        P(("groups", "dp"), None, None),
        P(),
        P("groups", "dp", None),
        P("groups", "dp", None),
        P("groups", None),
        P("groups"),
        P("groups"),
    )
    return jax.shard_map(
        on_device,
        mesh=mesh,
        in_specs=placed,
        out_specs=(
            P(("groups", "dp"), None, None),
            P("groups", "dp", None),
            P("groups", "dp", None),
        ),
        check_vma=False,
    )
```

```python
import functools

import jax
import jax.numpy as jnp
from jax import lax
from jax.experimental import pallas as pl
from jax.experimental.pallas import tpu as pltpu
from jax.sharding import PartitionSpec as P


def adapter_kernel(slot_ref, len_ref, frames_ref, cot_ref, gain_ref, wd_ref, wu_ref, scale_ref,
                   out_ref, gd_out, gu_out, gd_ref, gu_ref):
    u = pl.program_id(0)

    @pl.when(u == 0)
    def _():
        gd_ref[...] = jnp.zeros_like(gd_ref)
        gu_ref[...] = jnp.zeros_like(gu_ref)

    slot = slot_ref[u]
    length = len_ref[u]
    gain = gain_ref[...]
    values = frames_ref[0].astype(jnp.float32)
    centre_mean = jnp.mean(values, axis=1, keepdims=True)
    mean_removed = values - centre_mean
    variance = jnp.mean(mean_removed * mean_removed, axis=1, keepdims=True)
    reciprocal_deviation = lax.rsqrt(variance + 1e-06)
    standardized_input = mean_removed * reciprocal_deviation
    layer_normed = (standardized_input * gain).astype(jnp.bfloat16)
    w_down = wd_ref[0]
    w_up = wu_ref[0]
    pre_act = jnp.dot(layer_normed, w_down, preferred_element_type=jnp.float32)
    sigmoid_pre = 1.0 / (1.0 + jnp.exp(-pre_act))
    hidden = (pre_act * sigmoid_pre).astype(jnp.bfloat16)
    upstream = cot_ref[0]
    live = lax.broadcasted_iota(jnp.int32, (upstream.shape[0], 1), 0) < length
    masked_up = jnp.where(live, upstream, jnp.zeros_like(upstream))
    contract_rows = (((0,), (0,)), ((), ()))
    gu_ref[slot] += lax.dot_general(
        masked_up, hidden, contract_rows, preferred_element_type=jnp.float32
    )
    d_hidden = jnp.dot(masked_up, w_up, preferred_element_type=jnp.float32)
    d_pre = (d_hidden * sigmoid_pre * (1.0 + pre_act * (1.0 - sigmoid_pre))).astype(jnp.bfloat16)
    gd_ref[slot] += lax.dot_general(
        layer_normed, d_pre, contract_rows, preferred_element_type=jnp.float32
    )
    d_normed = lax.dot_general(
        d_pre, w_down, (((1,), (1,)), ((), ())), preferred_element_type=jnp.float32
    )
    scaled_rows = d_normed * gain
    inner_gradient = (
        scaled_rows
        - jnp.mean(scaled_rows, axis=1, keepdims=True)
        - standardized_input * jnp.mean(scaled_rows * standardized_input, axis=1, keepdims=True)
    ) * reciprocal_deviation
    out_ref[0] = (upstream.astype(jnp.float32) + inner_gradient).astype(out_ref.dtype)

    @pl.when(u == pl.num_programs(0) - 1)
    def _():
        gd_out[...] = (gd_ref[...] * scale_ref[...]).astype(gd_out.dtype)
        gu_out[...] = (gu_ref[...] * scale_ref[...]).astype(gu_out.dtype)


def combine_kernel(lang_ref, back_ref, out_ref, acc_ref):
    block = out_ref.shape[0]
    base = pl.program_id(0) * block
    acc_ref[...] = jnp.zeros_like(acc_ref)

    def add_member(m, carry):
        local = lang_ref[m] - base

        @pl.when((local >= 0) & (local < block))
        def _():
            acc_ref[local] += back_ref[m].astype(jnp.float32)

        return carry

    lax.fori_loop(0, back_ref.shape[0], add_member, 0)
    out_ref[...] = acc_ref[...].astype(out_ref.dtype)


def combine(member_langs, back, lang_count):
    members, row_count, bottleneck = back.shape
    block = 16 if lang_count % 16 == 0 else (8 if lang_count % 8 == 0 else 1)
    grid_spec = pltpu.PrefetchScalarGridSpec(
        num_scalar_prefetch=1,
        grid=(lang_count // block,),
        in_specs=[pl.BlockSpec((members, row_count, bottleneck), lambda b, ml: (0, 0, 0))],
        out_specs=pl.BlockSpec((block, row_count, bottleneck), lambda b, ml: (b, 0, 0)),
        scratch_shapes=[pltpu.VMEM((block, row_count, bottleneck), jnp.float32)],
    )
    return pl.pallas_call(
        combine_kernel,
        grid_spec=grid_spec,
        out_shape=jax.ShapeDtypeStruct((lang_count, row_count, bottleneck), jnp.bfloat16),
        compiler_params=pltpu.CompilerParams(dimension_semantics=("arbitrary",)),
        cost_estimate=pl.CostEstimate(
            flops=back.size, bytes_accessed=back.size * 2 + lang_count * row_count * bottleneck * 2,
            transcendentals=0,
        ),
    )(member_langs, back)


def local_pass(frames, cotangent, gain, weights, own_slot, own_lengths, slots, own_scale):
    utts, frame_count, width = frames.shape
    bottleneck = weights.shape[2]
    flops = 10 * utts * frame_count * width * bottleneck
    moved = 3 * frames.size * 2 + 2 * utts * width * bottleneck * 2 + 4 * slots * width * bottleneck * 4
    grid_spec = pltpu.PrefetchScalarGridSpec(
        num_scalar_prefetch=2,
        grid=(utts,),
        in_specs=[
            pl.BlockSpec((1, frame_count, width), lambda u, sl, ln: (u, 0, 0)),
            pl.BlockSpec((1, frame_count, width), lambda u, sl, ln: (u, 0, 0)),
            pl.BlockSpec((1, width), lambda u, sl, ln: (0, 0)),
            pl.BlockSpec((1, width, bottleneck), lambda u, sl, ln: (sl[u], 0, 0)),
            pl.BlockSpec((1, width, bottleneck), lambda u, sl, ln: (sl[u] + slots, 0, 0)),
            pl.BlockSpec((slots, 1, 1), lambda u, sl, ln: (0, 0, 0)),
        ],
        out_specs=[
            pl.BlockSpec((1, frame_count, width), lambda u, sl, ln: (u, 0, 0)),
            pl.BlockSpec((slots, width, bottleneck), lambda u, sl, ln: (0, 0, 0)),
            pl.BlockSpec((slots, width, bottleneck), lambda u, sl, ln: (0, 0, 0)),
        ],
        scratch_shapes=[
            pltpu.VMEM((slots, width, bottleneck), jnp.float32),
            pltpu.VMEM((slots, width, bottleneck), jnp.float32),
        ],
    )
    return pl.pallas_call(
        adapter_kernel,
        grid_spec=grid_spec,
        out_shape=[
            jax.ShapeDtypeStruct(frames.shape, jnp.bfloat16),
            jax.ShapeDtypeStruct((slots, width, bottleneck), jnp.bfloat16),
            jax.ShapeDtypeStruct((slots, width, bottleneck), jnp.bfloat16),
        ],

        compiler_params=pltpu.CompilerParams(
            dimension_semantics=("arbitrary",), vmem_limit_bytes=60 * 1024 * 1024
        ),
        cost_estimate=pl.CostEstimate(flops=flops, bytes_accessed=moved, transcendentals=utts * frame_count * bottleneck),
    )(own_slot, own_lengths, frames, cotangent, gain.reshape(1, width), weights, weights,
      own_scale.reshape(slots, 1, 1))


def on_device(frames, cotangent, gain, down_weight, up_weight, slot_lang, utt_slot, lengths):
    devices = lax.axis_size("dp")
    self_index = lax.axis_index("dp")
    per_device = frames.shape[0]
    slots = slot_lang.shape[1]
    lang_count, row_count, bottleneck = down_weight.shape
    owners = jnp.arange(utt_slot.shape[0], dtype=jnp.int32) // per_device
    utt_lang = slot_lang[owners, utt_slot]
    own_lengths = lax.dynamic_slice_in_dim(lengths, self_index * per_device, per_device)
    own_slot = lax.dynamic_slice_in_dim(utt_slot, self_index * per_device, per_device)
    lang_ids = jnp.arange(lang_count, dtype=jnp.int32)
    counts = jnp.sum(jnp.where(utt_lang[None, :] == lang_ids[:, None], lengths[None, :], 0), axis=1)
    scaling = lax.rsqrt(jnp.maximum(counts, 1).astype(jnp.float32))
    member_langs = slot_lang.reshape(-1)
    send_down = jnp.take(down_weight, member_langs, axis=0).reshape(
        devices, slots, row_count, bottleneck
    )
    send_up = jnp.take(up_weight, member_langs, axis=0).reshape(
        devices, slots, row_count, bottleneck
    )
    sent = jnp.concatenate([send_down, send_up], axis=1)
    got = lax.all_to_all(sent, "dp", split_axis=0, concat_axis=0, tiled=True)

    weights = got.transpose(1, 0, 2, 3).reshape(2 * slots, devices * row_count, bottleneck)
    own_scale = jnp.take(scaling, lax.dynamic_index_in_dim(slot_lang, self_index, 0, False))
    d_frames, grad_down, grad_up = local_pass(
        frames, cotangent, gain, weights, own_slot, own_lengths, slots, own_scale
    )

    def exchange_back(grad):
        scaled = grad.reshape(slots, devices, row_count, bottleneck).transpose(1, 0, 2, 3)
        back = lax.all_to_all(scaled, "dp", split_axis=0, concat_axis=0, tiled=True)
        return combine(member_langs, back.reshape(devices * slots, row_count, bottleneck), lang_count)

    down_grads = exchange_back(grad_down)
    up_grads = exchange_back(grad_up)
    return (d_frames, down_grads, up_grads)


def solution(mesh):
    placed = (
        P(("groups", "dp"), None, None),
        P(("groups", "dp"), None, None),
        P(),
        P("groups", "dp", None),
        P("groups", "dp", None),
        P("groups", None),
        P("groups"),
        P("groups"),
    )
    return jax.shard_map(
        on_device,
        mesh=mesh,
        in_specs=placed,
        out_specs=(
            P(("groups", "dp"), None, None),
            P("groups", "dp", None),
            P("groups", "dp", None),
        ),
        check_vma=False,
    )
```

```python
import functools

import jax
import jax.numpy as jnp
from jax import lax
from jax.experimental import pallas as pl
from jax.experimental.pallas import tpu as pltpu
from jax.sharding import PartitionSpec as P


def adapter_kernel(slot_ref, len_ref, frames_ref, cot_ref, gain_ref, wd_ref, wu_ref, scale_ref,
                   out_ref, grads_out, gd_ref, gu_ref):
    u = pl.program_id(0)

    @pl.when(u == 0)
    def _():
        gd_ref[...] = jnp.zeros_like(gd_ref)
        gu_ref[...] = jnp.zeros_like(gu_ref)

    slot = slot_ref[u]
    length = len_ref[u]
    gain = gain_ref[...]
    values = frames_ref[0].astype(jnp.float32)
    centre_mean = jnp.mean(values, axis=1, keepdims=True)
    mean_removed = values - centre_mean
    variance = jnp.mean(mean_removed * mean_removed, axis=1, keepdims=True)
    reciprocal_deviation = lax.rsqrt(variance + 1e-06)
    standardized_input = mean_removed * reciprocal_deviation
    layer_normed = (standardized_input * gain).astype(jnp.bfloat16)
    w_down = wd_ref[0]
    w_up = wu_ref[0]
    pre_act = jnp.dot(layer_normed, w_down, preferred_element_type=jnp.float32)
    sigmoid_pre = 1.0 / (1.0 + jnp.exp(-pre_act))
    hidden = (pre_act * sigmoid_pre).astype(jnp.bfloat16)
    upstream = cot_ref[0]
    live = lax.broadcasted_iota(jnp.int32, (upstream.shape[0], 1), 0) < length
    masked_up = jnp.where(live, upstream, jnp.zeros_like(upstream))
    contract_rows = (((0,), (0,)), ((), ()))
    gu_ref[slot] += lax.dot_general(
        masked_up, hidden, contract_rows, preferred_element_type=jnp.float32
    )
    d_hidden = jnp.dot(masked_up, w_up, preferred_element_type=jnp.float32)
    d_pre = (d_hidden * sigmoid_pre * (1.0 + pre_act * (1.0 - sigmoid_pre))).astype(jnp.bfloat16)
    gd_ref[slot] += lax.dot_general(
        layer_normed, d_pre, contract_rows, preferred_element_type=jnp.float32
    )
    d_normed = lax.dot_general(
        d_pre, w_down, (((1,), (1,)), ((), ())), preferred_element_type=jnp.float32
    )
    scaled_rows = d_normed * gain
    inner_gradient = (
        scaled_rows
        - jnp.mean(scaled_rows, axis=1, keepdims=True)
        - standardized_input * jnp.mean(scaled_rows * standardized_input, axis=1, keepdims=True)
    ) * reciprocal_deviation
    out_ref[0] = (upstream.astype(jnp.float32) + inner_gradient).astype(out_ref.dtype)

    @pl.when(u == pl.num_programs(0) - 1)
    def _():
        slots = gd_ref.shape[0]
        grads_out[pl.ds(0, slots)] = (gd_ref[...] * scale_ref[...]).astype(grads_out.dtype)
        grads_out[pl.ds(slots, slots)] = (gu_ref[...] * scale_ref[...]).astype(grads_out.dtype)


def combine_kernel(order_ref, lang_ref, start_ref, back_ref, down_ref, up_ref, acc_d, acc_u,
                   *, slots):
    block = down_ref.shape[0]
    b = pl.program_id(0)
    base = b * block
    down_ref[...] = jnp.zeros_like(down_ref)
    up_ref[...] = jnp.zeros_like(up_ref)
    first_at = start_ref[b]
    end_at = start_ref[b + 1]
    last_member = lang_ref.shape[0] - 1

    def add_member(i, carry):
        m = order_ref[i]
        lang = lang_ref[i]
        first = (i == first_at) | (lang_ref[jnp.maximum(i - 1, 0)] != lang)
        last = (i == end_at - 1) | (lang_ref[jnp.minimum(i + 1, last_member)] != lang)
        val_d = back_ref[m].astype(jnp.float32)
        val_u = back_ref[m + slots].astype(jnp.float32)

        @pl.when(first)
        def _():
            acc_d[...] = val_d
            acc_u[...] = val_u

        @pl.when(jnp.logical_not(first))
        def _():
            acc_d[...] += val_d
            acc_u[...] += val_u

        @pl.when(last)
        def _():
            down_ref[lang - base] = acc_d[...].astype(down_ref.dtype)
            up_ref[lang - base] = acc_u[...].astype(up_ref.dtype)

        return carry

    lax.fori_loop(first_at, end_at, add_member, 0)


def combine(slot_lang, back, lang_count):
    devices, slots = slot_lang.shape
    members, row_count, bottleneck = back.shape
    block = 32 if lang_count % 32 == 0 else (8 if lang_count % 8 == 0 else 1)
    blocks = lang_count // block
    langs = slot_lang.reshape(-1)
    down_index = (
        jnp.arange(devices, dtype=jnp.int32)[:, None] * (2 * slots)
        + jnp.arange(slots, dtype=jnp.int32)[None, :]
    ).reshape(-1)
    order = jnp.argsort(langs, stable=True)
    sorted_langs = langs[order]
    member_order = down_index[order]
    edges = jnp.arange(blocks + 1, dtype=jnp.int32) * block
    starts = jnp.sum((sorted_langs[None, :] < edges[:, None]).astype(jnp.int32), axis=1)
    grid_spec = pltpu.PrefetchScalarGridSpec(
        num_scalar_prefetch=3,
        grid=(blocks,),
        in_specs=[pl.BlockSpec((members, row_count, bottleneck), lambda b, o, l, st: (0, 0, 0))],
        out_specs=[
            pl.BlockSpec((block, row_count, bottleneck), lambda b, o, l, st: (b, 0, 0)),
            pl.BlockSpec((block, row_count, bottleneck), lambda b, o, l, st: (b, 0, 0)),
        ],
        scratch_shapes=[
            pltpu.VMEM((row_count, bottleneck), jnp.float32),
            pltpu.VMEM((row_count, bottleneck), jnp.float32),
        ],
    )
    out_shape = jax.ShapeDtypeStruct((lang_count, row_count, bottleneck), jnp.bfloat16)
    return pl.pallas_call(
        functools.partial(combine_kernel, slots=slots),
        grid_spec=grid_spec,
        out_shape=[out_shape, out_shape],
        compiler_params=pltpu.CompilerParams(
            dimension_semantics=("arbitrary",), vmem_limit_bytes=48 * 1024 * 1024
        ),
        cost_estimate=pl.CostEstimate(
            flops=back.size, bytes_accessed=back.size * 2 + 2 * lang_count * row_count * bottleneck * 2,
            transcendentals=0,
        ),
    )(member_order.astype(jnp.int32), sorted_langs.astype(jnp.int32), starts, back)


def local_pass(frames, cotangent, gain, weights, own_slot, own_lengths, slots, own_scale):
    utts, frame_count, width = frames.shape
    bottleneck = weights.shape[2]
    flops = 10 * utts * frame_count * width * bottleneck
    moved = 3 * frames.size * 2 + 2 * utts * width * bottleneck * 2 + 4 * slots * width * bottleneck * 4
    grid_spec = pltpu.PrefetchScalarGridSpec(
        num_scalar_prefetch=2,
        grid=(utts,),
        in_specs=[
            pl.BlockSpec((1, frame_count, width), lambda u, sl, ln: (u, 0, 0)),
            pl.BlockSpec((1, frame_count, width), lambda u, sl, ln: (u, 0, 0)),
            pl.BlockSpec((1, width), lambda u, sl, ln: (0, 0)),
            pl.BlockSpec((1, width, bottleneck), lambda u, sl, ln: (sl[u], 0, 0)),
            pl.BlockSpec((1, width, bottleneck), lambda u, sl, ln: (sl[u] + slots, 0, 0)),
            pl.BlockSpec((slots, 1, 1), lambda u, sl, ln: (0, 0, 0)),
        ],
        out_specs=[
            pl.BlockSpec((1, frame_count, width), lambda u, sl, ln: (u, 0, 0)),
            pl.BlockSpec((2 * slots, width, bottleneck), lambda u, sl, ln: (0, 0, 0)),
        ],
        scratch_shapes=[
            pltpu.VMEM((slots, width, bottleneck), jnp.float32),
            pltpu.VMEM((slots, width, bottleneck), jnp.float32),
        ],
    )
    return pl.pallas_call(
        adapter_kernel,
        grid_spec=grid_spec,
        out_shape=[
            jax.ShapeDtypeStruct(frames.shape, jnp.bfloat16),
            jax.ShapeDtypeStruct((2 * slots, width, bottleneck), jnp.bfloat16),
        ],

        compiler_params=pltpu.CompilerParams(
            dimension_semantics=("arbitrary",), vmem_limit_bytes=60 * 1024 * 1024
        ),
        cost_estimate=pl.CostEstimate(flops=flops, bytes_accessed=moved, transcendentals=utts * frame_count * bottleneck),
    )(own_slot, own_lengths, frames, cotangent, gain.reshape(1, width), weights, weights,
      own_scale.reshape(slots, 1, 1))


def on_device(frames, cotangent, gain, down_weight, up_weight, slot_lang, utt_slot, lengths):
    devices = lax.axis_size("dp")
    self_index = lax.axis_index("dp")
    per_device = frames.shape[0]
    slots = slot_lang.shape[1]
    lang_count, row_count, bottleneck = down_weight.shape
    owners = jnp.arange(utt_slot.shape[0], dtype=jnp.int32) // per_device
    utt_lang = slot_lang[owners, utt_slot]
    own_lengths = lax.dynamic_slice_in_dim(lengths, self_index * per_device, per_device)
    own_slot = lax.dynamic_slice_in_dim(utt_slot, self_index * per_device, per_device)
    lang_ids = jnp.arange(lang_count, dtype=jnp.int32)
    counts = jnp.sum(jnp.where(utt_lang[None, :] == lang_ids[:, None], lengths[None, :], 0), axis=1)
    scaling = lax.rsqrt(jnp.maximum(counts, 1).astype(jnp.float32))
    member_langs = slot_lang.reshape(-1)
    send_down = jnp.take(down_weight, member_langs, axis=0).reshape(
        devices, slots, row_count, bottleneck
    )
    send_up = jnp.take(up_weight, member_langs, axis=0).reshape(
        devices, slots, row_count, bottleneck
    )
    sent = jnp.concatenate([send_down, send_up], axis=1)
    got = lax.all_to_all(sent, "dp", split_axis=0, concat_axis=0, tiled=True)

    weights = got.transpose(1, 0, 2, 3).reshape(2 * slots, devices * row_count, bottleneck)
    own_scale = jnp.take(scaling, lax.dynamic_index_in_dim(slot_lang, self_index, 0, False))
    d_frames, grads = local_pass(
        frames, cotangent, gain, weights, own_slot, own_lengths, slots, own_scale
    )
    grads = grads.reshape(2 * slots, devices, row_count, bottleneck).transpose(1, 0, 2, 3)
    back = lax.all_to_all(grads, "dp", split_axis=0, concat_axis=0, tiled=True)
    back = back.reshape(devices * 2 * slots, row_count, bottleneck)
    down_grads, up_grads = combine(slot_lang, back, lang_count)
    return (d_frames, down_grads, up_grads)


def solution(mesh):
    placed = (
        P(("groups", "dp"), None, None),
        P(("groups", "dp"), None, None),
        P(),
        P("groups", "dp", None),
        P("groups", "dp", None),
        P("groups", None),
        P("groups"),
        P("groups"),
    )
    return jax.shard_map(
        on_device,
        mesh=mesh,
        in_specs=placed,
        out_specs=(
            P(("groups", "dp"), None, None),
            P("groups", "dp", None),
            P("groups", "dp", None),
        ),
        check_vma=False,
    )
```

```python
import functools

import jax
import jax.numpy as jnp
from jax import lax
from jax.experimental import pallas as pl
from jax.experimental.pallas import tpu as pltpu
from jax.sharding import PartitionSpec as P


def adapter_kernel(slot_ref, len_ref, frames_ref, cot_ref, gain_ref, wd_ref, wu_ref, scale_ref,
                   out_ref, grads_out, gd_ref, gu_ref, *, direct):
    u = pl.program_id(0)

    @pl.when(u == 0)
    def _():
        gd_ref[...] = jnp.zeros_like(gd_ref)
        gu_ref[...] = jnp.zeros_like(gu_ref)

    slot = slot_ref[u]
    length = len_ref[u]
    gain = gain_ref[...]
    values = frames_ref[0].astype(jnp.float32)
    centre_mean = jnp.mean(values, axis=1, keepdims=True)
    mean_removed = values - centre_mean
    variance = jnp.mean(mean_removed * mean_removed, axis=1, keepdims=True)
    reciprocal_deviation = lax.rsqrt(variance + 1e-06)
    standardized_input = mean_removed * reciprocal_deviation
    layer_normed = (standardized_input * gain).astype(jnp.bfloat16)
    if direct:
        devices, _, row_count, bottleneck = wd_ref.shape
        w_down = wd_ref[:, 0].reshape(devices * row_count, bottleneck)
        w_up = wu_ref[:, 0].reshape(devices * row_count, bottleneck)
    else:
        w_down = wd_ref[0]
        w_up = wu_ref[0]
    pre_act = jnp.dot(layer_normed, w_down, preferred_element_type=jnp.float32)
    sigmoid_pre = 1.0 / (1.0 + jnp.exp(-pre_act))
    hidden = (pre_act * sigmoid_pre).astype(jnp.bfloat16)
    upstream = cot_ref[0]
    live = lax.broadcasted_iota(jnp.int32, (upstream.shape[0], 1), 0) < length
    masked_up = jnp.where(live, upstream, jnp.zeros_like(upstream))
    contract_rows = (((0,), (0,)), ((), ()))
    gu_ref[slot] += lax.dot_general(
        masked_up, hidden, contract_rows, preferred_element_type=jnp.float32
    )
    d_hidden = jnp.dot(masked_up, w_up, preferred_element_type=jnp.float32)
    d_pre = (d_hidden * sigmoid_pre * (1.0 + pre_act * (1.0 - sigmoid_pre))).astype(jnp.bfloat16)
    gd_ref[slot] += lax.dot_general(
        layer_normed, d_pre, contract_rows, preferred_element_type=jnp.float32
    )
    d_normed = lax.dot_general(
        d_pre, w_down, (((1,), (1,)), ((), ())), preferred_element_type=jnp.float32
    )
    scaled_rows = d_normed * gain
    inner_gradient = (
        scaled_rows
        - jnp.mean(scaled_rows, axis=1, keepdims=True)
        - standardized_input * jnp.mean(scaled_rows * standardized_input, axis=1, keepdims=True)
    ) * reciprocal_deviation
    out_ref[0] = (upstream.astype(jnp.float32) + inner_gradient).astype(out_ref.dtype)

    @pl.when(u == pl.num_programs(0) - 1)
    def _():
        slots = gd_ref.shape[0]
        if direct:
            devices, _, row_count, _ = grads_out.shape
            for dev in range(devices):
                rows = pl.ds(dev * row_count, row_count)
                grads_out[dev, pl.ds(0, slots)] = (
                    gd_ref[:, rows, :] * scale_ref[...]
                ).astype(grads_out.dtype)
                grads_out[dev, pl.ds(slots, slots)] = (
                    gu_ref[:, rows, :] * scale_ref[...]
                ).astype(grads_out.dtype)
        else:
            grads_out[pl.ds(0, slots)] = (gd_ref[...] * scale_ref[...]).astype(grads_out.dtype)
            grads_out[pl.ds(slots, slots)] = (gu_ref[...] * scale_ref[...]).astype(
                grads_out.dtype
            )


def combine_kernel(order_ref, lang_ref, start_ref, back_ref, down_ref, up_ref, acc_d, acc_u,
                   *, slots):
    block = down_ref.shape[0]
    b = pl.program_id(0)
    base = b * block
    down_ref[...] = jnp.zeros_like(down_ref)
    up_ref[...] = jnp.zeros_like(up_ref)
    first_at = start_ref[b]
    end_at = start_ref[b + 1]
    last_member = lang_ref.shape[0] - 1

    def add_member(i, carry):
        m = order_ref[i]
        lang = lang_ref[i]
        first = (i == first_at) | (lang_ref[jnp.maximum(i - 1, 0)] != lang)
        last = (i == end_at - 1) | (lang_ref[jnp.minimum(i + 1, last_member)] != lang)
        val_d = back_ref[m].astype(jnp.float32)
        val_u = back_ref[m + slots].astype(jnp.float32)

        @pl.when(first)
        def _():
            acc_d[...] = val_d
            acc_u[...] = val_u

        @pl.when(jnp.logical_not(first))
        def _():
            acc_d[...] += val_d
            acc_u[...] += val_u

        @pl.when(last)
        def _():
            down_ref[lang - base] = acc_d[...].astype(down_ref.dtype)
            up_ref[lang - base] = acc_u[...].astype(up_ref.dtype)

        return carry

    lax.fori_loop(first_at, end_at, add_member, 0)


def combine(slot_lang, back, lang_count):
    devices, slots = slot_lang.shape
    members, row_count, bottleneck = back.shape
    block = 32 if lang_count % 32 == 0 else (8 if lang_count % 8 == 0 else 1)
    blocks = lang_count // block
    langs = slot_lang.reshape(-1)
    down_index = (
        jnp.arange(devices, dtype=jnp.int32)[:, None] * (2 * slots)
        + jnp.arange(slots, dtype=jnp.int32)[None, :]
    ).reshape(-1)
    order = jnp.argsort(langs, stable=True)
    sorted_langs = langs[order]
    member_order = down_index[order]
    edges = jnp.arange(blocks + 1, dtype=jnp.int32) * block
    starts = jnp.sum((sorted_langs[None, :] < edges[:, None]).astype(jnp.int32), axis=1)
    grid_spec = pltpu.PrefetchScalarGridSpec(
        num_scalar_prefetch=3,
        grid=(blocks,),
        in_specs=[pl.BlockSpec((members, row_count, bottleneck), lambda b, o, l, st: (0, 0, 0))],
        out_specs=[
            pl.BlockSpec((block, row_count, bottleneck), lambda b, o, l, st: (b, 0, 0)),
            pl.BlockSpec((block, row_count, bottleneck), lambda b, o, l, st: (b, 0, 0)),
        ],
        scratch_shapes=[
            pltpu.VMEM((row_count, bottleneck), jnp.float32),
            pltpu.VMEM((row_count, bottleneck), jnp.float32),
        ],
    )
    out_shape = jax.ShapeDtypeStruct((lang_count, row_count, bottleneck), jnp.bfloat16)
    return pl.pallas_call(
        functools.partial(combine_kernel, slots=slots),
        grid_spec=grid_spec,
        out_shape=[out_shape, out_shape],
        compiler_params=pltpu.CompilerParams(
            dimension_semantics=("arbitrary",), vmem_limit_bytes=48 * 1024 * 1024
        ),
        cost_estimate=pl.CostEstimate(
            flops=back.size, bytes_accessed=back.size * 2 + 2 * lang_count * row_count * bottleneck * 2,
            transcendentals=0,
        ),
    )(member_order.astype(jnp.int32), sorted_langs.astype(jnp.int32), starts, back)


def gather_kernel(lang_ref, down_hbm, up_hbm, out_ref, sems, *, slots):
    members = lang_ref.shape[0]

    def copies(m):
        lang = lang_ref[m]
        dev = m // slots
        s = m % slots
        return (
            pltpu.make_async_copy(down_hbm.at[lang], out_ref.at[dev, s], sems.at[0, m]),
            pltpu.make_async_copy(up_hbm.at[lang], out_ref.at[dev, slots + s], sems.at[1, m]),
        )

    def start(m, carry):
        for c in copies(m):
            c.start()
        return carry

    def finish(m, carry):
        for c in copies(m):
            c.wait()
        return carry

    lax.fori_loop(0, members, start, 0)
    lax.fori_loop(0, members, finish, 0)


def gather_rows(slot_lang, down_weight, up_weight):
    devices, slots = slot_lang.shape
    _, row_count, bottleneck = down_weight.shape
    members = devices * slots
    grid_spec = pltpu.PrefetchScalarGridSpec(
        num_scalar_prefetch=1,
        grid=(1,),
        in_specs=[pl.BlockSpec(memory_space=pl.ANY), pl.BlockSpec(memory_space=pl.ANY)],
        out_specs=pl.BlockSpec(
            (devices, 2 * slots, row_count, bottleneck), lambda i, ml: (0, 0, 0, 0)
        ),
        scratch_shapes=[pltpu.SemaphoreType.DMA((2, members))],
    )
    size = members * 2 * row_count * bottleneck * 2
    return pl.pallas_call(
        functools.partial(gather_kernel, slots=slots),
        grid_spec=grid_spec,
        out_shape=jax.ShapeDtypeStruct((devices, 2 * slots, row_count, bottleneck), jnp.bfloat16),
        compiler_params=pltpu.CompilerParams(vmem_limit_bytes=48 * 1024 * 1024),
        cost_estimate=pl.CostEstimate(flops=0, bytes_accessed=2 * size, transcendentals=0),
    )(slot_lang.reshape(-1), down_weight, up_weight)


def local_pass(frames, cotangent, gain, got, own_slot, own_lengths, own_scale):
    utts, frame_count, width = frames.shape
    devices, double_slots, row_count, bottleneck = got.shape
    slots = double_slots // 2
    direct = row_count % 16 == 0
    if direct:
        weights = got
        w_specs = [
            pl.BlockSpec((devices, 1, row_count, bottleneck), lambda u, sl, ln: (0, sl[u], 0, 0)),
            pl.BlockSpec(
                (devices, 1, row_count, bottleneck), lambda u, sl, ln: (0, sl[u] + slots, 0, 0)
            ),
        ]
        grads_shape = (devices, 2 * slots, row_count, bottleneck)
        grads_spec = pl.BlockSpec(grads_shape, lambda u, sl, ln: (0, 0, 0, 0))
    else:
        weights = got.transpose(1, 0, 2, 3).reshape(2 * slots, width, bottleneck)
        w_specs = [
            pl.BlockSpec((1, width, bottleneck), lambda u, sl, ln: (sl[u], 0, 0)),
            pl.BlockSpec((1, width, bottleneck), lambda u, sl, ln: (sl[u] + slots, 0, 0)),
        ]
        grads_shape = (2 * slots, width, bottleneck)
        grads_spec = pl.BlockSpec(grads_shape, lambda u, sl, ln: (0, 0, 0))
    flops = 10 * utts * frame_count * width * bottleneck
    moved = 3 * frames.size * 2 + 2 * utts * width * bottleneck * 2 + 4 * slots * width * bottleneck * 4
    grid_spec = pltpu.PrefetchScalarGridSpec(
        num_scalar_prefetch=2,
        grid=(utts,),
        in_specs=[
            pl.BlockSpec((1, frame_count, width), lambda u, sl, ln: (u, 0, 0)),
            pl.BlockSpec((1, frame_count, width), lambda u, sl, ln: (u, 0, 0)),
            pl.BlockSpec((1, width), lambda u, sl, ln: (0, 0)),
            *w_specs,
            pl.BlockSpec((slots, 1, 1), lambda u, sl, ln: (0, 0, 0)),
        ],
        out_specs=[
            pl.BlockSpec((1, frame_count, width), lambda u, sl, ln: (u, 0, 0)),
            grads_spec,
        ],
        scratch_shapes=[
            pltpu.VMEM((slots, width, bottleneck), jnp.float32),
            pltpu.VMEM((slots, width, bottleneck), jnp.float32),
        ],
    )
    d_frames, grads = pl.pallas_call(
        functools.partial(adapter_kernel, direct=direct),
        grid_spec=grid_spec,
        out_shape=[
            jax.ShapeDtypeStruct(frames.shape, jnp.bfloat16),
            jax.ShapeDtypeStruct(grads_shape, jnp.bfloat16),
        ],
        compiler_params=pltpu.CompilerParams(
            dimension_semantics=("arbitrary",), vmem_limit_bytes=60 * 1024 * 1024
        ),
        cost_estimate=pl.CostEstimate(flops=flops, bytes_accessed=moved, transcendentals=utts * frame_count * bottleneck),
    )(own_slot, own_lengths, frames, cotangent, gain.reshape(1, width), weights, weights,
      own_scale.reshape(slots, 1, 1))
    if not direct:
        grads = grads.reshape(2 * slots, devices, row_count, bottleneck).transpose(1, 0, 2, 3)
    return d_frames, grads


def on_device(frames, cotangent, gain, down_weight, up_weight, slot_lang, utt_slot, lengths):
    devices = lax.axis_size("dp")
    self_index = lax.axis_index("dp")
    per_device = frames.shape[0]
    slots = slot_lang.shape[1]
    lang_count, row_count, bottleneck = down_weight.shape
    owners = jnp.arange(utt_slot.shape[0], dtype=jnp.int32) // per_device
    utt_lang = slot_lang[owners, utt_slot]
    own_lengths = lax.dynamic_slice_in_dim(lengths, self_index * per_device, per_device)
    own_slot = lax.dynamic_slice_in_dim(utt_slot, self_index * per_device, per_device)
    lang_ids = jnp.arange(lang_count, dtype=jnp.int32)
    counts = jnp.sum(jnp.where(utt_lang[None, :] == lang_ids[:, None], lengths[None, :], 0), axis=1)
    scaling = lax.rsqrt(jnp.maximum(counts, 1).astype(jnp.float32))
    member_langs = slot_lang.reshape(-1)
    sent = gather_rows(slot_lang, down_weight, up_weight)
    got = lax.all_to_all(sent, "dp", split_axis=0, concat_axis=0, tiled=True)

    own_scale = jnp.take(scaling, lax.dynamic_index_in_dim(slot_lang, self_index, 0, False))
    d_frames, grads = local_pass(frames, cotangent, gain, got, own_slot, own_lengths, own_scale)
    back = lax.all_to_all(grads, "dp", split_axis=0, concat_axis=0, tiled=True)
    back = back.reshape(devices * 2 * slots, row_count, bottleneck)
    down_grads, up_grads = combine(slot_lang, back, lang_count)
    return (d_frames, down_grads, up_grads)


def solution(mesh):
    placed = (
        P(("groups", "dp"), None, None),
        P(("groups", "dp"), None, None),
        P(),
        P("groups", "dp", None),
        P("groups", "dp", None),
        P("groups", None),
        P("groups"),
        P("groups"),
    )
    return jax.shard_map(
        on_device,
        mesh=mesh,
        in_specs=placed,
        out_specs=(
            P(("groups", "dp"), None, None),
            P("groups", "dp", None),
            P("groups", "dp", None),
        ),
        check_vma=False,
    )
```

```python
import functools

import jax
import jax.numpy as jnp
from jax import lax
from jax.experimental import pallas as pl
from jax.experimental.pallas import tpu as pltpu
from jax.sharding import PartitionSpec as P


def _weights(ref, direct):
    if direct:
        devices, _, row_count, bottleneck = ref.shape
        return ref[:, 0].reshape(devices * row_count, bottleneck)
    return ref[0]


def _flush(acc_ref, scale_ref, out_ref, direct):
    if direct:
        devices, slots, row_count, _ = out_ref.shape
        for dev in range(devices):
            rows = pl.ds(dev * row_count, row_count)
            out_ref[dev] = (acc_ref[:, rows, :] * scale_ref[...]).astype(out_ref.dtype)
    else:
        out_ref[...] = (acc_ref[...] * scale_ref[...]).astype(out_ref.dtype)


def _normalize(frames_ref, gain):
    values = frames_ref[0].astype(jnp.float32)
    centre_mean = jnp.mean(values, axis=1, keepdims=True)
    mean_removed = values - centre_mean
    variance = jnp.mean(mean_removed * mean_removed, axis=1, keepdims=True)
    reciprocal_deviation = lax.rsqrt(variance + 1e-06)
    standardized_input = mean_removed * reciprocal_deviation
    layer_normed = (standardized_input * gain).astype(jnp.bfloat16)
    return reciprocal_deviation, standardized_input, layer_normed


def _masked(cot_ref, length):
    upstream = cot_ref[0]
    live = lax.broadcasted_iota(jnp.int32, (upstream.shape[0], 1), 0) < length
    return upstream, jnp.where(live, upstream, jnp.zeros_like(upstream))


CONTRACT_ROWS = (((0,), (0,)), ((), ()))


def forward_kernel(slot_ref, len_ref, frames_ref, cot_ref, gain_ref, wd_ref, scale_ref,
                   pre_ref, gu_out, gu_ref, *, direct):
    u = pl.program_id(0)

    @pl.when(u == 0)
    def _():
        gu_ref[...] = jnp.zeros_like(gu_ref)

    slot = slot_ref[u]
    _, _, layer_normed = _normalize(frames_ref, gain_ref[...])
    pre_act = jnp.dot(layer_normed, _weights(wd_ref, direct), preferred_element_type=jnp.float32)
    pre_ref[0] = pre_act
    sigmoid_pre = 1.0 / (1.0 + jnp.exp(-pre_act))
    hidden = (pre_act * sigmoid_pre).astype(jnp.bfloat16)
    _, masked_up = _masked(cot_ref, len_ref[u])
    gu_ref[slot] += lax.dot_general(
        masked_up, hidden, CONTRACT_ROWS, preferred_element_type=jnp.float32
    )

    @pl.when(u == pl.num_programs(0) - 1)
    def _():
        _flush(gu_ref, scale_ref, gu_out, direct)


def backward_kernel(slot_ref, len_ref, frames_ref, cot_ref, gain_ref, wd_ref, wu_ref, pre_ref,
                    scale_ref, out_ref, gd_out, gd_ref, *, direct):
    u = pl.program_id(0)

    @pl.when(u == 0)
    def _():
        gd_ref[...] = jnp.zeros_like(gd_ref)

    slot = slot_ref[u]
    gain = gain_ref[...]
    reciprocal_deviation, standardized_input, layer_normed = _normalize(frames_ref, gain)
    pre_act = pre_ref[0]
    sigmoid_pre = 1.0 / (1.0 + jnp.exp(-pre_act))
    upstream, masked_up = _masked(cot_ref, len_ref[u])
    d_hidden = jnp.dot(masked_up, _weights(wu_ref, direct), preferred_element_type=jnp.float32)
    d_pre = (d_hidden * sigmoid_pre * (1.0 + pre_act * (1.0 - sigmoid_pre))).astype(jnp.bfloat16)
    gd_ref[slot] += lax.dot_general(
        layer_normed, d_pre, CONTRACT_ROWS, preferred_element_type=jnp.float32
    )
    d_normed = lax.dot_general(
        d_pre, _weights(wd_ref, direct), (((1,), (1,)), ((), ())),
        preferred_element_type=jnp.float32,
    )
    scaled_rows = d_normed * gain
    inner_gradient = (
        scaled_rows
        - jnp.mean(scaled_rows, axis=1, keepdims=True)
        - standardized_input * jnp.mean(scaled_rows * standardized_input, axis=1, keepdims=True)
    ) * reciprocal_deviation
    out_ref[0] = (upstream.astype(jnp.float32) + inner_gradient).astype(out_ref.dtype)

    @pl.when(u == pl.num_programs(0) - 1)
    def _():
        _flush(gd_ref, scale_ref, gd_out, direct)


def combine_kernel(order_ref, lang_ref, start_ref, back_ref, out_ref, acc_ref):
    block = out_ref.shape[0]
    b = pl.program_id(0)
    base = b * block
    out_ref[...] = jnp.zeros_like(out_ref)
    first_at = start_ref[b]
    end_at = start_ref[b + 1]
    last_member = lang_ref.shape[0] - 1

    def add_member(i, carry):
        m = order_ref[i]
        lang = lang_ref[i]
        first = (i == first_at) | (lang_ref[jnp.maximum(i - 1, 0)] != lang)
        last = (i == end_at - 1) | (lang_ref[jnp.minimum(i + 1, last_member)] != lang)
        val = back_ref[m].astype(jnp.float32)

        @pl.when(first)
        def _():
            acc_ref[...] = val

        @pl.when(jnp.logical_not(first))
        def _():
            acc_ref[...] += val

        @pl.when(last)
        def _():
            out_ref[lang - base] = acc_ref[...].astype(out_ref.dtype)

        return carry

    lax.fori_loop(first_at, end_at, add_member, 0)


def combine_plan(slot_lang, lang_count):
    block = 32 if lang_count % 32 == 0 else (8 if lang_count % 8 == 0 else 1)
    langs = slot_lang.reshape(-1)
    order = jnp.argsort(langs, stable=True).astype(jnp.int32)
    sorted_langs = langs[order].astype(jnp.int32)
    edges = jnp.arange(lang_count // block + 1, dtype=jnp.int32) * block
    starts = jnp.sum((sorted_langs[None, :] < edges[:, None]).astype(jnp.int32), axis=1)
    return block, order, sorted_langs, starts


def combine(plan, back, lang_count):
    block, order, sorted_langs, starts = plan
    members, row_count, bottleneck = back.shape
    grid_spec = pltpu.PrefetchScalarGridSpec(
        num_scalar_prefetch=3,
        grid=(lang_count // block,),
        in_specs=[pl.BlockSpec((members, row_count, bottleneck), lambda b, o, l, st: (0, 0, 0))],
        out_specs=pl.BlockSpec((block, row_count, bottleneck), lambda b, o, l, st: (b, 0, 0)),
        scratch_shapes=[pltpu.VMEM((row_count, bottleneck), jnp.float32)],
    )
    return pl.pallas_call(
        combine_kernel,
        grid_spec=grid_spec,
        out_shape=jax.ShapeDtypeStruct((lang_count, row_count, bottleneck), jnp.bfloat16),
        compiler_params=pltpu.CompilerParams(
            dimension_semantics=("arbitrary",), vmem_limit_bytes=48 * 1024 * 1024
        ),
        cost_estimate=pl.CostEstimate(
            flops=back.size, bytes_accessed=back.size * 2 + lang_count * row_count * bottleneck * 2,
            transcendentals=0,
        ),
    )(order, sorted_langs, starts, back)


def gather_kernel(lang_ref, weight_hbm, out_ref, sems, *, slots):
    members = lang_ref.shape[0]

    def copy(m):
        return pltpu.make_async_copy(
            weight_hbm.at[lang_ref[m]], out_ref.at[m // slots, m % slots], sems.at[m]
        )

    def start(m, carry):
        copy(m).start()
        return carry

    def finish(m, carry):
        copy(m).wait()
        return carry

    lax.fori_loop(0, members, start, 0)
    lax.fori_loop(0, members, finish, 0)


def gather_rows(slot_lang, weight):
    devices, slots = slot_lang.shape
    _, row_count, bottleneck = weight.shape
    members = devices * slots
    grid_spec = pltpu.PrefetchScalarGridSpec(
        num_scalar_prefetch=1,
        grid=(1,),
        in_specs=[pl.BlockSpec(memory_space=pl.ANY)],
        out_specs=pl.BlockSpec((devices, slots, row_count, bottleneck), lambda i, ml: (0, 0, 0, 0)),
        scratch_shapes=[pltpu.SemaphoreType.DMA((members,))],
    )
    size = members * row_count * bottleneck * 2
    return pl.pallas_call(
        functools.partial(gather_kernel, slots=slots),
        grid_spec=grid_spec,
        out_shape=jax.ShapeDtypeStruct((devices, slots, row_count, bottleneck), jnp.bfloat16),
        compiler_params=pltpu.CompilerParams(vmem_limit_bytes=48 * 1024 * 1024),
        cost_estimate=pl.CostEstimate(flops=0, bytes_accessed=2 * size, transcendentals=0),
    )(slot_lang.reshape(-1), weight)


def _layouts(got):
    devices, slots, row_count, bottleneck = got.shape
    width = devices * row_count
    direct = row_count % 16 == 0
    if direct:
        weights = got
        w_spec = pl.BlockSpec((devices, 1, row_count, bottleneck), lambda u, sl, ln: (0, sl[u], 0, 0))
        g_shape = (devices, slots, row_count, bottleneck)
        g_spec = pl.BlockSpec(g_shape, lambda u, sl, ln: (0, 0, 0, 0))
    else:
        weights = got.transpose(1, 0, 2, 3).reshape(slots, width, bottleneck)
        w_spec = pl.BlockSpec((1, width, bottleneck), lambda u, sl, ln: (sl[u], 0, 0))
        g_shape = (slots, width, bottleneck)
        g_spec = pl.BlockSpec(g_shape, lambda u, sl, ln: (0, 0, 0))
    return direct, weights, w_spec, g_shape, g_spec


def _to_send(grads, got_shape, direct):
    if direct:
        return grads
    devices, slots, row_count, bottleneck = got_shape
    return grads.reshape(slots, devices, row_count, bottleneck).transpose(1, 0, 2, 3)


def _utt_spec(frame_count, width):
    return pl.BlockSpec((1, frame_count, width), lambda u, sl, ln: (u, 0, 0))


def forward_pass(frames, cotangent, gain, got_down, own_slot, own_lengths, own_scale):
    utts, frame_count, width = frames.shape
    slots, bottleneck = got_down.shape[1], got_down.shape[3]
    direct, w_down, w_spec, g_shape, g_spec = _layouts(got_down)
    grid_spec = pltpu.PrefetchScalarGridSpec(
        num_scalar_prefetch=2,
        grid=(utts,),
        in_specs=[
            _utt_spec(frame_count, width),
            _utt_spec(frame_count, width),
            pl.BlockSpec((1, width), lambda u, sl, ln: (0, 0)),
            w_spec,
            pl.BlockSpec((slots, 1, 1), lambda u, sl, ln: (0, 0, 0)),
        ],
        out_specs=[
            pl.BlockSpec((1, frame_count, bottleneck), lambda u, sl, ln: (u, 0, 0)),
            g_spec,
        ],
        scratch_shapes=[pltpu.VMEM((slots, width, bottleneck), jnp.float32)],
    )
    pre_act, grads = pl.pallas_call(
        functools.partial(forward_kernel, direct=direct),
        grid_spec=grid_spec,
        out_shape=[
            jax.ShapeDtypeStruct((utts, frame_count, bottleneck), jnp.float32),
            jax.ShapeDtypeStruct(g_shape, jnp.bfloat16),
        ],
        compiler_params=pltpu.CompilerParams(
            dimension_semantics=("arbitrary",), vmem_limit_bytes=60 * 1024 * 1024
        ),
        cost_estimate=pl.CostEstimate(
            flops=4 * utts * frame_count * width * bottleneck,
            bytes_accessed=2 * frames.size * 2 + utts * width * bottleneck * 2,
            transcendentals=utts * frame_count * bottleneck,
        ),
    )(own_slot, own_lengths, frames, cotangent, gain.reshape(1, width), w_down,
      own_scale.reshape(slots, 1, 1))
    return pre_act, _to_send(grads, got_down.shape, direct)


def backward_pass(frames, cotangent, gain, got_down, got_up, pre_act, own_slot, own_lengths,
                  own_scale):
    utts, frame_count, width = frames.shape
    slots, bottleneck = got_down.shape[1], got_down.shape[3]
    direct, w_down, w_spec, g_shape, g_spec = _layouts(got_down)
    _, w_up, _, _, _ = _layouts(got_up)
    grid_spec = pltpu.PrefetchScalarGridSpec(
        num_scalar_prefetch=2,
        grid=(utts,),
        in_specs=[
            _utt_spec(frame_count, width),
            _utt_spec(frame_count, width),
            pl.BlockSpec((1, width), lambda u, sl, ln: (0, 0)),
            w_spec,
            w_spec,
            pl.BlockSpec((1, frame_count, bottleneck), lambda u, sl, ln: (u, 0, 0)),
            pl.BlockSpec((slots, 1, 1), lambda u, sl, ln: (0, 0, 0)),
        ],
        out_specs=[_utt_spec(frame_count, width), g_spec],
        scratch_shapes=[pltpu.VMEM((slots, width, bottleneck), jnp.float32)],
    )
    d_frames, grads = pl.pallas_call(
        functools.partial(backward_kernel, direct=direct),
        grid_spec=grid_spec,
        out_shape=[
            jax.ShapeDtypeStruct(frames.shape, jnp.bfloat16),
            jax.ShapeDtypeStruct(g_shape, jnp.bfloat16),
        ],
        compiler_params=pltpu.CompilerParams(
            dimension_semantics=("arbitrary",), vmem_limit_bytes=60 * 1024 * 1024
        ),
        cost_estimate=pl.CostEstimate(
            flops=6 * utts * frame_count * width * bottleneck,
            bytes_accessed=3 * frames.size * 2 + 2 * utts * width * bottleneck * 2,
            transcendentals=utts * frame_count * bottleneck,
        ),
    )(own_slot, own_lengths, frames, cotangent, gain.reshape(1, width), w_down, w_up, pre_act,
      own_scale.reshape(slots, 1, 1))
    return d_frames, _to_send(grads, got_down.shape, direct)


def on_device(frames, cotangent, gain, down_weight, up_weight, slot_lang, utt_slot, lengths):
    devices = lax.axis_size("dp")
    self_index = lax.axis_index("dp")
    per_device = frames.shape[0]
    slots = slot_lang.shape[1]
    lang_count, row_count, bottleneck = down_weight.shape
    owners = jnp.arange(utt_slot.shape[0], dtype=jnp.int32) // per_device
    utt_lang = slot_lang[owners, utt_slot]
    own_lengths = lax.dynamic_slice_in_dim(lengths, self_index * per_device, per_device)
    own_slot = lax.dynamic_slice_in_dim(utt_slot, self_index * per_device, per_device)
    lang_ids = jnp.arange(lang_count, dtype=jnp.int32)
    counts = jnp.sum(jnp.where(utt_lang[None, :] == lang_ids[:, None], lengths[None, :], 0), axis=1)
    scaling = lax.rsqrt(jnp.maximum(counts, 1).astype(jnp.float32))
    member_langs = slot_lang.reshape(-1)
    own_scale = jnp.take(scaling, lax.dynamic_index_in_dim(slot_lang, self_index, 0, False))
    exchange = functools.partial(lax.all_to_all, axis_name="dp", split_axis=0, concat_axis=0, tiled=True)
    got_down = exchange(gather_rows(slot_lang, down_weight))
    got_up = exchange(gather_rows(slot_lang, up_weight))
    pre_act, send_up = forward_pass(
        frames, cotangent, gain, got_down, own_slot, own_lengths, own_scale
    )
    back_up = exchange(send_up).reshape(devices * slots, row_count, bottleneck)
    d_frames, send_down = backward_pass(
        frames, cotangent, gain, got_down, got_up, pre_act, own_slot, own_lengths, own_scale
    )
    send_down, back_up = lax.optimization_barrier((send_down, back_up))
    back_down = exchange(send_down).reshape(devices * slots, row_count, bottleneck)
    plan = combine_plan(slot_lang, lang_count)
    up_grads = combine(plan, back_up, lang_count)
    down_grads = combine(plan, back_down, lang_count)
    return (d_frames, down_grads, up_grads)


def solution(mesh):
    placed = (
        P(("groups", "dp"), None, None),
        P(("groups", "dp"), None, None),
        P(),
        P("groups", "dp", None),
        P("groups", "dp", None),
        P("groups", None),
        P("groups"),
        P("groups"),
    )
    return jax.shard_map(
        on_device,
        mesh=mesh,
        in_specs=placed,
        out_specs=(
            P(("groups", "dp"), None, None),
            P("groups", "dp", None),
            P("groups", "dp", None),
        ),
        check_vma=False,
    )
```

```python
import functools

import jax
import jax.numpy as jnp
from jax import lax
from jax.experimental import pallas as pl
from jax.experimental.pallas import tpu as pltpu
from jax.sharding import PartitionSpec as P


def _weights(ref, direct):
    if direct:
        devices, _, row_count, bottleneck = ref.shape
        return ref[:, 0].reshape(devices * row_count, bottleneck)
    return ref[0]


def _flush(acc_ref, scale_ref, out_ref, direct):
    if direct:
        devices, slots, row_count, _ = out_ref.shape
        for dev in range(devices):
            rows = pl.ds(dev * row_count, row_count)
            out_ref[dev] = (acc_ref[:, rows, :] * scale_ref[...]).astype(out_ref.dtype)
    else:
        out_ref[...] = (acc_ref[...] * scale_ref[...]).astype(out_ref.dtype)


def _normalize(frames_ref, gain):
    values = frames_ref[0].astype(jnp.float32)
    centre_mean = jnp.mean(values, axis=1, keepdims=True)
    mean_removed = values - centre_mean
    variance = jnp.mean(mean_removed * mean_removed, axis=1, keepdims=True)
    reciprocal_deviation = lax.rsqrt(variance + 1e-06)
    standardized_input = mean_removed * reciprocal_deviation
    layer_normed = (standardized_input * gain).astype(jnp.bfloat16)
    return reciprocal_deviation, standardized_input, layer_normed


def _masked(cot_ref, length):
    upstream = cot_ref[0]
    live = lax.broadcasted_iota(jnp.int32, (upstream.shape[0], 1), 0) < length
    return upstream, jnp.where(live, upstream, jnp.zeros_like(upstream))


CONTRACT_ROWS = (((0,), (0,)), ((), ()))


def forward_kernel(slot_ref, len_ref, frames_ref, cot_ref, gain_ref, wd_ref, scale_ref,
                   pre_ref, gu_out, gu_ref, *, direct):
    u = pl.program_id(0)

    @pl.when(u == 0)
    def _():
        gu_ref[...] = jnp.zeros_like(gu_ref)

    slot = slot_ref[u]
    _, _, layer_normed = _normalize(frames_ref, gain_ref[...])
    pre_act = jnp.dot(layer_normed, _weights(wd_ref, direct), preferred_element_type=jnp.float32)
    pre_ref[0] = pre_act
    sigmoid_pre = 1.0 / (1.0 + jnp.exp(-pre_act))
    hidden = (pre_act * sigmoid_pre).astype(jnp.bfloat16)
    _, masked_up = _masked(cot_ref, len_ref[u])
    gu_ref[slot] += lax.dot_general(
        masked_up, hidden, CONTRACT_ROWS, preferred_element_type=jnp.float32
    )

    @pl.when(u == pl.num_programs(0) - 1)
    def _():
        _flush(gu_ref, scale_ref, gu_out, direct)


def backward_kernel(slot_ref, len_ref, frames_ref, cot_ref, gain_ref, wd_ref, wu_ref, pre_ref,
                    scale_ref, out_ref, gd_out, gd_ref, *, direct):
    u = pl.program_id(0)

    @pl.when(u == 0)
    def _():
        gd_ref[...] = jnp.zeros_like(gd_ref)

    slot = slot_ref[u]
    gain = gain_ref[...]
    reciprocal_deviation, standardized_input, layer_normed = _normalize(frames_ref, gain)
    pre_act = pre_ref[0]
    sigmoid_pre = 1.0 / (1.0 + jnp.exp(-pre_act))
    upstream, masked_up = _masked(cot_ref, len_ref[u])
    d_hidden = jnp.dot(masked_up, _weights(wu_ref, direct), preferred_element_type=jnp.float32)
    d_pre = (d_hidden * sigmoid_pre * (1.0 + pre_act * (1.0 - sigmoid_pre))).astype(jnp.bfloat16)
    gd_ref[slot] += lax.dot_general(
        layer_normed, d_pre, CONTRACT_ROWS, preferred_element_type=jnp.float32
    )
    d_normed = lax.dot_general(
        d_pre, _weights(wd_ref, direct), (((1,), (1,)), ((), ())),
        preferred_element_type=jnp.float32,
    )
    scaled_rows = d_normed * gain
    inner_gradient = (
        scaled_rows
        - jnp.mean(scaled_rows, axis=1, keepdims=True)
        - standardized_input * jnp.mean(scaled_rows * standardized_input, axis=1, keepdims=True)
    ) * reciprocal_deviation
    out_ref[0] = (upstream.astype(jnp.float32) + inner_gradient).astype(out_ref.dtype)

    @pl.when(u == pl.num_programs(0) - 1)
    def _():
        _flush(gd_ref, scale_ref, gd_out, direct)


def combine_kernel(order_ref, lang_ref, start_ref, back_ref, out_ref, acc_ref):
    block = out_ref.shape[0]
    b = pl.program_id(0)
    base = b * block
    out_ref[...] = jnp.zeros_like(out_ref)
    first_at = start_ref[b]
    end_at = start_ref[b + 1]
    last_member = lang_ref.shape[0] - 1

    def add_member(i, carry):
        m = order_ref[i]
        lang = lang_ref[i]
        first = (i == first_at) | (lang_ref[jnp.maximum(i - 1, 0)] != lang)
        last = (i == end_at - 1) | (lang_ref[jnp.minimum(i + 1, last_member)] != lang)
        val = back_ref[m].astype(jnp.float32)

        @pl.when(first)
        def _():
            acc_ref[...] = val

        @pl.when(jnp.logical_not(first))
        def _():
            acc_ref[...] += val

        @pl.when(last)
        def _():
            out_ref[lang - base] = acc_ref[...].astype(out_ref.dtype)

        return carry

    lax.fori_loop(first_at, end_at, add_member, 0)


def combine_plan(slot_lang, lang_count):
    block = 32 if lang_count % 32 == 0 else (8 if lang_count % 8 == 0 else 1)
    langs = slot_lang.reshape(-1)
    order = jnp.argsort(langs, stable=True).astype(jnp.int32)
    sorted_langs = langs[order].astype(jnp.int32)
    edges = jnp.arange(lang_count // block + 1, dtype=jnp.int32) * block
    starts = jnp.sum((sorted_langs[None, :] < edges[:, None]).astype(jnp.int32), axis=1)
    return block, order, sorted_langs, starts


def combine(plan, back, lang_count):
    block, order, sorted_langs, starts = plan
    members, row_count, bottleneck = back.shape
    grid_spec = pltpu.PrefetchScalarGridSpec(
        num_scalar_prefetch=3,
        grid=(lang_count // block,),
        in_specs=[pl.BlockSpec((members, row_count, bottleneck), lambda b, o, l, st: (0, 0, 0))],
        out_specs=pl.BlockSpec((block, row_count, bottleneck), lambda b, o, l, st: (b, 0, 0)),
        scratch_shapes=[pltpu.VMEM((row_count, bottleneck), jnp.float32)],
    )
    return pl.pallas_call(
        combine_kernel,
        grid_spec=grid_spec,
        out_shape=jax.ShapeDtypeStruct((lang_count, row_count, bottleneck), jnp.bfloat16),
        compiler_params=pltpu.CompilerParams(
            dimension_semantics=("arbitrary",), vmem_limit_bytes=48 * 1024 * 1024
        ),
        cost_estimate=pl.CostEstimate(
            flops=back.size, bytes_accessed=back.size * 2 + lang_count * row_count * bottleneck * 2,
            transcendentals=0,
        ),
    )(order, sorted_langs, starts, back)


def gather_kernel(lang_ref, weight_hbm, out_ref, sems, *, slots):
    members = lang_ref.shape[0]

    def copy(m):
        return pltpu.make_async_copy(
            weight_hbm.at[lang_ref[m]], out_ref.at[m // slots, m % slots], sems.at[m]
        )

    def start(m, carry):
        copy(m).start()
        return carry

    def finish(m, carry):
        copy(m).wait()
        return carry

    lax.fori_loop(0, members, start, 0)
    lax.fori_loop(0, members, finish, 0)


def gather_rows(slot_lang, weight):
    devices, slots = slot_lang.shape
    _, row_count, bottleneck = weight.shape
    members = devices * slots
    grid_spec = pltpu.PrefetchScalarGridSpec(
        num_scalar_prefetch=1,
        grid=(1,),
        in_specs=[pl.BlockSpec(memory_space=pl.ANY)],
        out_specs=pl.BlockSpec((devices, slots, row_count, bottleneck), lambda i, ml: (0, 0, 0, 0)),
        scratch_shapes=[pltpu.SemaphoreType.DMA((members,))],
    )
    size = members * row_count * bottleneck * 2
    return pl.pallas_call(
        functools.partial(gather_kernel, slots=slots),
        grid_spec=grid_spec,
        out_shape=jax.ShapeDtypeStruct((devices, slots, row_count, bottleneck), jnp.bfloat16),
        compiler_params=pltpu.CompilerParams(vmem_limit_bytes=48 * 1024 * 1024),
        cost_estimate=pl.CostEstimate(flops=0, bytes_accessed=2 * size, transcendentals=0),
    )(slot_lang.reshape(-1), weight)


def _layouts(got):
    devices, slots, row_count, bottleneck = got.shape
    width = devices * row_count
    direct = row_count % 16 == 0
    if direct:
        weights = got
        w_spec = pl.BlockSpec((devices, 1, row_count, bottleneck), lambda u, sl, ln: (0, sl[u], 0, 0))
        g_shape = (devices, slots, row_count, bottleneck)
        g_spec = pl.BlockSpec(g_shape, lambda u, sl, ln: (0, 0, 0, 0))
    else:
        weights = got.transpose(1, 0, 2, 3).reshape(slots, width, bottleneck)
        w_spec = pl.BlockSpec((1, width, bottleneck), lambda u, sl, ln: (sl[u], 0, 0))
        g_shape = (slots, width, bottleneck)
        g_spec = pl.BlockSpec(g_shape, lambda u, sl, ln: (0, 0, 0))
    return direct, weights, w_spec, g_shape, g_spec


def _to_send(grads, got_shape, direct):
    if direct:
        return grads
    devices, slots, row_count, bottleneck = got_shape
    return grads.reshape(slots, devices, row_count, bottleneck).transpose(1, 0, 2, 3)


def _utt_spec(frame_count, width):
    return pl.BlockSpec((1, frame_count, width), lambda u, sl, ln: (u, 0, 0))


def forward_pass(frames, cotangent, gain, got_down, own_slot, own_lengths, own_scale):
    utts, frame_count, width = frames.shape
    slots, bottleneck = got_down.shape[1], got_down.shape[3]
    direct, w_down, w_spec, g_shape, g_spec = _layouts(got_down)
    grid_spec = pltpu.PrefetchScalarGridSpec(
        num_scalar_prefetch=2,
        grid=(utts,),
        in_specs=[
            _utt_spec(frame_count, width),
            _utt_spec(frame_count, width),
            pl.BlockSpec((1, width), lambda u, sl, ln: (0, 0)),
            w_spec,
            pl.BlockSpec((slots, 1, 1), lambda u, sl, ln: (0, 0, 0)),
        ],
        out_specs=[
            pl.BlockSpec((1, frame_count, bottleneck), lambda u, sl, ln: (u, 0, 0)),
            g_spec,
        ],
        scratch_shapes=[pltpu.VMEM((slots, width, bottleneck), jnp.float32)],
    )
    pre_act, grads = pl.pallas_call(
        functools.partial(forward_kernel, direct=direct),
        grid_spec=grid_spec,
        out_shape=[
            jax.ShapeDtypeStruct((utts, frame_count, bottleneck), jnp.float32),
            jax.ShapeDtypeStruct(g_shape, jnp.bfloat16),
        ],
        compiler_params=pltpu.CompilerParams(
            dimension_semantics=("arbitrary",), vmem_limit_bytes=60 * 1024 * 1024
        ),
        cost_estimate=pl.CostEstimate(
            flops=4 * utts * frame_count * width * bottleneck,
            bytes_accessed=2 * frames.size * 2 + utts * width * bottleneck * 2,
            transcendentals=utts * frame_count * bottleneck,
        ),
    )(own_slot, own_lengths, frames, cotangent, gain.reshape(1, width), w_down,
      own_scale.reshape(slots, 1, 1))
    return pre_act, _to_send(grads, got_down.shape, direct)


def backward_pass(frames, cotangent, gain, got_down, got_up, pre_act, own_slot, own_lengths,
                  own_scale):
    utts, frame_count, width = frames.shape
    slots, bottleneck = got_down.shape[1], got_down.shape[3]
    direct, w_down, w_spec, g_shape, g_spec = _layouts(got_down)
    _, w_up, _, _, _ = _layouts(got_up)
    grid_spec = pltpu.PrefetchScalarGridSpec(
        num_scalar_prefetch=2,
        grid=(utts,),
        in_specs=[
            _utt_spec(frame_count, width),
            _utt_spec(frame_count, width),
            pl.BlockSpec((1, width), lambda u, sl, ln: (0, 0)),
            w_spec,
            w_spec,
            pl.BlockSpec((1, frame_count, bottleneck), lambda u, sl, ln: (u, 0, 0)),
            pl.BlockSpec((slots, 1, 1), lambda u, sl, ln: (0, 0, 0)),
        ],
        out_specs=[_utt_spec(frame_count, width), g_spec],
        scratch_shapes=[pltpu.VMEM((slots, width, bottleneck), jnp.float32)],
    )
    d_frames, grads = pl.pallas_call(
        functools.partial(backward_kernel, direct=direct),
        grid_spec=grid_spec,
        out_shape=[
            jax.ShapeDtypeStruct(frames.shape, jnp.bfloat16),
            jax.ShapeDtypeStruct(g_shape, jnp.bfloat16),
        ],
        compiler_params=pltpu.CompilerParams(
            dimension_semantics=("arbitrary",), vmem_limit_bytes=60 * 1024 * 1024
        ),
        cost_estimate=pl.CostEstimate(
            flops=6 * utts * frame_count * width * bottleneck,
            bytes_accessed=3 * frames.size * 2 + 2 * utts * width * bottleneck * 2,
            transcendentals=utts * frame_count * bottleneck,
        ),
    )(own_slot, own_lengths, frames, cotangent, gain.reshape(1, width), w_down, w_up, pre_act,
      own_scale.reshape(slots, 1, 1))
    return d_frames, _to_send(grads, got_down.shape, direct)


def exchange_blocks(x, axis):
    n = x.shape[0]
    if n > 16:
        return lax.all_to_all(x, axis, split_axis=0, concat_axis=0, tiled=True)
    me = lax.axis_index(axis)
    ahead = jnp.take(x, (me + jnp.arange(n, dtype=jnp.int32)) % n, axis=0)
    parts = [ahead[0]]
    for shift in range(1, n):
        pairs = [(j, (j + shift) % n) for j in range(n)]
        parts.append(lax.ppermute(ahead[shift], axis, perm=pairs))
    behind = jnp.stack(parts)
    return jnp.take(behind, (me - jnp.arange(n, dtype=jnp.int32)) % n, axis=0)


def on_device(frames, cotangent, gain, down_weight, up_weight, slot_lang, utt_slot, lengths):
    devices = lax.axis_size("dp")
    self_index = lax.axis_index("dp")
    per_device = frames.shape[0]
    slots = slot_lang.shape[1]
    lang_count, row_count, bottleneck = down_weight.shape
    owners = jnp.arange(utt_slot.shape[0], dtype=jnp.int32) // per_device
    utt_lang = slot_lang[owners, utt_slot]
    own_lengths = lax.dynamic_slice_in_dim(lengths, self_index * per_device, per_device)
    own_slot = lax.dynamic_slice_in_dim(utt_slot, self_index * per_device, per_device)
    lang_ids = jnp.arange(lang_count, dtype=jnp.int32)
    counts = jnp.sum(jnp.where(utt_lang[None, :] == lang_ids[:, None], lengths[None, :], 0), axis=1)
    scaling = lax.rsqrt(jnp.maximum(counts, 1).astype(jnp.float32))
    member_langs = slot_lang.reshape(-1)
    own_scale = jnp.take(scaling, lax.dynamic_index_in_dim(slot_lang, self_index, 0, False))
    exchange = functools.partial(exchange_blocks, axis="dp")
    got_down = exchange(gather_rows(slot_lang, down_weight))
    got_up = exchange(gather_rows(slot_lang, up_weight))
    pre_act, send_up = forward_pass(
        frames, cotangent, gain, got_down, own_slot, own_lengths, own_scale
    )
    back_up = exchange(send_up).reshape(devices * slots, row_count, bottleneck)
    d_frames, send_down = backward_pass(
        frames, cotangent, gain, got_down, got_up, pre_act, own_slot, own_lengths, own_scale
    )
    send_down, back_up = lax.optimization_barrier((send_down, back_up))
    back_down = exchange(send_down).reshape(devices * slots, row_count, bottleneck)
    plan = combine_plan(slot_lang, lang_count)
    up_grads = combine(plan, back_up, lang_count)
    down_grads = combine(plan, back_down, lang_count)
    return (d_frames, down_grads, up_grads)


def solution(mesh):
    placed = (
        P(("groups", "dp"), None, None),
        P(("groups", "dp"), None, None),
        P(),
        P("groups", "dp", None),
        P("groups", "dp", None),
        P("groups", None),
        P("groups"),
        P("groups"),
    )
    return jax.shard_map(
        on_device,
        mesh=mesh,
        in_specs=placed,
        out_specs=(
            P(("groups", "dp"), None, None),
            P("groups", "dp", None),
            P("groups", "dp", None),
        ),
        check_vma=False,
    )
```

```python
import functools

import jax
import jax.numpy as jnp
from jax import lax
from jax.experimental import pallas as pl
from jax.experimental.pallas import tpu as pltpu
from jax.sharding import PartitionSpec as P


def _weights(ref, direct):
    if direct:
        devices, _, row_count, bottleneck = ref.shape
        return ref[:, 0].reshape(devices * row_count, bottleneck)
    return ref[0]


def _flush(acc_ref, scale_ref, out_ref, direct):
    if direct:
        devices, slots, row_count, _ = out_ref.shape
        for dev in range(devices):
            rows = pl.ds(dev * row_count, row_count)
            out_ref[dev] = (acc_ref[:, rows, :] * scale_ref[...]).astype(out_ref.dtype)
    else:
        out_ref[...] = (acc_ref[...] * scale_ref[...]).astype(out_ref.dtype)


def _normalize(frames_ref, gain):
    values = frames_ref[0].astype(jnp.float32)
    centre_mean = jnp.mean(values, axis=1, keepdims=True)
    mean_removed = values - centre_mean
    variance = jnp.mean(mean_removed * mean_removed, axis=1, keepdims=True)
    reciprocal_deviation = lax.rsqrt(variance + 1e-06)
    standardized_input = mean_removed * reciprocal_deviation
    layer_normed = (standardized_input * gain).astype(jnp.bfloat16)
    return reciprocal_deviation, standardized_input, layer_normed


def _masked(cot_ref, length):
    upstream = cot_ref[0]
    live = lax.broadcasted_iota(jnp.int32, (upstream.shape[0], 1), 0) < length
    return upstream, jnp.where(live, upstream, jnp.zeros_like(upstream))


CONTRACT_ROWS = (((0,), (0,)), ((), ()))


def forward_kernel(slot_ref, len_ref, frames_ref, cot_ref, gain_ref, wd_ref, scale_ref,
                   pre_ref, gu_out, gu_ref, *, direct):
    u = pl.program_id(0)

    @pl.when(u == 0)
    def _():
        gu_ref[...] = jnp.zeros_like(gu_ref)

    slot = slot_ref[u]
    _, _, layer_normed = _normalize(frames_ref, gain_ref[...])
    pre_act = jnp.dot(layer_normed, _weights(wd_ref, direct), preferred_element_type=jnp.float32)
    pre_ref[0] = pre_act
    sigmoid_pre = 1.0 / (1.0 + jnp.exp(-pre_act))
    hidden = (pre_act * sigmoid_pre).astype(jnp.bfloat16)
    _, masked_up = _masked(cot_ref, len_ref[u])
    gu_ref[slot] += lax.dot_general(
        masked_up, hidden, CONTRACT_ROWS, preferred_element_type=jnp.float32
    )

    @pl.when(u == pl.num_programs(0) - 1)
    def _():
        _flush(gu_ref, scale_ref, gu_out, direct)


def backward_kernel(slot_ref, len_ref, frames_ref, cot_ref, gain_ref, wd_ref, wu_ref, pre_ref,
                    scale_ref, out_ref, gd_out, gd_ref, *, direct):
    u = pl.program_id(0)

    @pl.when(u == 0)
    def _():
        gd_ref[...] = jnp.zeros_like(gd_ref)

    slot = slot_ref[u]
    gain = gain_ref[...]
    reciprocal_deviation, standardized_input, layer_normed = _normalize(frames_ref, gain)
    pre_act = pre_ref[0]
    sigmoid_pre = 1.0 / (1.0 + jnp.exp(-pre_act))
    upstream, masked_up = _masked(cot_ref, len_ref[u])
    d_hidden = jnp.dot(masked_up, _weights(wu_ref, direct), preferred_element_type=jnp.float32)
    d_pre = (d_hidden * sigmoid_pre * (1.0 + pre_act * (1.0 - sigmoid_pre))).astype(jnp.bfloat16)
    gd_ref[slot] += lax.dot_general(
        layer_normed, d_pre, CONTRACT_ROWS, preferred_element_type=jnp.float32
    )
    d_normed = lax.dot_general(
        d_pre, _weights(wd_ref, direct), (((1,), (1,)), ((), ())),
        preferred_element_type=jnp.float32,
    )
    scaled_rows = d_normed * gain
    inner_gradient = (
        scaled_rows
        - jnp.mean(scaled_rows, axis=1, keepdims=True)
        - standardized_input * jnp.mean(scaled_rows * standardized_input, axis=1, keepdims=True)
    ) * reciprocal_deviation
    out_ref[0] = (upstream.astype(jnp.float32) + inner_gradient).astype(out_ref.dtype)

    @pl.when(u == pl.num_programs(0) - 1)
    def _():
        _flush(gd_ref, scale_ref, gd_out, direct)


def combine_kernel(order_ref, lang_ref, start_ref, back_ref, out_ref, *rest):
    acc_ref = rest[-1]
    if len(rest) == 2:
        rest[0][...] = jnp.zeros_like(rest[0])
    block = out_ref.shape[0]
    b = pl.program_id(0)
    base = b * block
    out_ref[...] = jnp.zeros_like(out_ref)
    first_at = start_ref[b]
    end_at = start_ref[b + 1]
    last_member = lang_ref.shape[0] - 1

    def add_member(i, carry):
        m = order_ref[i]
        lang = lang_ref[i]
        first = (i == first_at) | (lang_ref[jnp.maximum(i - 1, 0)] != lang)
        last = (i == end_at - 1) | (lang_ref[jnp.minimum(i + 1, last_member)] != lang)
        val = back_ref[m].astype(jnp.float32)

        @pl.when(first)
        def _():
            acc_ref[...] = val

        @pl.when(jnp.logical_not(first))
        def _():
            acc_ref[...] += val

        @pl.when(last)
        def _():
            out_ref[lang - base] = acc_ref[...].astype(out_ref.dtype)

        return carry

    lax.fori_loop(first_at, end_at, add_member, 0)


def scatter_kernel(order_ref, lang_ref, back_ref, zeros_hbm, out_hbm, acc_ref, stage_ref, sems):
    del zeros_hbm
    members = lang_ref.shape[0]
    last_member = members - 1

    def run_end(i):
        return (i == last_member) | (lang_ref[jnp.minimum(i + 1, last_member)] != lang_ref[i])

    def copy(i):
        return pltpu.make_async_copy(stage_ref.at[i], out_hbm.at[lang_ref[i]], sems.at[i])

    def add_member(i, carry):
        first = (i == 0) | (lang_ref[jnp.maximum(i - 1, 0)] != lang_ref[i])
        val = back_ref[order_ref[i]].astype(jnp.float32)

        @pl.when(first)
        def _():
            acc_ref[...] = val

        @pl.when(jnp.logical_not(first))
        def _():
            acc_ref[...] += val

        @pl.when(run_end(i))
        def _():
            stage_ref[i] = acc_ref[...].astype(stage_ref.dtype)
            copy(i).start()

        return carry

    def finish(i, carry):
        @pl.when(run_end(i))
        def _():
            copy(i).wait()

        return carry

    lax.fori_loop(0, members, add_member, 0)
    lax.fori_loop(0, members, finish, 0)


def scatter_combine(plan, back, zeros):
    _, order, sorted_langs, _ = plan
    members, row_count, bottleneck = back.shape
    lang_count = zeros.shape[0]
    grid_spec = pltpu.PrefetchScalarGridSpec(
        num_scalar_prefetch=2,
        grid=(1,),
        in_specs=[
            pl.BlockSpec((members, row_count, bottleneck), lambda i, o, l: (0, 0, 0)),
            pl.BlockSpec(memory_space=pl.ANY),
        ],
        out_specs=pl.BlockSpec(memory_space=pl.ANY),
        scratch_shapes=[
            pltpu.VMEM((row_count, bottleneck), jnp.float32),
            pltpu.VMEM((members, row_count, bottleneck), jnp.bfloat16),
            pltpu.SemaphoreType.DMA((members,)),
        ],
    )
    return pl.pallas_call(
        scatter_kernel,
        grid_spec=grid_spec,
        out_shape=jax.ShapeDtypeStruct((lang_count, row_count, bottleneck), jnp.bfloat16),
        input_output_aliases={3: 0},
        compiler_params=pltpu.CompilerParams(vmem_limit_bytes=48 * 1024 * 1024),
        cost_estimate=pl.CostEstimate(
            flops=back.size, bytes_accessed=back.size * 4, transcendentals=0
        ),
    )(order, sorted_langs, back, zeros)


def combine_plan(slot_lang, lang_count):
    block = 32 if lang_count % 32 == 0 else (8 if lang_count % 8 == 0 else 1)
    langs = slot_lang.reshape(-1)
    order = jnp.argsort(langs, stable=True).astype(jnp.int32)
    sorted_langs = langs[order].astype(jnp.int32)
    edges = jnp.arange(lang_count // block + 1, dtype=jnp.int32) * block
    starts = jnp.sum((sorted_langs[None, :] < edges[:, None]).astype(jnp.int32), axis=1)
    return block, order, sorted_langs, starts


def combine(plan, back, lang_count, with_zeros=False):
    block, order, sorted_langs, starts = plan
    members, row_count, bottleneck = back.shape
    outputs = 2 if with_zeros else 1
    out_spec = pl.BlockSpec((block, row_count, bottleneck), lambda b, o, l, st: (b, 0, 0))
    out_shape = jax.ShapeDtypeStruct((lang_count, row_count, bottleneck), jnp.bfloat16)
    grid_spec = pltpu.PrefetchScalarGridSpec(
        num_scalar_prefetch=3,
        grid=(lang_count // block,),
        in_specs=[pl.BlockSpec((members, row_count, bottleneck), lambda b, o, l, st: (0, 0, 0))],
        out_specs=[out_spec] * outputs,
        scratch_shapes=[pltpu.VMEM((row_count, bottleneck), jnp.float32)],
    )
    result = pl.pallas_call(
        combine_kernel,
        grid_spec=grid_spec,
        out_shape=[out_shape] * outputs,
        compiler_params=pltpu.CompilerParams(
            dimension_semantics=("arbitrary",), vmem_limit_bytes=48 * 1024 * 1024
        ),
        cost_estimate=pl.CostEstimate(
            flops=back.size,
            bytes_accessed=back.size * 2 + outputs * lang_count * row_count * bottleneck * 2,
            transcendentals=0,
        ),
    )(order, sorted_langs, starts, back)
    return tuple(result) if with_zeros else result[0]


def gather_kernel(lang_ref, weight_hbm, out_ref, sems, *, slots):
    members = lang_ref.shape[0]

    def copy(m):
        return pltpu.make_async_copy(
            weight_hbm.at[lang_ref[m]], out_ref.at[m // slots, m % slots], sems.at[m]
        )

    def start(m, carry):
        copy(m).start()
        return carry

    def finish(m, carry):
        copy(m).wait()
        return carry

    lax.fori_loop(0, members, start, 0)
    lax.fori_loop(0, members, finish, 0)


def gather_rows(slot_lang, weight):
    devices, slots = slot_lang.shape
    _, row_count, bottleneck = weight.shape
    members = devices * slots
    grid_spec = pltpu.PrefetchScalarGridSpec(
        num_scalar_prefetch=1,
        grid=(1,),
        in_specs=[pl.BlockSpec(memory_space=pl.ANY)],
        out_specs=pl.BlockSpec((devices, slots, row_count, bottleneck), lambda i, ml: (0, 0, 0, 0)),
        scratch_shapes=[pltpu.SemaphoreType.DMA((members,))],
    )
    size = members * row_count * bottleneck * 2
    return pl.pallas_call(
        functools.partial(gather_kernel, slots=slots),
        grid_spec=grid_spec,
        out_shape=jax.ShapeDtypeStruct((devices, slots, row_count, bottleneck), jnp.bfloat16),
        compiler_params=pltpu.CompilerParams(vmem_limit_bytes=48 * 1024 * 1024),
        cost_estimate=pl.CostEstimate(flops=0, bytes_accessed=2 * size, transcendentals=0),
    )(slot_lang.reshape(-1), weight)


def _layouts(got):
    devices, slots, row_count, bottleneck = got.shape
    width = devices * row_count
    direct = row_count % 16 == 0
    if direct:
        weights = got
        w_spec = pl.BlockSpec((devices, 1, row_count, bottleneck), lambda u, sl, ln: (0, sl[u], 0, 0))
        g_shape = (devices, slots, row_count, bottleneck)
        g_spec = pl.BlockSpec(g_shape, lambda u, sl, ln: (0, 0, 0, 0))
    else:
        weights = got.transpose(1, 0, 2, 3).reshape(slots, width, bottleneck)
        w_spec = pl.BlockSpec((1, width, bottleneck), lambda u, sl, ln: (sl[u], 0, 0))
        g_shape = (slots, width, bottleneck)
        g_spec = pl.BlockSpec(g_shape, lambda u, sl, ln: (0, 0, 0))
    return direct, weights, w_spec, g_shape, g_spec


def _to_send(grads, got_shape, direct):
    if direct:
        return grads
    devices, slots, row_count, bottleneck = got_shape
    return grads.reshape(slots, devices, row_count, bottleneck).transpose(1, 0, 2, 3)


def _utt_spec(frame_count, width):
    return pl.BlockSpec((1, frame_count, width), lambda u, sl, ln: (u, 0, 0))


def forward_pass(frames, cotangent, gain, got_down, own_slot, own_lengths, own_scale):
    utts, frame_count, width = frames.shape
    slots, bottleneck = got_down.shape[1], got_down.shape[3]
    direct, w_down, w_spec, g_shape, g_spec = _layouts(got_down)
    grid_spec = pltpu.PrefetchScalarGridSpec(
        num_scalar_prefetch=2,
        grid=(utts,),
        in_specs=[
            _utt_spec(frame_count, width),
            _utt_spec(frame_count, width),
            pl.BlockSpec((1, width), lambda u, sl, ln: (0, 0)),
            w_spec,
            pl.BlockSpec((slots, 1, 1), lambda u, sl, ln: (0, 0, 0)),
        ],
        out_specs=[
            pl.BlockSpec((1, frame_count, bottleneck), lambda u, sl, ln: (u, 0, 0)),
            g_spec,
        ],
        scratch_shapes=[pltpu.VMEM((slots, width, bottleneck), jnp.float32)],
    )
    pre_act, grads = pl.pallas_call(
        functools.partial(forward_kernel, direct=direct),
        grid_spec=grid_spec,
        out_shape=[
            jax.ShapeDtypeStruct((utts, frame_count, bottleneck), jnp.float32),
            jax.ShapeDtypeStruct(g_shape, jnp.bfloat16),
        ],
        compiler_params=pltpu.CompilerParams(
            dimension_semantics=("arbitrary",), vmem_limit_bytes=60 * 1024 * 1024
        ),
        cost_estimate=pl.CostEstimate(
            flops=4 * utts * frame_count * width * bottleneck,
            bytes_accessed=2 * frames.size * 2 + utts * width * bottleneck * 2,
            transcendentals=utts * frame_count * bottleneck,
        ),
    )(own_slot, own_lengths, frames, cotangent, gain.reshape(1, width), w_down,
      own_scale.reshape(slots, 1, 1))
    return pre_act, _to_send(grads, got_down.shape, direct)


def backward_pass(frames, cotangent, gain, got_down, got_up, pre_act, own_slot, own_lengths,
                  own_scale):
    utts, frame_count, width = frames.shape
    slots, bottleneck = got_down.shape[1], got_down.shape[3]
    direct, w_down, w_spec, g_shape, g_spec = _layouts(got_down)
    _, w_up, _, _, _ = _layouts(got_up)
    grid_spec = pltpu.PrefetchScalarGridSpec(
        num_scalar_prefetch=2,
        grid=(utts,),
        in_specs=[
            _utt_spec(frame_count, width),
            _utt_spec(frame_count, width),
            pl.BlockSpec((1, width), lambda u, sl, ln: (0, 0)),
            w_spec,
            w_spec,
            pl.BlockSpec((1, frame_count, bottleneck), lambda u, sl, ln: (u, 0, 0)),
            pl.BlockSpec((slots, 1, 1), lambda u, sl, ln: (0, 0, 0)),
        ],
        out_specs=[_utt_spec(frame_count, width), g_spec],
        scratch_shapes=[pltpu.VMEM((slots, width, bottleneck), jnp.float32)],
    )
    d_frames, grads = pl.pallas_call(
        functools.partial(backward_kernel, direct=direct),
        grid_spec=grid_spec,
        out_shape=[
            jax.ShapeDtypeStruct(frames.shape, jnp.bfloat16),
            jax.ShapeDtypeStruct(g_shape, jnp.bfloat16),
        ],
        compiler_params=pltpu.CompilerParams(
            dimension_semantics=("arbitrary",), vmem_limit_bytes=60 * 1024 * 1024
        ),
        cost_estimate=pl.CostEstimate(
            flops=6 * utts * frame_count * width * bottleneck,
            bytes_accessed=3 * frames.size * 2 + 2 * utts * width * bottleneck * 2,
            transcendentals=utts * frame_count * bottleneck,
        ),
    )(own_slot, own_lengths, frames, cotangent, gain.reshape(1, width), w_down, w_up, pre_act,
      own_scale.reshape(slots, 1, 1))
    return d_frames, _to_send(grads, got_down.shape, direct)


def on_device(frames, cotangent, gain, down_weight, up_weight, slot_lang, utt_slot, lengths):
    devices = lax.axis_size("dp")
    self_index = lax.axis_index("dp")
    per_device = frames.shape[0]
    slots = slot_lang.shape[1]
    lang_count, row_count, bottleneck = down_weight.shape
    owners = jnp.arange(utt_slot.shape[0], dtype=jnp.int32) // per_device
    utt_lang = slot_lang[owners, utt_slot]
    own_lengths = lax.dynamic_slice_in_dim(lengths, self_index * per_device, per_device)
    own_slot = lax.dynamic_slice_in_dim(utt_slot, self_index * per_device, per_device)
    lang_ids = jnp.arange(lang_count, dtype=jnp.int32)
    counts = jnp.sum(jnp.where(utt_lang[None, :] == lang_ids[:, None], lengths[None, :], 0), axis=1)
    scaling = lax.rsqrt(jnp.maximum(counts, 1).astype(jnp.float32))
    member_langs = slot_lang.reshape(-1)
    own_scale = jnp.take(scaling, lax.dynamic_index_in_dim(slot_lang, self_index, 0, False))
    exchange = functools.partial(lax.all_to_all, axis_name="dp", split_axis=0, concat_axis=0, tiled=True)
    got_down = exchange(gather_rows(slot_lang, down_weight))
    got_up = exchange(gather_rows(slot_lang, up_weight))
    pre_act, send_up = forward_pass(
        frames, cotangent, gain, got_down, own_slot, own_lengths, own_scale
    )
    back_up = exchange(send_up).reshape(devices * slots, row_count, bottleneck)
    d_frames, send_down = backward_pass(
        frames, cotangent, gain, got_down, got_up, pre_act, own_slot, own_lengths, own_scale
    )
    send_down, back_up = lax.optimization_barrier((send_down, back_up))
    back_down = exchange(send_down).reshape(devices * slots, row_count, bottleneck)
    plan = combine_plan(slot_lang, lang_count)
    up_grads, zeros = combine(plan, back_up, lang_count, with_zeros=True)
    down_grads = scatter_combine(plan, back_down, zeros)
    return (d_frames, down_grads, up_grads)


def solution(mesh):
    placed = (
        P(("groups", "dp"), None, None),
        P(("groups", "dp"), None, None),
        P(),
        P("groups", "dp", None),
        P("groups", "dp", None),
        P("groups", None),
        P("groups"),
        P("groups"),
    )
    return jax.shard_map(
        on_device,
        mesh=mesh,
        in_specs=placed,
        out_specs=(
            P(("groups", "dp"), None, None),
            P("groups", "dp", None),
            P("groups", "dp", None),
        ),
        check_vma=False,
    )
```

```python
import functools

import jax
import jax.numpy as jnp
from jax import lax
from jax.experimental import pallas as pl
from jax.experimental.pallas import tpu as pltpu
from jax.sharding import PartitionSpec as P


def _weights(ref, direct):
    if direct:
        devices, _, row_count, bottleneck = ref.shape
        return ref[:, 0].reshape(devices * row_count, bottleneck)
    return ref[0]


def _flush(acc_ref, scale_ref, out_ref, direct):
    if direct:
        devices, slots, row_count, _ = out_ref.shape
        for dev in range(devices):
            rows = pl.ds(dev * row_count, row_count)
            out_ref[dev] = (acc_ref[:, rows, :] * scale_ref[...]).astype(out_ref.dtype)
    else:
        out_ref[...] = (acc_ref[...] * scale_ref[...]).astype(out_ref.dtype)


def _normalize(frames_ref, gain):
    values = frames_ref[0].astype(jnp.float32)
    centre_mean = jnp.mean(values, axis=1, keepdims=True)
    mean_removed = values - centre_mean
    variance = jnp.mean(mean_removed * mean_removed, axis=1, keepdims=True)
    reciprocal_deviation = lax.rsqrt(variance + 1e-06)
    standardized_input = mean_removed * reciprocal_deviation
    layer_normed = (standardized_input * gain).astype(jnp.bfloat16)
    return reciprocal_deviation, standardized_input, layer_normed


def _masked(cot_ref, length):
    upstream = cot_ref[0]
    live = lax.broadcasted_iota(jnp.int32, (upstream.shape[0], 1), 0) < length
    return upstream, jnp.where(live, upstream, jnp.zeros_like(upstream))


CONTRACT_ROWS = (((0,), (0,)), ((), ()))


def forward_kernel(slot_ref, len_ref, frames_ref, cot_ref, gain_ref, wd_ref, scale_ref,
                   pre_ref, gu_out, gu_ref, *, direct):
    u = pl.program_id(0)

    @pl.when(u == 0)
    def _():
        gu_ref[...] = jnp.zeros_like(gu_ref)

    slot = slot_ref[u]
    _, _, layer_normed = _normalize(frames_ref, gain_ref[...])
    pre_act = jnp.dot(layer_normed, _weights(wd_ref, direct), preferred_element_type=jnp.float32)
    pre_ref[0] = pre_act
    sigmoid_pre = 1.0 / (1.0 + jnp.exp(-pre_act))
    hidden = (pre_act * sigmoid_pre).astype(jnp.bfloat16)
    _, masked_up = _masked(cot_ref, len_ref[u])
    gu_ref[slot] += lax.dot_general(
        masked_up, hidden, CONTRACT_ROWS, preferred_element_type=jnp.float32
    )

    @pl.when(u == pl.num_programs(0) - 1)
    def _():
        _flush(gu_ref, scale_ref, gu_out, direct)


def backward_kernel(slot_ref, len_ref, frames_ref, cot_ref, gain_ref, wd_ref, wu_ref, pre_ref,
                    scale_ref, out_ref, gd_out, gd_ref, *, direct):
    u = pl.program_id(0)

    @pl.when(u == 0)
    def _():
        gd_ref[...] = jnp.zeros_like(gd_ref)

    slot = slot_ref[u]
    gain = gain_ref[...]
    reciprocal_deviation, standardized_input, layer_normed = _normalize(frames_ref, gain)
    pre_act = pre_ref[0]
    sigmoid_pre = 1.0 / (1.0 + jnp.exp(-pre_act))
    upstream, masked_up = _masked(cot_ref, len_ref[u])
    d_hidden = jnp.dot(masked_up, _weights(wu_ref, direct), preferred_element_type=jnp.float32)
    d_pre = (d_hidden * sigmoid_pre * (1.0 + pre_act * (1.0 - sigmoid_pre))).astype(jnp.bfloat16)
    gd_ref[slot] += lax.dot_general(
        layer_normed, d_pre, CONTRACT_ROWS, preferred_element_type=jnp.float32
    )
    d_normed = lax.dot_general(
        d_pre, _weights(wd_ref, direct), (((1,), (1,)), ((), ())),
        preferred_element_type=jnp.float32,
    )
    scaled_rows = d_normed * gain
    inner_gradient = (
        scaled_rows
        - jnp.mean(scaled_rows, axis=1, keepdims=True)
        - standardized_input * jnp.mean(scaled_rows * standardized_input, axis=1, keepdims=True)
    ) * reciprocal_deviation
    out_ref[0] = (upstream.astype(jnp.float32) + inner_gradient).astype(out_ref.dtype)

    @pl.when(u == pl.num_programs(0) - 1)
    def _():
        _flush(gd_ref, scale_ref, gd_out, direct)


def combine_kernel(order_ref, lang_ref, start_ref, back_ref, out_ref, *rest):
    acc_ref = rest[-1]
    if len(rest) == 2:
        rest[0][...] = jnp.zeros_like(rest[0])
    block = out_ref.shape[0]
    b = pl.program_id(0)
    base = b * block
    out_ref[...] = jnp.zeros_like(out_ref)
    first_at = start_ref[b]
    end_at = start_ref[b + 1]
    last_member = lang_ref.shape[0] - 1

    def add_member(i, carry):
        m = order_ref[i]
        lang = lang_ref[i]
        first = (i == first_at) | (lang_ref[jnp.maximum(i - 1, 0)] != lang)
        last = (i == end_at - 1) | (lang_ref[jnp.minimum(i + 1, last_member)] != lang)
        val = back_ref[m].astype(jnp.float32)

        @pl.when(first)
        def _():
            acc_ref[...] = val

        @pl.when(jnp.logical_not(first))
        def _():
            acc_ref[...] += val

        @pl.when(last)
        def _():
            out_ref[lang - base] = acc_ref[...].astype(out_ref.dtype)

        return carry

    lax.fori_loop(first_at, end_at, add_member, 0)


def scatter_kernel(order_ref, lang_ref, back_ref, zeros_hbm, out_hbm, acc_ref, stage_ref, sems):
    del zeros_hbm
    members = lang_ref.shape[0]
    last_member = members - 1

    def run_end(i):
        return (i == last_member) | (lang_ref[jnp.minimum(i + 1, last_member)] != lang_ref[i])

    def copy(i):
        return pltpu.make_async_copy(stage_ref.at[i], out_hbm.at[lang_ref[i]], sems.at[i])

    def add_member(i, carry):
        first = (i == 0) | (lang_ref[jnp.maximum(i - 1, 0)] != lang_ref[i])
        val = back_ref[order_ref[i]].astype(jnp.float32)

        @pl.when(first)
        def _():
            acc_ref[...] = val

        @pl.when(jnp.logical_not(first))
        def _():
            acc_ref[...] += val

        @pl.when(run_end(i))
        def _():
            stage_ref[i] = acc_ref[...].astype(stage_ref.dtype)
            copy(i).start()

        return carry

    def finish(i, carry):
        @pl.when(run_end(i))
        def _():
            copy(i).wait()

        return carry

    lax.fori_loop(0, members, add_member, 0)
    lax.fori_loop(0, members, finish, 0)


def scatter_combine(plan, back, zeros):
    _, order, sorted_langs, _ = plan
    members, row_count, bottleneck = back.shape
    lang_count = zeros.shape[0]
    grid_spec = pltpu.PrefetchScalarGridSpec(
        num_scalar_prefetch=2,
        grid=(1,),
        in_specs=[
            pl.BlockSpec((members, row_count, bottleneck), lambda i, o, l: (0, 0, 0)),
            pl.BlockSpec(memory_space=pl.ANY),
        ],
        out_specs=pl.BlockSpec(memory_space=pl.ANY),
        scratch_shapes=[
            pltpu.VMEM((row_count, bottleneck), jnp.float32),
            pltpu.VMEM((members, row_count, bottleneck), jnp.bfloat16),
            pltpu.SemaphoreType.DMA((members,)),
        ],
    )
    return pl.pallas_call(
        scatter_kernel,
        grid_spec=grid_spec,
        out_shape=jax.ShapeDtypeStruct((lang_count, row_count, bottleneck), jnp.bfloat16),
        input_output_aliases={3: 0},
        compiler_params=pltpu.CompilerParams(vmem_limit_bytes=48 * 1024 * 1024),
        cost_estimate=pl.CostEstimate(
            flops=back.size, bytes_accessed=back.size * 4, transcendentals=0
        ),
    )(order, sorted_langs, back, zeros)


def combine_plan(slot_lang, lang_count):
    block = 32 if lang_count % 32 == 0 else (8 if lang_count % 8 == 0 else 1)
    langs = slot_lang.reshape(-1)
    order = jnp.argsort(langs, stable=True).astype(jnp.int32)
    sorted_langs = langs[order].astype(jnp.int32)
    edges = jnp.arange(lang_count // block + 1, dtype=jnp.int32) * block
    starts = jnp.sum((sorted_langs[None, :] < edges[:, None]).astype(jnp.int32), axis=1)
    return block, order, sorted_langs, starts


def combine(plan, back, lang_count, with_zeros=False):
    block, order, sorted_langs, starts = plan
    members, row_count, bottleneck = back.shape
    outputs = 2 if with_zeros else 1
    out_spec = pl.BlockSpec((block, row_count, bottleneck), lambda b, o, l, st: (b, 0, 0))
    out_shape = jax.ShapeDtypeStruct((lang_count, row_count, bottleneck), jnp.bfloat16)
    grid_spec = pltpu.PrefetchScalarGridSpec(
        num_scalar_prefetch=3,
        grid=(lang_count // block,),
        in_specs=[pl.BlockSpec((members, row_count, bottleneck), lambda b, o, l, st: (0, 0, 0))],
        out_specs=[out_spec] * outputs,
        scratch_shapes=[pltpu.VMEM((row_count, bottleneck), jnp.float32)],
    )
    result = pl.pallas_call(
        combine_kernel,
        grid_spec=grid_spec,
        out_shape=[out_shape] * outputs,
        compiler_params=pltpu.CompilerParams(
            dimension_semantics=("arbitrary",), vmem_limit_bytes=48 * 1024 * 1024
        ),
        cost_estimate=pl.CostEstimate(
            flops=back.size,
            bytes_accessed=back.size * 2 + outputs * lang_count * row_count * bottleneck * 2,
            transcendentals=0,
        ),
    )(order, sorted_langs, starts, back)
    return tuple(result) if with_zeros else result[0]


def gather_kernel(lang_ref, weight_hbm, out_hbm, stage_ref, sems_in, sems_out, *, slots):
    members = lang_ref.shape[0]

    def copy_in(m):
        return pltpu.make_async_copy(weight_hbm.at[lang_ref[m]], stage_ref.at[m], sems_in.at[m])

    def copy_out(m):
        return pltpu.make_async_copy(
            stage_ref.at[m], out_hbm.at[m // slots, m % slots], sems_out.at[m]
        )

    def start(m, carry):
        copy_in(m).start()
        return carry

    def forward(m, carry):
        copy_in(m).wait()
        copy_out(m).start()
        return carry

    def finish(m, carry):
        copy_out(m).wait()
        return carry

    lax.fori_loop(0, members, start, 0)
    lax.fori_loop(0, members, forward, 0)
    lax.fori_loop(0, members, finish, 0)


def gather_rows(slot_lang, weight):
    devices, slots = slot_lang.shape
    _, row_count, bottleneck = weight.shape
    members = devices * slots
    grid_spec = pltpu.PrefetchScalarGridSpec(
        num_scalar_prefetch=1,
        grid=(1,),
        in_specs=[pl.BlockSpec(memory_space=pl.ANY)],
        out_specs=pl.BlockSpec(memory_space=pl.ANY),
        scratch_shapes=[
            pltpu.VMEM((members, row_count, bottleneck), weight.dtype),
            pltpu.SemaphoreType.DMA((members,)),
            pltpu.SemaphoreType.DMA((members,)),
        ],
    )
    size = members * row_count * bottleneck * 2
    return pl.pallas_call(
        functools.partial(gather_kernel, slots=slots),
        grid_spec=grid_spec,
        out_shape=jax.ShapeDtypeStruct((devices, slots, row_count, bottleneck), weight.dtype),
        compiler_params=pltpu.CompilerParams(vmem_limit_bytes=48 * 1024 * 1024),
        cost_estimate=pl.CostEstimate(flops=0, bytes_accessed=2 * size, transcendentals=0),
    )(slot_lang.reshape(-1), weight)


def _layouts(got):
    devices, slots, row_count, bottleneck = got.shape
    width = devices * row_count
    direct = row_count % 16 == 0
    if direct:
        weights = got
        w_spec = pl.BlockSpec((devices, 1, row_count, bottleneck), lambda u, sl, ln: (0, sl[u], 0, 0))
        g_shape = (devices, slots, row_count, bottleneck)
        g_spec = pl.BlockSpec(g_shape, lambda u, sl, ln: (0, 0, 0, 0))
    else:
        weights = got.transpose(1, 0, 2, 3).reshape(slots, width, bottleneck)
        w_spec = pl.BlockSpec((1, width, bottleneck), lambda u, sl, ln: (sl[u], 0, 0))
        g_shape = (slots, width, bottleneck)
        g_spec = pl.BlockSpec(g_shape, lambda u, sl, ln: (0, 0, 0))
    return direct, weights, w_spec, g_shape, g_spec


def _to_send(grads, got_shape, direct):
    if direct:
        return grads
    devices, slots, row_count, bottleneck = got_shape
    return grads.reshape(slots, devices, row_count, bottleneck).transpose(1, 0, 2, 3)


def _utt_spec(frame_count, width):
    return pl.BlockSpec((1, frame_count, width), lambda u, sl, ln: (u, 0, 0))


def forward_pass(frames, cotangent, gain, got_down, own_slot, own_lengths, own_scale):
    utts, frame_count, width = frames.shape
    slots, bottleneck = got_down.shape[1], got_down.shape[3]
    direct, w_down, w_spec, g_shape, g_spec = _layouts(got_down)
    grid_spec = pltpu.PrefetchScalarGridSpec(
        num_scalar_prefetch=2,
        grid=(utts,),
        in_specs=[
            _utt_spec(frame_count, width),
            _utt_spec(frame_count, width),
            pl.BlockSpec((1, width), lambda u, sl, ln: (0, 0)),
            w_spec,
            pl.BlockSpec((slots, 1, 1), lambda u, sl, ln: (0, 0, 0)),
        ],
        out_specs=[
            pl.BlockSpec((1, frame_count, bottleneck), lambda u, sl, ln: (u, 0, 0)),
            g_spec,
        ],
        scratch_shapes=[pltpu.VMEM((slots, width, bottleneck), jnp.float32)],
    )
    pre_act, grads = pl.pallas_call(
        functools.partial(forward_kernel, direct=direct),
        grid_spec=grid_spec,
        out_shape=[
            jax.ShapeDtypeStruct((utts, frame_count, bottleneck), jnp.float32),
            jax.ShapeDtypeStruct(g_shape, jnp.bfloat16),
        ],
        compiler_params=pltpu.CompilerParams(
            dimension_semantics=("arbitrary",), vmem_limit_bytes=60 * 1024 * 1024
        ),
        cost_estimate=pl.CostEstimate(
            flops=4 * utts * frame_count * width * bottleneck,
            bytes_accessed=2 * frames.size * 2 + utts * width * bottleneck * 2,
            transcendentals=utts * frame_count * bottleneck,
        ),
    )(own_slot, own_lengths, frames, cotangent, gain.reshape(1, width), w_down,
      own_scale.reshape(slots, 1, 1))
    return pre_act, _to_send(grads, got_down.shape, direct)


def backward_pass(frames, cotangent, gain, got_down, got_up, pre_act, own_slot, own_lengths,
                  own_scale):
    utts, frame_count, width = frames.shape
    slots, bottleneck = got_down.shape[1], got_down.shape[3]
    direct, w_down, w_spec, g_shape, g_spec = _layouts(got_down)
    _, w_up, _, _, _ = _layouts(got_up)
    grid_spec = pltpu.PrefetchScalarGridSpec(
        num_scalar_prefetch=2,
        grid=(utts,),
        in_specs=[
            _utt_spec(frame_count, width),
            _utt_spec(frame_count, width),
            pl.BlockSpec((1, width), lambda u, sl, ln: (0, 0)),
            w_spec,
            w_spec,
            pl.BlockSpec((1, frame_count, bottleneck), lambda u, sl, ln: (u, 0, 0)),
            pl.BlockSpec((slots, 1, 1), lambda u, sl, ln: (0, 0, 0)),
        ],
        out_specs=[_utt_spec(frame_count, width), g_spec],
        scratch_shapes=[pltpu.VMEM((slots, width, bottleneck), jnp.float32)],
    )
    d_frames, grads = pl.pallas_call(
        functools.partial(backward_kernel, direct=direct),
        grid_spec=grid_spec,
        out_shape=[
            jax.ShapeDtypeStruct(frames.shape, jnp.bfloat16),
            jax.ShapeDtypeStruct(g_shape, jnp.bfloat16),
        ],
        compiler_params=pltpu.CompilerParams(
            dimension_semantics=("arbitrary",), vmem_limit_bytes=60 * 1024 * 1024
        ),
        cost_estimate=pl.CostEstimate(
            flops=6 * utts * frame_count * width * bottleneck,
            bytes_accessed=3 * frames.size * 2 + 2 * utts * width * bottleneck * 2,
            transcendentals=utts * frame_count * bottleneck,
        ),
    )(own_slot, own_lengths, frames, cotangent, gain.reshape(1, width), w_down, w_up, pre_act,
      own_scale.reshape(slots, 1, 1))
    return d_frames, _to_send(grads, got_down.shape, direct)


def on_device(frames, cotangent, gain, down_weight, up_weight, slot_lang, utt_slot, lengths):
    devices = lax.axis_size("dp")
    self_index = lax.axis_index("dp")
    per_device = frames.shape[0]
    slots = slot_lang.shape[1]
    lang_count, row_count, bottleneck = down_weight.shape
    owners = jnp.arange(utt_slot.shape[0], dtype=jnp.int32) // per_device
    utt_lang = slot_lang[owners, utt_slot]
    own_lengths = lax.dynamic_slice_in_dim(lengths, self_index * per_device, per_device)
    own_slot = lax.dynamic_slice_in_dim(utt_slot, self_index * per_device, per_device)
    lang_ids = jnp.arange(lang_count, dtype=jnp.int32)
    counts = jnp.sum(jnp.where(utt_lang[None, :] == lang_ids[:, None], lengths[None, :], 0), axis=1)
    scaling = lax.rsqrt(jnp.maximum(counts, 1).astype(jnp.float32))
    member_langs = slot_lang.reshape(-1)
    own_scale = jnp.take(scaling, lax.dynamic_index_in_dim(slot_lang, self_index, 0, False))
    exchange = functools.partial(lax.all_to_all, axis_name="dp", split_axis=0, concat_axis=0, tiled=True)
    got_down = exchange(gather_rows(slot_lang, down_weight))
    got_up = exchange(gather_rows(slot_lang, up_weight))
    pre_act, send_up = forward_pass(
        frames, cotangent, gain, got_down, own_slot, own_lengths, own_scale
    )
    back_up = exchange(send_up).reshape(devices * slots, row_count, bottleneck)
    d_frames, send_down = backward_pass(
        frames, cotangent, gain, got_down, got_up, pre_act, own_slot, own_lengths, own_scale
    )
    send_down, back_up = lax.optimization_barrier((send_down, back_up))
    back_down = exchange(send_down).reshape(devices * slots, row_count, bottleneck)
    plan = combine_plan(slot_lang, lang_count)
    up_grads, zeros = combine(plan, back_up, lang_count, with_zeros=True)
    down_grads = scatter_combine(plan, back_down, zeros)
    return (d_frames, down_grads, up_grads)


def solution(mesh):
    placed = (
        P(("groups", "dp"), None, None),
        P(("groups", "dp"), None, None),
        P(),
        P("groups", "dp", None),
        P("groups", "dp", None),
        P("groups", None),
        P("groups"),
        P("groups"),
    )
    return jax.shard_map(
        on_device,
        mesh=mesh,
        in_specs=placed,
        out_specs=(
            P(("groups", "dp"), None, None),
            P("groups", "dp", None),
            P("groups", "dp", None),
        ),
        check_vma=False,
    )
```

```python
import functools

import jax
import jax.numpy as jnp
from jax import lax
from jax.experimental import pallas as pl
from jax.experimental.pallas import tpu as pltpu
from jax.sharding import PartitionSpec as P


def _weights(ref, direct):
    if direct:
        devices, _, row_count, bottleneck = ref.shape
        return ref[:, 0].reshape(devices * row_count, bottleneck)
    return ref[0]


def _flush(acc_ref, scale_ref, out_ref, direct):
    if direct:
        devices, slots, row_count, _ = out_ref.shape
        for dev in range(devices):
            rows = pl.ds(dev * row_count, row_count)
            out_ref[dev] = (acc_ref[:, rows, :] * scale_ref[...]).astype(out_ref.dtype)
    else:
        out_ref[...] = (acc_ref[...] * scale_ref[...]).astype(out_ref.dtype)


def _normalize(frames_ref, gain):
    values = frames_ref[0].astype(jnp.float32)
    centre_mean = jnp.mean(values, axis=1, keepdims=True)
    mean_removed = values - centre_mean
    variance = jnp.mean(mean_removed * mean_removed, axis=1, keepdims=True)
    reciprocal_deviation = lax.rsqrt(variance + 1e-06)
    standardized_input = mean_removed * reciprocal_deviation
    layer_normed = (standardized_input * gain).astype(jnp.bfloat16)
    return reciprocal_deviation, standardized_input, layer_normed


def _masked(cot_ref, length):
    upstream = cot_ref[0]
    live = lax.broadcasted_iota(jnp.int32, (upstream.shape[0], 1), 0) < length
    return upstream, jnp.where(live, upstream, jnp.zeros_like(upstream))


CONTRACT_ROWS = (((0,), (0,)), ((), ()))


def forward_kernel(slot_ref, len_ref, frames_ref, cot_ref, gain_ref, wd_ref, scale_ref,
                   pre_ref, gu_out, gu_ref, *, direct):
    u = pl.program_id(0)

    @pl.when(u == 0)
    def _():
        gu_ref[...] = jnp.zeros_like(gu_ref)

    slot = slot_ref[u]
    _, _, layer_normed = _normalize(frames_ref, gain_ref[...])
    pre_act = jnp.dot(layer_normed, _weights(wd_ref, direct), preferred_element_type=jnp.float32)
    pre_ref[0] = pre_act
    sigmoid_pre = 1.0 / (1.0 + jnp.exp(-pre_act))
    hidden = (pre_act * sigmoid_pre).astype(jnp.bfloat16)
    _, masked_up = _masked(cot_ref, len_ref[u])
    gu_ref[slot] += lax.dot_general(
        masked_up, hidden, CONTRACT_ROWS, preferred_element_type=jnp.float32
    )

    @pl.when(u == pl.num_programs(0) - 1)
    def _():
        _flush(gu_ref, scale_ref, gu_out, direct)


def backward_kernel(slot_ref, len_ref, frames_ref, cot_ref, gain_ref, wd_ref, wu_ref, pre_ref,
                    scale_ref, out_ref, gd_out, gd_ref, *, direct):
    u = pl.program_id(0)

    @pl.when(u == 0)
    def _():
        gd_ref[...] = jnp.zeros_like(gd_ref)

    slot = slot_ref[u]
    gain = gain_ref[...]
    reciprocal_deviation, standardized_input, layer_normed = _normalize(frames_ref, gain)
    pre_act = pre_ref[0]
    sigmoid_pre = 1.0 / (1.0 + jnp.exp(-pre_act))
    upstream, masked_up = _masked(cot_ref, len_ref[u])
    d_hidden = jnp.dot(masked_up, _weights(wu_ref, direct), preferred_element_type=jnp.float32)
    d_pre = (d_hidden * sigmoid_pre * (1.0 + pre_act * (1.0 - sigmoid_pre))).astype(jnp.bfloat16)
    gd_ref[slot] += lax.dot_general(
        layer_normed, d_pre, CONTRACT_ROWS, preferred_element_type=jnp.float32
    )
    d_normed = lax.dot_general(
        d_pre, _weights(wd_ref, direct), (((1,), (1,)), ((), ())),
        preferred_element_type=jnp.float32,
    )
    scaled_rows = d_normed * gain
    inner_gradient = (
        scaled_rows
        - jnp.mean(scaled_rows, axis=1, keepdims=True)
        - standardized_input * jnp.mean(scaled_rows * standardized_input, axis=1, keepdims=True)
    ) * reciprocal_deviation
    out_ref[0] = (upstream.astype(jnp.float32) + inner_gradient).astype(out_ref.dtype)

    @pl.when(u == pl.num_programs(0) - 1)
    def _():
        _flush(gd_ref, scale_ref, gd_out, direct)


def combine_kernel(order_ref, lang_ref, start_ref, back_ref, out_ref, *rest):
    acc_ref = rest[-1]
    if len(rest) == 2:
        rest[0][...] = jnp.zeros_like(rest[0])
    block = out_ref.shape[0]
    b = pl.program_id(0)
    base = b * block
    out_ref[...] = jnp.zeros_like(out_ref)
    first_at = start_ref[b]
    end_at = start_ref[b + 1]
    last_member = lang_ref.shape[0] - 1

    def add_member(i, carry):
        m = order_ref[i]
        lang = lang_ref[i]
        first = (i == first_at) | (lang_ref[jnp.maximum(i - 1, 0)] != lang)
        last = (i == end_at - 1) | (lang_ref[jnp.minimum(i + 1, last_member)] != lang)
        val = back_ref[m].astype(jnp.float32)

        @pl.when(first)
        def _():
            acc_ref[...] = val

        @pl.when(jnp.logical_not(first))
        def _():
            acc_ref[...] += val

        @pl.when(last)
        def _():
            out_ref[lang - base] = acc_ref[...].astype(out_ref.dtype)

        return carry

    lax.fori_loop(first_at, end_at, add_member, 0)


def scatter_kernel(order_ref, lang_ref, back_ref, zeros_hbm, out_hbm, acc_ref, stage_ref, sems):
    del zeros_hbm
    members = lang_ref.shape[0]
    last_member = members - 1

    def run_end(i):
        return (i == last_member) | (lang_ref[jnp.minimum(i + 1, last_member)] != lang_ref[i])

    def copy(i):
        return pltpu.make_async_copy(stage_ref.at[i], out_hbm.at[lang_ref[i]], sems.at[i])

    def add_member(i, carry):
        first = (i == 0) | (lang_ref[jnp.maximum(i - 1, 0)] != lang_ref[i])
        val = back_ref[order_ref[i]].astype(jnp.float32)

        @pl.when(first)
        def _():
            acc_ref[...] = val

        @pl.when(jnp.logical_not(first))
        def _():
            acc_ref[...] += val

        @pl.when(run_end(i))
        def _():
            stage_ref[i] = acc_ref[...].astype(stage_ref.dtype)
            copy(i).start()

        return carry

    def finish(i, carry):
        @pl.when(run_end(i))
        def _():
            copy(i).wait()

        return carry

    lax.fori_loop(0, members, add_member, 0)
    lax.fori_loop(0, members, finish, 0)


def scatter_combine(plan, back, zeros):
    _, order, sorted_langs, _ = plan
    members, row_count, bottleneck = back.shape
    lang_count = zeros.shape[0]
    grid_spec = pltpu.PrefetchScalarGridSpec(
        num_scalar_prefetch=2,
        grid=(1,),
        in_specs=[
            pl.BlockSpec((members, row_count, bottleneck), lambda i, o, l: (0, 0, 0)),
            pl.BlockSpec(memory_space=pl.ANY),
        ],
        out_specs=pl.BlockSpec(memory_space=pl.ANY),
        scratch_shapes=[
            pltpu.VMEM((row_count, bottleneck), jnp.float32),
            pltpu.VMEM((members, row_count, bottleneck), jnp.bfloat16),
            pltpu.SemaphoreType.DMA((members,)),
        ],
    )
    return pl.pallas_call(
        scatter_kernel,
        grid_spec=grid_spec,
        out_shape=jax.ShapeDtypeStruct((lang_count, row_count, bottleneck), jnp.bfloat16),
        input_output_aliases={3: 0},
        compiler_params=pltpu.CompilerParams(vmem_limit_bytes=48 * 1024 * 1024),
        cost_estimate=pl.CostEstimate(
            flops=back.size, bytes_accessed=back.size * 4, transcendentals=0
        ),
    )(order, sorted_langs, back, zeros)


def combine_plan(slot_lang, lang_count):
    block = 32 if lang_count % 32 == 0 else (8 if lang_count % 8 == 0 else 1)
    langs = slot_lang.reshape(-1)
    order = jnp.argsort(langs, stable=True).astype(jnp.int32)
    sorted_langs = langs[order].astype(jnp.int32)
    edges = jnp.arange(lang_count // block + 1, dtype=jnp.int32) * block
    starts = jnp.sum((sorted_langs[None, :] < edges[:, None]).astype(jnp.int32), axis=1)
    return block, order, sorted_langs, starts


def combine(plan, back, lang_count, with_zeros=False):
    block, order, sorted_langs, starts = plan
    members, row_count, bottleneck = back.shape
    outputs = 2 if with_zeros else 1
    out_spec = pl.BlockSpec((block, row_count, bottleneck), lambda b, o, l, st: (b, 0, 0))
    out_shape = jax.ShapeDtypeStruct((lang_count, row_count, bottleneck), jnp.bfloat16)
    grid_spec = pltpu.PrefetchScalarGridSpec(
        num_scalar_prefetch=3,
        grid=(lang_count // block,),
        in_specs=[pl.BlockSpec((members, row_count, bottleneck), lambda b, o, l, st: (0, 0, 0))],
        out_specs=[out_spec] * outputs,
        scratch_shapes=[pltpu.VMEM((row_count, bottleneck), jnp.float32)],
    )
    result = pl.pallas_call(
        combine_kernel,
        grid_spec=grid_spec,
        out_shape=[out_shape] * outputs,
        compiler_params=pltpu.CompilerParams(
            dimension_semantics=("arbitrary",), vmem_limit_bytes=48 * 1024 * 1024
        ),
        cost_estimate=pl.CostEstimate(
            flops=back.size,
            bytes_accessed=back.size * 2 + outputs * lang_count * row_count * bottleneck * 2,
            transcendentals=0,
        ),
    )(order, sorted_langs, starts, back)
    return tuple(result) if with_zeros else result[0]


def gather_kernel(lang_ref, weight_hbm, out_hbm, sems, *, slots):
    members = lang_ref.shape[0]

    def copy(m):
        return pltpu.make_async_copy(
            weight_hbm.at[lang_ref[m]], out_hbm.at[m // slots, m % slots], sems.at[m]
        )

    def start(m, carry):
        copy(m).start()
        return carry

    def finish(m, carry):
        copy(m).wait()
        return carry

    lax.fori_loop(0, members, start, 0)
    lax.fori_loop(0, members, finish, 0)


def gather_rows(slot_lang, weight):
    devices, slots = slot_lang.shape
    _, row_count, bottleneck = weight.shape
    members = devices * slots
    grid_spec = pltpu.PrefetchScalarGridSpec(
        num_scalar_prefetch=1,
        grid=(1,),
        in_specs=[pl.BlockSpec(memory_space=pl.ANY)],
        out_specs=pl.BlockSpec(memory_space=pl.ANY),
        scratch_shapes=[pltpu.SemaphoreType.DMA((members,))],
    )
    size = members * row_count * bottleneck * 2
    return pl.pallas_call(
        functools.partial(gather_kernel, slots=slots),
        grid_spec=grid_spec,
        out_shape=jax.ShapeDtypeStruct((devices, slots, row_count, bottleneck), weight.dtype),
        cost_estimate=pl.CostEstimate(flops=0, bytes_accessed=2 * size, transcendentals=0),
    )(slot_lang.reshape(-1), weight)


def _layouts(got):
    devices, slots, row_count, bottleneck = got.shape
    width = devices * row_count
    direct = row_count % 16 == 0
    if direct:
        weights = got
        w_spec = pl.BlockSpec((devices, 1, row_count, bottleneck), lambda u, sl, ln: (0, sl[u], 0, 0))
        g_shape = (devices, slots, row_count, bottleneck)
        g_spec = pl.BlockSpec(g_shape, lambda u, sl, ln: (0, 0, 0, 0))
    else:
        weights = got.transpose(1, 0, 2, 3).reshape(slots, width, bottleneck)
        w_spec = pl.BlockSpec((1, width, bottleneck), lambda u, sl, ln: (sl[u], 0, 0))
        g_shape = (slots, width, bottleneck)
        g_spec = pl.BlockSpec(g_shape, lambda u, sl, ln: (0, 0, 0))
    return direct, weights, w_spec, g_shape, g_spec


def _to_send(grads, got_shape, direct):
    if direct:
        return grads
    devices, slots, row_count, bottleneck = got_shape
    return grads.reshape(slots, devices, row_count, bottleneck).transpose(1, 0, 2, 3)


def _utt_spec(frame_count, width):
    return pl.BlockSpec((1, frame_count, width), lambda u, sl, ln: (u, 0, 0))


def forward_pass(frames, cotangent, gain, got_down, own_slot, own_lengths, own_scale):
    utts, frame_count, width = frames.shape
    slots, bottleneck = got_down.shape[1], got_down.shape[3]
    direct, w_down, w_spec, g_shape, g_spec = _layouts(got_down)
    grid_spec = pltpu.PrefetchScalarGridSpec(
        num_scalar_prefetch=2,
        grid=(utts,),
        in_specs=[
            _utt_spec(frame_count, width),
            _utt_spec(frame_count, width),
            pl.BlockSpec((1, width), lambda u, sl, ln: (0, 0)),
            w_spec,
            pl.BlockSpec((slots, 1, 1), lambda u, sl, ln: (0, 0, 0)),
        ],
        out_specs=[
            pl.BlockSpec((1, frame_count, bottleneck), lambda u, sl, ln: (u, 0, 0)),
            g_spec,
        ],
        scratch_shapes=[pltpu.VMEM((slots, width, bottleneck), jnp.float32)],
    )
    pre_act, grads = pl.pallas_call(
        functools.partial(forward_kernel, direct=direct),
        grid_spec=grid_spec,
        out_shape=[
            jax.ShapeDtypeStruct((utts, frame_count, bottleneck), jnp.float32),
            jax.ShapeDtypeStruct(g_shape, jnp.bfloat16),
        ],
        compiler_params=pltpu.CompilerParams(
            dimension_semantics=("arbitrary",), vmem_limit_bytes=60 * 1024 * 1024
        ),
        cost_estimate=pl.CostEstimate(
            flops=4 * utts * frame_count * width * bottleneck,
            bytes_accessed=2 * frames.size * 2 + utts * width * bottleneck * 2,
            transcendentals=utts * frame_count * bottleneck,
        ),
    )(own_slot, own_lengths, frames, cotangent, gain.reshape(1, width), w_down,
      own_scale.reshape(slots, 1, 1))
    return pre_act, _to_send(grads, got_down.shape, direct)


def backward_pass(frames, cotangent, gain, got_down, got_up, pre_act, own_slot, own_lengths,
                  own_scale):
    utts, frame_count, width = frames.shape
    slots, bottleneck = got_down.shape[1], got_down.shape[3]
    direct, w_down, w_spec, g_shape, g_spec = _layouts(got_down)
    _, w_up, _, _, _ = _layouts(got_up)
    grid_spec = pltpu.PrefetchScalarGridSpec(
        num_scalar_prefetch=2,
        grid=(utts,),
        in_specs=[
            _utt_spec(frame_count, width),
            _utt_spec(frame_count, width),
            pl.BlockSpec((1, width), lambda u, sl, ln: (0, 0)),
            w_spec,
            w_spec,
            pl.BlockSpec((1, frame_count, bottleneck), lambda u, sl, ln: (u, 0, 0)),
            pl.BlockSpec((slots, 1, 1), lambda u, sl, ln: (0, 0, 0)),
        ],
        out_specs=[_utt_spec(frame_count, width), g_spec],
        scratch_shapes=[pltpu.VMEM((slots, width, bottleneck), jnp.float32)],
    )
    d_frames, grads = pl.pallas_call(
        functools.partial(backward_kernel, direct=direct),
        grid_spec=grid_spec,
        out_shape=[
            jax.ShapeDtypeStruct(frames.shape, jnp.bfloat16),
            jax.ShapeDtypeStruct(g_shape, jnp.bfloat16),
        ],
        compiler_params=pltpu.CompilerParams(
            dimension_semantics=("arbitrary",), vmem_limit_bytes=60 * 1024 * 1024
        ),
        cost_estimate=pl.CostEstimate(
            flops=6 * utts * frame_count * width * bottleneck,
            bytes_accessed=3 * frames.size * 2 + 2 * utts * width * bottleneck * 2,
            transcendentals=utts * frame_count * bottleneck,
        ),
    )(own_slot, own_lengths, frames, cotangent, gain.reshape(1, width), w_down, w_up, pre_act,
      own_scale.reshape(slots, 1, 1))
    return d_frames, _to_send(grads, got_down.shape, direct)


def on_device(frames, cotangent, gain, down_weight, up_weight, slot_lang, utt_slot, lengths):
    devices = lax.axis_size("dp")
    self_index = lax.axis_index("dp")
    per_device = frames.shape[0]
    slots = slot_lang.shape[1]
    lang_count, row_count, bottleneck = down_weight.shape
    owners = jnp.arange(utt_slot.shape[0], dtype=jnp.int32) // per_device
    utt_lang = slot_lang[owners, utt_slot]
    own_lengths = lax.dynamic_slice_in_dim(lengths, self_index * per_device, per_device)
    own_slot = lax.dynamic_slice_in_dim(utt_slot, self_index * per_device, per_device)
    lang_ids = jnp.arange(lang_count, dtype=jnp.int32)
    counts = jnp.sum(jnp.where(utt_lang[None, :] == lang_ids[:, None], lengths[None, :], 0), axis=1)
    scaling = lax.rsqrt(jnp.maximum(counts, 1).astype(jnp.float32))
    member_langs = slot_lang.reshape(-1)
    own_scale = jnp.take(scaling, lax.dynamic_index_in_dim(slot_lang, self_index, 0, False))
    exchange = functools.partial(lax.all_to_all, axis_name="dp", split_axis=0, concat_axis=0, tiled=True)
    got_down = exchange(gather_rows(slot_lang, down_weight))
    got_up = exchange(gather_rows(slot_lang, up_weight))
    pre_act, send_up = forward_pass(
        frames, cotangent, gain, got_down, own_slot, own_lengths, own_scale
    )
    back_up = exchange(send_up).reshape(devices * slots, row_count, bottleneck)
    d_frames, send_down = backward_pass(
        frames, cotangent, gain, got_down, got_up, pre_act, own_slot, own_lengths, own_scale
    )
    send_down, back_up = lax.optimization_barrier((send_down, back_up))
    back_down = exchange(send_down).reshape(devices * slots, row_count, bottleneck)
    plan = combine_plan(slot_lang, lang_count)
    up_grads, zeros = combine(plan, back_up, lang_count, with_zeros=True)
    down_grads = scatter_combine(plan, back_down, zeros)
    return (d_frames, down_grads, up_grads)


def solution(mesh):
    placed = (
        P(("groups", "dp"), None, None),
        P(("groups", "dp"), None, None),
        P(),
        P("groups", "dp", None),
        P("groups", "dp", None),
        P("groups", None),
        P("groups"),
        P("groups"),
    )
    return jax.shard_map(
        on_device,
        mesh=mesh,
        in_specs=placed,
        out_specs=(
            P(("groups", "dp"), None, None),
            P("groups", "dp", None),
            P("groups", "dp", None),
        ),
        check_vma=False,
    )
```

```python
import functools

import jax
import jax.numpy as jnp
from jax import lax
from jax.experimental import pallas as pl
from jax.experimental.pallas import tpu as pltpu
from jax.sharding import PartitionSpec as P


def _weights(ref, direct):
    if direct:
        devices, _, row_count, bottleneck = ref.shape
        return ref[:, 0].reshape(devices * row_count, bottleneck)
    return ref[0]


def _flush(acc_ref, scale_ref, out_ref, direct):
    if direct:
        devices, slots, row_count, _ = out_ref.shape
        for dev in range(devices):
            rows = pl.ds(dev * row_count, row_count)
            out_ref[dev] = (acc_ref[:, rows, :] * scale_ref[...]).astype(out_ref.dtype)
    else:
        out_ref[...] = (acc_ref[...] * scale_ref[...]).astype(out_ref.dtype)


def _normalize(frames_ref, gain):
    values = frames_ref[0].astype(jnp.float32)
    centre_mean = jnp.mean(values, axis=1, keepdims=True)
    mean_removed = values - centre_mean
    variance = jnp.mean(mean_removed * mean_removed, axis=1, keepdims=True)
    reciprocal_deviation = lax.rsqrt(variance + 1e-06)
    standardized_input = mean_removed * reciprocal_deviation
    layer_normed = (standardized_input * gain).astype(jnp.bfloat16)
    return reciprocal_deviation, standardized_input, layer_normed


def _masked(cot_ref, length):
    upstream = cot_ref[0]
    live = lax.broadcasted_iota(jnp.int32, (upstream.shape[0], 1), 0) < length
    return upstream, jnp.where(live, upstream, jnp.zeros_like(upstream))


CONTRACT_ROWS = (((0,), (0,)), ((), ()))


def forward_kernel(slot_ref, len_ref, frames_ref, cot_ref, gain_ref, wd_ref, scale_ref,
                   pre_ref, gu_out, gu_ref, *, direct):
    u = pl.program_id(0)

    @pl.when(u == 0)
    def _():
        gu_ref[...] = jnp.zeros_like(gu_ref)

    slot = slot_ref[u]
    _, _, layer_normed = _normalize(frames_ref, gain_ref[...])
    pre_act = jnp.dot(layer_normed, _weights(wd_ref, direct), preferred_element_type=jnp.float32)
    pre_ref[0] = pre_act
    sigmoid_pre = 1.0 / (1.0 + jnp.exp(-pre_act))
    hidden = (pre_act * sigmoid_pre).astype(jnp.bfloat16)
    _, masked_up = _masked(cot_ref, len_ref[u])
    gu_ref[slot] += lax.dot_general(
        masked_up, hidden, CONTRACT_ROWS, preferred_element_type=jnp.float32
    )

    @pl.when(u == pl.num_programs(0) - 1)
    def _():
        _flush(gu_ref, scale_ref, gu_out, direct)


def backward_kernel(slot_ref, len_ref, frames_ref, cot_ref, gain_ref, wd_ref, wu_ref, pre_ref,
                    scale_ref, out_ref, gd_out, gd_ref, *, direct):
    u = pl.program_id(0)

    @pl.when(u == 0)
    def _():
        gd_ref[...] = jnp.zeros_like(gd_ref)

    slot = slot_ref[u]
    gain = gain_ref[...]
    reciprocal_deviation, standardized_input, layer_normed = _normalize(frames_ref, gain)
    pre_act = pre_ref[0]
    sigmoid_pre = 1.0 / (1.0 + jnp.exp(-pre_act))
    upstream, masked_up = _masked(cot_ref, len_ref[u])
    d_hidden = jnp.dot(masked_up, _weights(wu_ref, direct), preferred_element_type=jnp.float32)
    d_pre = (d_hidden * sigmoid_pre * (1.0 + pre_act * (1.0 - sigmoid_pre))).astype(jnp.bfloat16)
    gd_ref[slot] += lax.dot_general(
        layer_normed, d_pre, CONTRACT_ROWS, preferred_element_type=jnp.float32
    )
    d_normed = lax.dot_general(
        d_pre, _weights(wd_ref, direct), (((1,), (1,)), ((), ())),
        preferred_element_type=jnp.float32,
    )
    scaled_rows = d_normed * gain
    inner_gradient = (
        scaled_rows
        - jnp.mean(scaled_rows, axis=1, keepdims=True)
        - standardized_input * jnp.mean(scaled_rows * standardized_input, axis=1, keepdims=True)
    ) * reciprocal_deviation
    out_ref[0] = (upstream.astype(jnp.float32) + inner_gradient).astype(out_ref.dtype)

    @pl.when(u == pl.num_programs(0) - 1)
    def _():
        _flush(gd_ref, scale_ref, gd_out, direct)


def combine_kernel(order_ref, lang_ref, start_ref, back_ref, out_ref, *rest):
    acc_ref = rest[-1]
    if len(rest) == 2:
        rest[0][...] = jnp.zeros_like(rest[0])
    block = out_ref.shape[0]
    b = pl.program_id(0)
    base = b * block
    out_ref[...] = jnp.zeros_like(out_ref)
    first_at = start_ref[b]
    end_at = start_ref[b + 1]
    last_member = lang_ref.shape[0] - 1

    def add_member(i, carry):
        m = order_ref[i]
        lang = lang_ref[i]
        first = (i == first_at) | (lang_ref[jnp.maximum(i - 1, 0)] != lang)
        last = (i == end_at - 1) | (lang_ref[jnp.minimum(i + 1, last_member)] != lang)
        val = back_ref[m].astype(jnp.float32)

        @pl.when(first)
        def _():
            acc_ref[...] = val

        @pl.when(jnp.logical_not(first))
        def _():
            acc_ref[...] += val

        @pl.when(last)
        def _():
            out_ref[lang - base] = acc_ref[...].astype(out_ref.dtype)

        return carry

    lax.fori_loop(first_at, end_at, add_member, 0)


def scatter_kernel(order_ref, lang_ref, back_ref, zeros_hbm, out_hbm, acc_ref, stage_ref, sems):
    del zeros_hbm
    members = lang_ref.shape[0]
    last_member = members - 1

    def run_end(i):
        return (i == last_member) | (lang_ref[jnp.minimum(i + 1, last_member)] != lang_ref[i])

    def copy(i):
        return pltpu.make_async_copy(stage_ref.at[i], out_hbm.at[lang_ref[i]], sems.at[i])

    def add_member(i, carry):
        first = (i == 0) | (lang_ref[jnp.maximum(i - 1, 0)] != lang_ref[i])
        val = back_ref[order_ref[i]].astype(jnp.float32)

        @pl.when(first)
        def _():
            acc_ref[...] = val

        @pl.when(jnp.logical_not(first))
        def _():
            acc_ref[...] += val

        @pl.when(run_end(i))
        def _():
            stage_ref[i] = acc_ref[...].astype(stage_ref.dtype)
            copy(i).start()

        return carry

    def finish(i, carry):
        @pl.when(run_end(i))
        def _():
            copy(i).wait()

        return carry

    lax.fori_loop(0, members, add_member, 0)
    lax.fori_loop(0, members, finish, 0)


def scatter_combine(plan, back, zeros):
    _, order, sorted_langs, _ = plan
    members, row_count, bottleneck = back.shape
    lang_count = zeros.shape[0]
    grid_spec = pltpu.PrefetchScalarGridSpec(
        num_scalar_prefetch=2,
        grid=(1,),
        in_specs=[
            pl.BlockSpec((members, row_count, bottleneck), lambda i, o, l: (0, 0, 0)),
            pl.BlockSpec(memory_space=pl.ANY),
        ],
        out_specs=pl.BlockSpec(memory_space=pl.ANY),
        scratch_shapes=[
            pltpu.VMEM((row_count, bottleneck), jnp.float32),
            pltpu.VMEM((members, row_count, bottleneck), jnp.bfloat16),
            pltpu.SemaphoreType.DMA((members,)),
        ],
    )
    return pl.pallas_call(
        scatter_kernel,
        grid_spec=grid_spec,
        out_shape=jax.ShapeDtypeStruct((lang_count, row_count, bottleneck), jnp.bfloat16),
        input_output_aliases={3: 0},
        compiler_params=pltpu.CompilerParams(vmem_limit_bytes=48 * 1024 * 1024),
        cost_estimate=pl.CostEstimate(
            flops=back.size, bytes_accessed=back.size * 4, transcendentals=0
        ),
    )(order, sorted_langs, back, zeros)


def combine_plan(slot_lang, lang_count):
    block = 32 if lang_count % 32 == 0 else (8 if lang_count % 8 == 0 else 1)
    langs = slot_lang.reshape(-1)
    order = jnp.argsort(langs, stable=True).astype(jnp.int32)
    sorted_langs = langs[order].astype(jnp.int32)
    edges = jnp.arange(lang_count // block + 1, dtype=jnp.int32) * block
    starts = jnp.sum((sorted_langs[None, :] < edges[:, None]).astype(jnp.int32), axis=1)
    return block, order, sorted_langs, starts


def combine(plan, back, lang_count, with_zeros=False):
    block, order, sorted_langs, starts = plan
    members, row_count, bottleneck = back.shape
    outputs = 2 if with_zeros else 1
    out_spec = pl.BlockSpec((block, row_count, bottleneck), lambda b, o, l, st: (b, 0, 0))
    out_shape = jax.ShapeDtypeStruct((lang_count, row_count, bottleneck), jnp.bfloat16)
    grid_spec = pltpu.PrefetchScalarGridSpec(
        num_scalar_prefetch=3,
        grid=(lang_count // block,),
        in_specs=[pl.BlockSpec((members, row_count, bottleneck), lambda b, o, l, st: (0, 0, 0))],
        out_specs=[out_spec] * outputs,
        scratch_shapes=[pltpu.VMEM((row_count, bottleneck), jnp.float32)],
    )
    result = pl.pallas_call(
        combine_kernel,
        grid_spec=grid_spec,
        out_shape=[out_shape] * outputs,
        compiler_params=pltpu.CompilerParams(
            dimension_semantics=("arbitrary",), vmem_limit_bytes=48 * 1024 * 1024
        ),
        cost_estimate=pl.CostEstimate(
            flops=back.size,
            bytes_accessed=back.size * 2 + outputs * lang_count * row_count * bottleneck * 2,
            transcendentals=0,
        ),
    )(order, sorted_langs, starts, back)
    return tuple(result) if with_zeros else result[0]


def gather_kernel(lang_ref, weight_hbm, out_ref, sems, *, slots):
    per_part = out_ref.shape[0] * slots
    base = pl.program_id(0) * per_part

    def copy(k):
        return pltpu.make_async_copy(
            weight_hbm.at[lang_ref[base + k]], out_ref.at[k // slots, k % slots], sems.at[k]
        )

    def start(k, carry):
        copy(k).start()
        return carry

    def finish(k, carry):
        copy(k).wait()
        return carry

    lax.fori_loop(0, per_part, start, 0)
    lax.fori_loop(0, per_part, finish, 0)


def gather_rows(slot_lang, weight):
    devices, slots = slot_lang.shape
    _, row_count, bottleneck = weight.shape
    parts = 4 if devices % 4 == 0 else 1
    grid_spec = pltpu.PrefetchScalarGridSpec(
        num_scalar_prefetch=1,
        grid=(parts,),
        in_specs=[pl.BlockSpec(memory_space=pl.ANY)],
        out_specs=pl.BlockSpec(
            (devices // parts, slots, row_count, bottleneck), lambda p, ml: (p, 0, 0, 0)
        ),
        scratch_shapes=[pltpu.SemaphoreType.DMA((devices // parts * slots,))],
    )
    size = devices * slots * row_count * bottleneck * 2
    return pl.pallas_call(
        functools.partial(gather_kernel, slots=slots),
        grid_spec=grid_spec,
        out_shape=jax.ShapeDtypeStruct((devices, slots, row_count, bottleneck), weight.dtype),
        compiler_params=pltpu.CompilerParams(
            dimension_semantics=("arbitrary",), vmem_limit_bytes=48 * 1024 * 1024
        ),
        cost_estimate=pl.CostEstimate(flops=0, bytes_accessed=2 * size, transcendentals=0),
    )(slot_lang.reshape(-1), weight)


def _layouts(got):
    devices, slots, row_count, bottleneck = got.shape
    width = devices * row_count
    direct = row_count % 16 == 0
    if direct:
        weights = got
        w_spec = pl.BlockSpec((devices, 1, row_count, bottleneck), lambda u, sl, ln: (0, sl[u], 0, 0))
        g_shape = (devices, slots, row_count, bottleneck)
        g_spec = pl.BlockSpec(g_shape, lambda u, sl, ln: (0, 0, 0, 0))
    else:
        weights = got.transpose(1, 0, 2, 3).reshape(slots, width, bottleneck)
        w_spec = pl.BlockSpec((1, width, bottleneck), lambda u, sl, ln: (sl[u], 0, 0))
        g_shape = (slots, width, bottleneck)
        g_spec = pl.BlockSpec(g_shape, lambda u, sl, ln: (0, 0, 0))
    return direct, weights, w_spec, g_shape, g_spec


def _to_send(grads, got_shape, direct):
    if direct:
        return grads
    devices, slots, row_count, bottleneck = got_shape
    return grads.reshape(slots, devices, row_count, bottleneck).transpose(1, 0, 2, 3)


def _utt_spec(frame_count, width):
    return pl.BlockSpec((1, frame_count, width), lambda u, sl, ln: (u, 0, 0))


def forward_pass(frames, cotangent, gain, got_down, own_slot, own_lengths, own_scale):
    utts, frame_count, width = frames.shape
    slots, bottleneck = got_down.shape[1], got_down.shape[3]
    direct, w_down, w_spec, g_shape, g_spec = _layouts(got_down)
    grid_spec = pltpu.PrefetchScalarGridSpec(
        num_scalar_prefetch=2,
        grid=(utts,),
        in_specs=[
            _utt_spec(frame_count, width),
            _utt_spec(frame_count, width),
            pl.BlockSpec((1, width), lambda u, sl, ln: (0, 0)),
            w_spec,
            pl.BlockSpec((slots, 1, 1), lambda u, sl, ln: (0, 0, 0)),
        ],
        out_specs=[
            pl.BlockSpec((1, frame_count, bottleneck), lambda u, sl, ln: (u, 0, 0)),
            g_spec,
        ],
        scratch_shapes=[pltpu.VMEM((slots, width, bottleneck), jnp.float32)],
    )
    pre_act, grads = pl.pallas_call(
        functools.partial(forward_kernel, direct=direct),
        grid_spec=grid_spec,
        out_shape=[
            jax.ShapeDtypeStruct((utts, frame_count, bottleneck), jnp.float32),
            jax.ShapeDtypeStruct(g_shape, jnp.bfloat16),
        ],
        compiler_params=pltpu.CompilerParams(
            dimension_semantics=("arbitrary",), vmem_limit_bytes=60 * 1024 * 1024
        ),
        cost_estimate=pl.CostEstimate(
            flops=4 * utts * frame_count * width * bottleneck,
            bytes_accessed=2 * frames.size * 2 + utts * width * bottleneck * 2,
            transcendentals=utts * frame_count * bottleneck,
        ),
    )(own_slot, own_lengths, frames, cotangent, gain.reshape(1, width), w_down,
      own_scale.reshape(slots, 1, 1))
    return pre_act, _to_send(grads, got_down.shape, direct)


def backward_pass(frames, cotangent, gain, got_down, got_up, pre_act, own_slot, own_lengths,
                  own_scale):
    utts, frame_count, width = frames.shape
    slots, bottleneck = got_down.shape[1], got_down.shape[3]
    direct, w_down, w_spec, g_shape, g_spec = _layouts(got_down)
    _, w_up, _, _, _ = _layouts(got_up)
    grid_spec = pltpu.PrefetchScalarGridSpec(
        num_scalar_prefetch=2,
        grid=(utts,),
        in_specs=[
            _utt_spec(frame_count, width),
            _utt_spec(frame_count, width),
            pl.BlockSpec((1, width), lambda u, sl, ln: (0, 0)),
            w_spec,
            w_spec,
            pl.BlockSpec((1, frame_count, bottleneck), lambda u, sl, ln: (u, 0, 0)),
            pl.BlockSpec((slots, 1, 1), lambda u, sl, ln: (0, 0, 0)),
        ],
        out_specs=[_utt_spec(frame_count, width), g_spec],
        scratch_shapes=[pltpu.VMEM((slots, width, bottleneck), jnp.float32)],
    )
    d_frames, grads = pl.pallas_call(
        functools.partial(backward_kernel, direct=direct),
        grid_spec=grid_spec,
        out_shape=[
            jax.ShapeDtypeStruct(frames.shape, jnp.bfloat16),
            jax.ShapeDtypeStruct(g_shape, jnp.bfloat16),
        ],
        compiler_params=pltpu.CompilerParams(
            dimension_semantics=("arbitrary",), vmem_limit_bytes=60 * 1024 * 1024
        ),
        cost_estimate=pl.CostEstimate(
            flops=6 * utts * frame_count * width * bottleneck,
            bytes_accessed=3 * frames.size * 2 + 2 * utts * width * bottleneck * 2,
            transcendentals=utts * frame_count * bottleneck,
        ),
    )(own_slot, own_lengths, frames, cotangent, gain.reshape(1, width), w_down, w_up, pre_act,
      own_scale.reshape(slots, 1, 1))
    return d_frames, _to_send(grads, got_down.shape, direct)


def on_device(frames, cotangent, gain, down_weight, up_weight, slot_lang, utt_slot, lengths):
    devices = lax.axis_size("dp")
    self_index = lax.axis_index("dp")
    per_device = frames.shape[0]
    slots = slot_lang.shape[1]
    lang_count, row_count, bottleneck = down_weight.shape
    owners = jnp.arange(utt_slot.shape[0], dtype=jnp.int32) // per_device
    utt_lang = slot_lang[owners, utt_slot]
    own_lengths = lax.dynamic_slice_in_dim(lengths, self_index * per_device, per_device)
    own_slot = lax.dynamic_slice_in_dim(utt_slot, self_index * per_device, per_device)
    lang_ids = jnp.arange(lang_count, dtype=jnp.int32)
    counts = jnp.sum(jnp.where(utt_lang[None, :] == lang_ids[:, None], lengths[None, :], 0), axis=1)
    scaling = lax.rsqrt(jnp.maximum(counts, 1).astype(jnp.float32))
    member_langs = slot_lang.reshape(-1)
    own_scale = jnp.take(scaling, lax.dynamic_index_in_dim(slot_lang, self_index, 0, False))
    exchange = functools.partial(lax.all_to_all, axis_name="dp", split_axis=0, concat_axis=0, tiled=True)
    got_down = exchange(gather_rows(slot_lang, down_weight))
    got_up = exchange(gather_rows(slot_lang, up_weight))
    pre_act, send_up = forward_pass(
        frames, cotangent, gain, got_down, own_slot, own_lengths, own_scale
    )
    back_up = exchange(send_up).reshape(devices * slots, row_count, bottleneck)
    d_frames, send_down = backward_pass(
        frames, cotangent, gain, got_down, got_up, pre_act, own_slot, own_lengths, own_scale
    )
    send_down, back_up = lax.optimization_barrier((send_down, back_up))
    back_down = exchange(send_down).reshape(devices * slots, row_count, bottleneck)
    plan = combine_plan(slot_lang, lang_count)
    up_grads, zeros = combine(plan, back_up, lang_count, with_zeros=True)
    down_grads = scatter_combine(plan, back_down, zeros)
    return (d_frames, down_grads, up_grads)


def solution(mesh):
    placed = (
        P(("groups", "dp"), None, None),
        P(("groups", "dp"), None, None),
        P(),
        P("groups", "dp", None),
        P("groups", "dp", None),
        P("groups", None),
        P("groups"),
        P("groups"),
    )
    return jax.shard_map(
        on_device,
        mesh=mesh,
        in_specs=placed,
        out_specs=(
            P(("groups", "dp"), None, None),
            P("groups", "dp", None),
            P("groups", "dp", None),
        ),
        check_vma=False,
    )
```

```python
import functools

import jax
import jax.numpy as jnp
from jax import lax
from jax.experimental import pallas as pl
from jax.experimental.pallas import tpu as pltpu
from jax.sharding import PartitionSpec as P


def _weights(ref, direct):
    if direct:
        devices, _, row_count, bottleneck = ref.shape
        return ref[:, 0].reshape(devices * row_count, bottleneck)
    return ref[0]


def _flush(acc_ref, scale_ref, out_ref, direct):
    if direct:
        devices, slots, row_count, _ = out_ref.shape
        for dev in range(devices):
            rows = pl.ds(dev * row_count, row_count)
            out_ref[dev] = (acc_ref[:, rows, :] * scale_ref[...]).astype(out_ref.dtype)
    else:
        out_ref[...] = (acc_ref[...] * scale_ref[...]).astype(out_ref.dtype)


def _normalize(frames_ref, gain):
    values = frames_ref[0].astype(jnp.float32)
    centre_mean = jnp.mean(values, axis=1, keepdims=True)
    mean_removed = values - centre_mean
    variance = jnp.mean(mean_removed * mean_removed, axis=1, keepdims=True)
    reciprocal_deviation = lax.rsqrt(variance + 1e-06)
    standardized_input = mean_removed * reciprocal_deviation
    layer_normed = (standardized_input * gain).astype(jnp.bfloat16)
    return reciprocal_deviation, standardized_input, layer_normed


def _masked(cot_ref, length):
    upstream = cot_ref[0]
    live = lax.broadcasted_iota(jnp.int32, (upstream.shape[0], 1), 0) < length
    return upstream, jnp.where(live, upstream, jnp.zeros_like(upstream))


CONTRACT_ROWS = (((0,), (0,)), ((), ()))


def forward_kernel(slot_ref, len_ref, frames_ref, cot_ref, gain_ref, wd_ref, scale_ref,
                   pre_ref, gu_out, gu_ref, *, direct):
    u = pl.program_id(0)

    @pl.when(u == 0)
    def _():
        gu_ref[...] = jnp.zeros_like(gu_ref)

    slot = slot_ref[u]
    _, _, layer_normed = _normalize(frames_ref, gain_ref[...])
    pre_act = jnp.dot(layer_normed, _weights(wd_ref, direct), preferred_element_type=jnp.float32)
    pre_ref[0] = pre_act
    sigmoid_pre = 1.0 / (1.0 + jnp.exp(-pre_act))
    hidden = (pre_act * sigmoid_pre).astype(jnp.bfloat16)
    _, masked_up = _masked(cot_ref, len_ref[u])
    gu_ref[slot] += lax.dot_general(
        masked_up, hidden, CONTRACT_ROWS, preferred_element_type=jnp.float32
    )

    @pl.when(u == pl.num_programs(0) - 1)
    def _():
        _flush(gu_ref, scale_ref, gu_out, direct)


def backward_kernel(slot_ref, len_ref, frames_ref, cot_ref, gain_ref, wd_ref, wu_ref, pre_ref,
                    scale_ref, out_ref, gd_out, gd_ref, *, direct):
    u = pl.program_id(0)

    @pl.when(u == 0)
    def _():
        gd_ref[...] = jnp.zeros_like(gd_ref)

    slot = slot_ref[u]
    gain = gain_ref[...]
    reciprocal_deviation, standardized_input, layer_normed = _normalize(frames_ref, gain)
    pre_act = pre_ref[0]
    sigmoid_pre = 1.0 / (1.0 + jnp.exp(-pre_act))
    upstream, masked_up = _masked(cot_ref, len_ref[u])
    d_hidden = jnp.dot(masked_up, _weights(wu_ref, direct), preferred_element_type=jnp.float32)
    d_pre = (d_hidden * sigmoid_pre * (1.0 + pre_act * (1.0 - sigmoid_pre))).astype(jnp.bfloat16)
    gd_ref[slot] += lax.dot_general(
        layer_normed, d_pre, CONTRACT_ROWS, preferred_element_type=jnp.float32
    )
    d_normed = lax.dot_general(
        d_pre, _weights(wd_ref, direct), (((1,), (1,)), ((), ())),
        preferred_element_type=jnp.float32,
    )
    scaled_rows = d_normed * gain
    inner_gradient = (
        scaled_rows
        - jnp.mean(scaled_rows, axis=1, keepdims=True)
        - standardized_input * jnp.mean(scaled_rows * standardized_input, axis=1, keepdims=True)
    ) * reciprocal_deviation
    out_ref[0] = (upstream.astype(jnp.float32) + inner_gradient).astype(out_ref.dtype)

    @pl.when(u == pl.num_programs(0) - 1)
    def _():
        _flush(gd_ref, scale_ref, gd_out, direct)


def combine_kernel(order_ref, lang_ref, start_ref, back_ref, out_ref, *rest):
    acc_ref = rest[-1]
    if len(rest) == 2:
        rest[0][...] = jnp.zeros_like(rest[0])
    block = out_ref.shape[0]
    b = pl.program_id(0)
    base = b * block
    out_ref[...] = jnp.zeros_like(out_ref)
    first_at = start_ref[b]
    end_at = start_ref[b + 1]
    last_member = lang_ref.shape[0] - 1

    def add_member(i, carry):
        m = order_ref[i]
        lang = lang_ref[i]
        first = (i == first_at) | (lang_ref[jnp.maximum(i - 1, 0)] != lang)
        last = (i == end_at - 1) | (lang_ref[jnp.minimum(i + 1, last_member)] != lang)
        val = back_ref[m].astype(jnp.float32)

        @pl.when(first)
        def _():
            acc_ref[...] = val

        @pl.when(jnp.logical_not(first))
        def _():
            acc_ref[...] += val

        @pl.when(last)
        def _():
            out_ref[lang - base] = acc_ref[...].astype(out_ref.dtype)

        return carry

    lax.fori_loop(first_at, end_at, add_member, 0)


def scatter_kernel(order_ref, lang_ref, back_hbm, zeros_hbm, out_hbm, acc_ref, in_ref, stage_ref,
                   sems_in, sems_out):
    del zeros_hbm
    members = lang_ref.shape[0]
    last_member = members - 1

    def run_end(i):
        return (i == last_member) | (lang_ref[jnp.minimum(i + 1, last_member)] != lang_ref[i])

    def copy_in(i):
        return pltpu.make_async_copy(back_hbm.at[order_ref[i]], in_ref.at[i], sems_in.at[i])

    def copy_out(i):
        return pltpu.make_async_copy(stage_ref.at[i], out_hbm.at[lang_ref[i]], sems_out.at[i])

    def fetch(i, carry):
        copy_in(i).start()
        return carry

    def add_member(i, carry):
        copy_in(i).wait()
        first = (i == 0) | (lang_ref[jnp.maximum(i - 1, 0)] != lang_ref[i])
        val = in_ref[i].astype(jnp.float32)

        @pl.when(first)
        def _():
            acc_ref[...] = val

        @pl.when(jnp.logical_not(first))
        def _():
            acc_ref[...] += val

        @pl.when(run_end(i))
        def _():
            stage_ref[i] = acc_ref[...].astype(stage_ref.dtype)
            copy_out(i).start()

        return carry

    def finish(i, carry):
        @pl.when(run_end(i))
        def _():
            copy_out(i).wait()

        return carry

    lax.fori_loop(0, members, fetch, 0)
    lax.fori_loop(0, members, add_member, 0)
    lax.fori_loop(0, members, finish, 0)


def scatter_combine(plan, back, zeros):
    _, order, sorted_langs, _ = plan
    members, row_count, bottleneck = back.shape
    lang_count = zeros.shape[0]
    grid_spec = pltpu.PrefetchScalarGridSpec(
        num_scalar_prefetch=2,
        grid=(1,),
        in_specs=[pl.BlockSpec(memory_space=pl.ANY), pl.BlockSpec(memory_space=pl.ANY)],
        out_specs=pl.BlockSpec(memory_space=pl.ANY),
        scratch_shapes=[
            pltpu.VMEM((row_count, bottleneck), jnp.float32),
            pltpu.VMEM((members, row_count, bottleneck), jnp.bfloat16),
            pltpu.VMEM((members, row_count, bottleneck), jnp.bfloat16),
            pltpu.SemaphoreType.DMA((members,)),
            pltpu.SemaphoreType.DMA((members,)),
        ],
    )
    return pl.pallas_call(
        scatter_kernel,
        grid_spec=grid_spec,
        out_shape=jax.ShapeDtypeStruct((lang_count, row_count, bottleneck), jnp.bfloat16),
        input_output_aliases={3: 0},
        compiler_params=pltpu.CompilerParams(vmem_limit_bytes=48 * 1024 * 1024),
        cost_estimate=pl.CostEstimate(
            flops=back.size, bytes_accessed=back.size * 4, transcendentals=0
        ),
    )(order, sorted_langs, back, zeros)


def combine_plan(slot_lang, lang_count):
    block = 32 if lang_count % 32 == 0 else (8 if lang_count % 8 == 0 else 1)
    langs = slot_lang.reshape(-1)
    order = jnp.argsort(langs, stable=True).astype(jnp.int32)
    sorted_langs = langs[order].astype(jnp.int32)
    edges = jnp.arange(lang_count // block + 1, dtype=jnp.int32) * block
    starts = jnp.sum((sorted_langs[None, :] < edges[:, None]).astype(jnp.int32), axis=1)
    return block, order, sorted_langs, starts


def combine(plan, back, lang_count, with_zeros=False):
    block, order, sorted_langs, starts = plan
    members, row_count, bottleneck = back.shape
    outputs = 2 if with_zeros else 1
    out_spec = pl.BlockSpec((block, row_count, bottleneck), lambda b, o, l, st: (b, 0, 0))
    out_shape = jax.ShapeDtypeStruct((lang_count, row_count, bottleneck), jnp.bfloat16)
    grid_spec = pltpu.PrefetchScalarGridSpec(
        num_scalar_prefetch=3,
        grid=(lang_count // block,),
        in_specs=[pl.BlockSpec((members, row_count, bottleneck), lambda b, o, l, st: (0, 0, 0))],
        out_specs=[out_spec] * outputs,
        scratch_shapes=[pltpu.VMEM((row_count, bottleneck), jnp.float32)],
    )
    result = pl.pallas_call(
        combine_kernel,
        grid_spec=grid_spec,
        out_shape=[out_shape] * outputs,
        compiler_params=pltpu.CompilerParams(
            dimension_semantics=("arbitrary",), vmem_limit_bytes=48 * 1024 * 1024
        ),
        cost_estimate=pl.CostEstimate(
            flops=back.size,
            bytes_accessed=back.size * 2 + outputs * lang_count * row_count * bottleneck * 2,
            transcendentals=0,
        ),
    )(order, sorted_langs, starts, back)
    return tuple(result) if with_zeros else result[0]


def gather_kernel(lang_ref, weight_hbm, out_ref, sems, *, slots):
    members = lang_ref.shape[0]

    def copy(m):
        return pltpu.make_async_copy(
            weight_hbm.at[lang_ref[m]], out_ref.at[m // slots, m % slots], sems.at[m]
        )

    def start(m, carry):
        copy(m).start()
        return carry

    def finish(m, carry):
        copy(m).wait()
        return carry

    lax.fori_loop(0, members, start, 0)
    lax.fori_loop(0, members, finish, 0)


def gather_rows(slot_lang, weight):
    devices, slots = slot_lang.shape
    _, row_count, bottleneck = weight.shape
    members = devices * slots
    grid_spec = pltpu.PrefetchScalarGridSpec(
        num_scalar_prefetch=1,
        grid=(1,),
        in_specs=[pl.BlockSpec(memory_space=pl.ANY)],
        out_specs=pl.BlockSpec((devices, slots, row_count, bottleneck), lambda i, ml: (0, 0, 0, 0)),
        scratch_shapes=[pltpu.SemaphoreType.DMA((members,))],
    )
    size = members * row_count * bottleneck * 2
    return pl.pallas_call(
        functools.partial(gather_kernel, slots=slots),
        grid_spec=grid_spec,
        out_shape=jax.ShapeDtypeStruct((devices, slots, row_count, bottleneck), jnp.bfloat16),
        compiler_params=pltpu.CompilerParams(vmem_limit_bytes=48 * 1024 * 1024),
        cost_estimate=pl.CostEstimate(flops=0, bytes_accessed=2 * size, transcendentals=0),
    )(slot_lang.reshape(-1), weight)


def _layouts(got):
    devices, slots, row_count, bottleneck = got.shape
    width = devices * row_count
    direct = row_count % 16 == 0
    if direct:
        weights = got
        w_spec = pl.BlockSpec((devices, 1, row_count, bottleneck), lambda u, sl, ln: (0, sl[u], 0, 0))
        g_shape = (devices, slots, row_count, bottleneck)
        g_spec = pl.BlockSpec(g_shape, lambda u, sl, ln: (0, 0, 0, 0))
    else:
        weights = got.transpose(1, 0, 2, 3).reshape(slots, width, bottleneck)
        w_spec = pl.BlockSpec((1, width, bottleneck), lambda u, sl, ln: (sl[u], 0, 0))
        g_shape = (slots, width, bottleneck)
        g_spec = pl.BlockSpec(g_shape, lambda u, sl, ln: (0, 0, 0))
    return direct, weights, w_spec, g_shape, g_spec


def _to_send(grads, got_shape, direct):
    if direct:
        return grads
    devices, slots, row_count, bottleneck = got_shape
    return grads.reshape(slots, devices, row_count, bottleneck).transpose(1, 0, 2, 3)


def _utt_spec(frame_count, width):
    return pl.BlockSpec((1, frame_count, width), lambda u, sl, ln: (u, 0, 0))


def forward_pass(frames, cotangent, gain, got_down, own_slot, own_lengths, own_scale):
    utts, frame_count, width = frames.shape
    slots, bottleneck = got_down.shape[1], got_down.shape[3]
    direct, w_down, w_spec, g_shape, g_spec = _layouts(got_down)
    grid_spec = pltpu.PrefetchScalarGridSpec(
        num_scalar_prefetch=2,
        grid=(utts,),
        in_specs=[
            _utt_spec(frame_count, width),
            _utt_spec(frame_count, width),
            pl.BlockSpec((1, width), lambda u, sl, ln: (0, 0)),
            w_spec,
            pl.BlockSpec((slots, 1, 1), lambda u, sl, ln: (0, 0, 0)),
        ],
        out_specs=[
            pl.BlockSpec((1, frame_count, bottleneck), lambda u, sl, ln: (u, 0, 0)),
            g_spec,
        ],
        scratch_shapes=[pltpu.VMEM((slots, width, bottleneck), jnp.float32)],
    )
    pre_act, grads = pl.pallas_call(
        functools.partial(forward_kernel, direct=direct),
        grid_spec=grid_spec,
        out_shape=[
            jax.ShapeDtypeStruct((utts, frame_count, bottleneck), jnp.float32),
            jax.ShapeDtypeStruct(g_shape, jnp.bfloat16),
        ],
        compiler_params=pltpu.CompilerParams(
            dimension_semantics=("arbitrary",), vmem_limit_bytes=60 * 1024 * 1024
        ),
        cost_estimate=pl.CostEstimate(
            flops=4 * utts * frame_count * width * bottleneck,
            bytes_accessed=2 * frames.size * 2 + utts * width * bottleneck * 2,
            transcendentals=utts * frame_count * bottleneck,
        ),
    )(own_slot, own_lengths, frames, cotangent, gain.reshape(1, width), w_down,
      own_scale.reshape(slots, 1, 1))
    return pre_act, _to_send(grads, got_down.shape, direct)


def backward_pass(frames, cotangent, gain, got_down, got_up, pre_act, own_slot, own_lengths,
                  own_scale):
    utts, frame_count, width = frames.shape
    slots, bottleneck = got_down.shape[1], got_down.shape[3]
    direct, w_down, w_spec, g_shape, g_spec = _layouts(got_down)
    _, w_up, _, _, _ = _layouts(got_up)
    grid_spec = pltpu.PrefetchScalarGridSpec(
        num_scalar_prefetch=2,
        grid=(utts,),
        in_specs=[
            _utt_spec(frame_count, width),
            _utt_spec(frame_count, width),
            pl.BlockSpec((1, width), lambda u, sl, ln: (0, 0)),
            w_spec,
            w_spec,
            pl.BlockSpec((1, frame_count, bottleneck), lambda u, sl, ln: (u, 0, 0)),
            pl.BlockSpec((slots, 1, 1), lambda u, sl, ln: (0, 0, 0)),
        ],
        out_specs=[_utt_spec(frame_count, width), g_spec],
        scratch_shapes=[pltpu.VMEM((slots, width, bottleneck), jnp.float32)],
    )
    d_frames, grads = pl.pallas_call(
        functools.partial(backward_kernel, direct=direct),
        grid_spec=grid_spec,
        out_shape=[
            jax.ShapeDtypeStruct(frames.shape, jnp.bfloat16),
            jax.ShapeDtypeStruct(g_shape, jnp.bfloat16),
        ],
        compiler_params=pltpu.CompilerParams(
            dimension_semantics=("arbitrary",), vmem_limit_bytes=60 * 1024 * 1024
        ),
        cost_estimate=pl.CostEstimate(
            flops=6 * utts * frame_count * width * bottleneck,
            bytes_accessed=3 * frames.size * 2 + 2 * utts * width * bottleneck * 2,
            transcendentals=utts * frame_count * bottleneck,
        ),
    )(own_slot, own_lengths, frames, cotangent, gain.reshape(1, width), w_down, w_up, pre_act,
      own_scale.reshape(slots, 1, 1))
    return d_frames, _to_send(grads, got_down.shape, direct)


def on_device(frames, cotangent, gain, down_weight, up_weight, slot_lang, utt_slot, lengths):
    devices = lax.axis_size("dp")
    self_index = lax.axis_index("dp")
    per_device = frames.shape[0]
    slots = slot_lang.shape[1]
    lang_count, row_count, bottleneck = down_weight.shape
    owners = jnp.arange(utt_slot.shape[0], dtype=jnp.int32) // per_device
    utt_lang = slot_lang[owners, utt_slot]
    own_lengths = lax.dynamic_slice_in_dim(lengths, self_index * per_device, per_device)
    own_slot = lax.dynamic_slice_in_dim(utt_slot, self_index * per_device, per_device)
    lang_ids = jnp.arange(lang_count, dtype=jnp.int32)
    counts = jnp.sum(jnp.where(utt_lang[None, :] == lang_ids[:, None], lengths[None, :], 0), axis=1)
    scaling = lax.rsqrt(jnp.maximum(counts, 1).astype(jnp.float32))
    member_langs = slot_lang.reshape(-1)
    own_scale = jnp.take(scaling, lax.dynamic_index_in_dim(slot_lang, self_index, 0, False))
    exchange = functools.partial(lax.all_to_all, axis_name="dp", split_axis=0, concat_axis=0, tiled=True)
    got_down = exchange(gather_rows(slot_lang, down_weight))
    got_up = exchange(gather_rows(slot_lang, up_weight))
    pre_act, send_up = forward_pass(
        frames, cotangent, gain, got_down, own_slot, own_lengths, own_scale
    )
    back_up = exchange(send_up).reshape(devices * slots, row_count, bottleneck)
    d_frames, send_down = backward_pass(
        frames, cotangent, gain, got_down, got_up, pre_act, own_slot, own_lengths, own_scale
    )
    send_down, back_up = lax.optimization_barrier((send_down, back_up))
    back_down = exchange(send_down).reshape(devices * slots, row_count, bottleneck)
    plan = combine_plan(slot_lang, lang_count)
    up_grads, zeros = combine(plan, back_up, lang_count, with_zeros=True)
    down_grads = scatter_combine(plan, back_down, zeros)
    return (d_frames, down_grads, up_grads)


def solution(mesh):
    placed = (
        P(("groups", "dp"), None, None),
        P(("groups", "dp"), None, None),
        P(),
        P("groups", "dp", None),
        P("groups", "dp", None),
        P("groups", None),
        P("groups"),
        P("groups"),
    )
    return jax.shard_map(
        on_device,
        mesh=mesh,
        in_specs=placed,
        out_specs=(
            P(("groups", "dp"), None, None),
            P("groups", "dp", None),
            P("groups", "dp", None),
        ),
        check_vma=False,
    )
```

```python
import functools

import jax
import jax.numpy as jnp
from jax import lax
from jax.experimental import pallas as pl
from jax.experimental.pallas import tpu as pltpu
from jax.sharding import PartitionSpec as P


def _weights(ref, direct):
    if direct:
        devices, _, row_count, bottleneck = ref.shape
        return ref[:, 0].reshape(devices * row_count, bottleneck)
    return ref[0]


def _flush(acc_ref, scale_ref, out_ref, direct):
    if direct:
        devices, slots, row_count, _ = out_ref.shape
        for dev in range(devices):
            rows = pl.ds(dev * row_count, row_count)
            out_ref[dev] = (acc_ref[:, rows, :] * scale_ref[...]).astype(out_ref.dtype)
    else:
        out_ref[...] = (acc_ref[...] * scale_ref[...]).astype(out_ref.dtype)


def _normalize(frames_ref, gain):
    values = frames_ref[0].astype(jnp.float32)
    centre_mean = jnp.mean(values, axis=1, keepdims=True)
    mean_removed = values - centre_mean
    variance = jnp.mean(mean_removed * mean_removed, axis=1, keepdims=True)
    reciprocal_deviation = lax.rsqrt(variance + 1e-06)
    standardized_input = mean_removed * reciprocal_deviation
    layer_normed = (standardized_input * gain).astype(jnp.bfloat16)
    return reciprocal_deviation, standardized_input, layer_normed


def _masked(cot_ref, length):
    upstream = cot_ref[0]
    live = lax.broadcasted_iota(jnp.int32, (upstream.shape[0], 1), 0) < length
    return upstream, jnp.where(live, upstream, jnp.zeros_like(upstream))


CONTRACT_ROWS = (((0,), (0,)), ((), ()))


def forward_kernel(slot_ref, len_ref, frames_ref, cot_ref, gain_ref, wd_ref, scale_ref,
                   pre_ref, gu_out, gu_ref, *, direct):
    u = pl.program_id(0)

    @pl.when(u == 0)
    def _():
        gu_ref[...] = jnp.zeros_like(gu_ref)

    slot = slot_ref[u]
    _, _, layer_normed = _normalize(frames_ref, gain_ref[...])
    pre_act = jnp.dot(layer_normed, _weights(wd_ref, direct), preferred_element_type=jnp.float32)
    pre_ref[0] = pre_act
    sigmoid_pre = 1.0 / (1.0 + jnp.exp(-pre_act))
    hidden = (pre_act * sigmoid_pre).astype(jnp.bfloat16)
    _, masked_up = _masked(cot_ref, len_ref[u])
    gu_ref[slot] += lax.dot_general(
        masked_up, hidden, CONTRACT_ROWS, preferred_element_type=jnp.float32
    )

    @pl.when(u == pl.num_programs(0) - 1)
    def _():
        _flush(gu_ref, scale_ref, gu_out, direct)


def backward_kernel(slot_ref, len_ref, frames_ref, cot_ref, gain_ref, wd_ref, wu_ref, pre_ref,
                    scale_ref, out_ref, gd_out, gd_ref, *, direct):
    u = pl.program_id(0)

    @pl.when(u == 0)
    def _():
        gd_ref[...] = jnp.zeros_like(gd_ref)

    slot = slot_ref[u]
    gain = gain_ref[...]
    reciprocal_deviation, standardized_input, layer_normed = _normalize(frames_ref, gain)
    pre_act = pre_ref[0]
    sigmoid_pre = 1.0 / (1.0 + jnp.exp(-pre_act))
    upstream, masked_up = _masked(cot_ref, len_ref[u])
    d_hidden = jnp.dot(masked_up, _weights(wu_ref, direct), preferred_element_type=jnp.float32)
    d_pre = (d_hidden * sigmoid_pre * (1.0 + pre_act * (1.0 - sigmoid_pre))).astype(jnp.bfloat16)
    gd_ref[slot] += lax.dot_general(
        layer_normed, d_pre, CONTRACT_ROWS, preferred_element_type=jnp.float32
    )
    d_normed = lax.dot_general(
        d_pre, _weights(wd_ref, direct), (((1,), (1,)), ((), ())),
        preferred_element_type=jnp.float32,
    )
    scaled_rows = d_normed * gain
    inner_gradient = (
        scaled_rows
        - jnp.mean(scaled_rows, axis=1, keepdims=True)
        - standardized_input * jnp.mean(scaled_rows * standardized_input, axis=1, keepdims=True)
    ) * reciprocal_deviation
    out_ref[0] = (upstream.astype(jnp.float32) + inner_gradient).astype(out_ref.dtype)

    @pl.when(u == pl.num_programs(0) - 1)
    def _():
        _flush(gd_ref, scale_ref, gd_out, direct)


def combine_kernel(order_ref, lang_ref, start_ref, back_ref, out_ref, *rest):
    acc_ref = rest[-1]
    if len(rest) == 2:
        rest[0][...] = jnp.zeros_like(rest[0])
    block = out_ref.shape[0]
    b = pl.program_id(0)
    base = b * block
    out_ref[...] = jnp.zeros_like(out_ref)
    first_at = start_ref[b]
    end_at = start_ref[b + 1]
    last_member = lang_ref.shape[0] - 1

    def add_member(i, carry):
        m = order_ref[i]
        lang = lang_ref[i]
        first = (i == first_at) | (lang_ref[jnp.maximum(i - 1, 0)] != lang)
        last = (i == end_at - 1) | (lang_ref[jnp.minimum(i + 1, last_member)] != lang)
        val = back_ref[m].astype(jnp.float32)

        @pl.when(first)
        def _():
            acc_ref[...] = val

        @pl.when(jnp.logical_not(first))
        def _():
            acc_ref[...] += val

        @pl.when(last)
        def _():
            out_ref[lang - base] = acc_ref[...].astype(out_ref.dtype)

        return carry

    lax.fori_loop(first_at, end_at, add_member, 0)


def scatter_kernel(order_ref, lang_ref, back_ref, zeros_hbm, out_hbm, acc_ref, stage_ref, sems):
    del zeros_hbm
    members = lang_ref.shape[0]
    last_member = members - 1

    def run_end(i):
        return (i == last_member) | (lang_ref[jnp.minimum(i + 1, last_member)] != lang_ref[i])

    def copy(i):
        return pltpu.make_async_copy(stage_ref.at[i], out_hbm.at[lang_ref[i]], sems.at[i])

    def add_member(i, carry):
        first = (i == 0) | (lang_ref[jnp.maximum(i - 1, 0)] != lang_ref[i])
        val = back_ref[order_ref[i]].astype(jnp.float32)

        @pl.when(first)
        def _():
            acc_ref[...] = val

        @pl.when(jnp.logical_not(first))
        def _():
            acc_ref[...] += val

        @pl.when(run_end(i))
        def _():
            stage_ref[i] = acc_ref[...].astype(stage_ref.dtype)
            copy(i).start()

        return carry

    def finish(i, carry):
        @pl.when(run_end(i))
        def _():
            copy(i).wait()

        return carry

    lax.fori_loop(0, members, add_member, 0)
    lax.fori_loop(0, members, finish, 0)


def scatter_combine(plan, back, zeros):
    _, order, sorted_langs, _ = plan
    members, row_count, bottleneck = back.shape
    lang_count = zeros.shape[0]
    grid_spec = pltpu.PrefetchScalarGridSpec(
        num_scalar_prefetch=2,
        grid=(1,),
        in_specs=[
            pl.BlockSpec((members, row_count, bottleneck), lambda i, o, l: (0, 0, 0)),
            pl.BlockSpec(memory_space=pl.ANY),
        ],
        out_specs=pl.BlockSpec(memory_space=pl.ANY),
        scratch_shapes=[
            pltpu.VMEM((row_count, bottleneck), jnp.float32),
            pltpu.VMEM((members, row_count, bottleneck), jnp.bfloat16),
            pltpu.SemaphoreType.DMA((members,)),
        ],
    )
    return pl.pallas_call(
        scatter_kernel,
        grid_spec=grid_spec,
        out_shape=jax.ShapeDtypeStruct((lang_count, row_count, bottleneck), jnp.bfloat16),
        input_output_aliases={3: 0},
        compiler_params=pltpu.CompilerParams(vmem_limit_bytes=48 * 1024 * 1024),
        cost_estimate=pl.CostEstimate(
            flops=back.size, bytes_accessed=back.size * 4, transcendentals=0
        ),
    )(order, sorted_langs, back, zeros)


def combine_plan(slot_lang, lang_count):
    block = 32 if lang_count % 32 == 0 else (8 if lang_count % 8 == 0 else 1)
    langs = slot_lang.reshape(-1)
    order = jnp.argsort(langs, stable=True).astype(jnp.int32)
    sorted_langs = langs[order].astype(jnp.int32)
    edges = jnp.arange(lang_count // block + 1, dtype=jnp.int32) * block
    starts = jnp.sum((sorted_langs[None, :] < edges[:, None]).astype(jnp.int32), axis=1)
    return block, order, sorted_langs, starts


def combine(plan, back, lang_count, with_zeros=False):
    block, order, sorted_langs, starts = plan
    members, row_count, bottleneck = back.shape
    outputs = 2 if with_zeros else 1
    out_spec = pl.BlockSpec((block, row_count, bottleneck), lambda b, o, l, st: (b, 0, 0))
    out_shape = jax.ShapeDtypeStruct((lang_count, row_count, bottleneck), jnp.bfloat16)
    grid_spec = pltpu.PrefetchScalarGridSpec(
        num_scalar_prefetch=3,
        grid=(lang_count // block,),
        in_specs=[pl.BlockSpec((members, row_count, bottleneck), lambda b, o, l, st: (0, 0, 0))],
        out_specs=[out_spec] * outputs,
        scratch_shapes=[pltpu.VMEM((row_count, bottleneck), jnp.float32)],
    )
    result = pl.pallas_call(
        combine_kernel,
        grid_spec=grid_spec,
        out_shape=[out_shape] * outputs,
        compiler_params=pltpu.CompilerParams(
            dimension_semantics=("arbitrary",), vmem_limit_bytes=48 * 1024 * 1024
        ),
        cost_estimate=pl.CostEstimate(
            flops=back.size,
            bytes_accessed=back.size * 2 + outputs * lang_count * row_count * bottleneck * 2,
            transcendentals=0,
        ),
    )(order, sorted_langs, starts, back)
    return tuple(result) if with_zeros else result[0]


def gather_kernel(lang_ref, weight_hbm, out_ref, sems, *, slots):
    members = lang_ref.shape[0]

    def copy(m):
        return pltpu.make_async_copy(
            weight_hbm.at[lang_ref[m]], out_ref.at[m // slots, m % slots], sems.at[m]
        )

    def start(m, carry):
        copy(m).start()
        return carry

    def finish(m, carry):
        copy(m).wait()
        return carry

    lax.fori_loop(0, members, start, 0)
    lax.fori_loop(0, members, finish, 0)


def gather_rows(slot_lang, weight):
    devices, slots = slot_lang.shape
    _, row_count, bottleneck = weight.shape
    members = devices * slots
    grid_spec = pltpu.PrefetchScalarGridSpec(
        num_scalar_prefetch=1,
        grid=(1,),
        in_specs=[pl.BlockSpec(memory_space=pl.ANY)],
        out_specs=pl.BlockSpec((devices, slots, row_count, bottleneck), lambda i, ml: (0, 0, 0, 0)),
        scratch_shapes=[pltpu.SemaphoreType.DMA((members,))],
    )
    size = members * row_count * bottleneck * 2
    return pl.pallas_call(
        functools.partial(gather_kernel, slots=slots),
        grid_spec=grid_spec,
        out_shape=jax.ShapeDtypeStruct((devices, slots, row_count, bottleneck), jnp.bfloat16),
        compiler_params=pltpu.CompilerParams(vmem_limit_bytes=48 * 1024 * 1024),
        cost_estimate=pl.CostEstimate(flops=0, bytes_accessed=2 * size, transcendentals=0),
    )(slot_lang.reshape(-1), weight)


def _layouts(got):
    devices, slots, row_count, bottleneck = got.shape
    width = devices * row_count
    direct = row_count % 16 == 0
    if direct:
        weights = got
        w_spec = pl.BlockSpec((devices, 1, row_count, bottleneck), lambda u, sl, ln: (0, sl[u], 0, 0))
        g_shape = (devices, slots, row_count, bottleneck)
        g_spec = pl.BlockSpec(g_shape, lambda u, sl, ln: (0, 0, 0, 0))
    else:
        weights = got.transpose(1, 0, 2, 3).reshape(slots, width, bottleneck)
        w_spec = pl.BlockSpec((1, width, bottleneck), lambda u, sl, ln: (sl[u], 0, 0))
        g_shape = (slots, width, bottleneck)
        g_spec = pl.BlockSpec(g_shape, lambda u, sl, ln: (0, 0, 0))
    return direct, weights, w_spec, g_shape, g_spec


def _to_send(grads, got_shape, direct):
    if direct:
        return grads
    devices, slots, row_count, bottleneck = got_shape
    return grads.reshape(slots, devices, row_count, bottleneck).transpose(1, 0, 2, 3)


def _utt_spec(frame_count, width):
    return pl.BlockSpec((1, frame_count, width), lambda u, sl, ln: (u, 0, 0))


def forward_pass(frames, cotangent, gain, got_down, own_slot, own_lengths, own_scale):
    utts, frame_count, width = frames.shape
    slots, bottleneck = got_down.shape[1], got_down.shape[3]
    direct, w_down, w_spec, g_shape, g_spec = _layouts(got_down)
    grid_spec = pltpu.PrefetchScalarGridSpec(
        num_scalar_prefetch=2,
        grid=(utts,),
        in_specs=[
            _utt_spec(frame_count, width),
            _utt_spec(frame_count, width),
            pl.BlockSpec((1, width), lambda u, sl, ln: (0, 0)),
            w_spec,
            pl.BlockSpec((slots, 1, 1), lambda u, sl, ln: (0, 0, 0)),
        ],
        out_specs=[
            pl.BlockSpec((1, frame_count, bottleneck), lambda u, sl, ln: (u, 0, 0)),
            g_spec,
        ],
        scratch_shapes=[pltpu.VMEM((slots, width, bottleneck), jnp.float32)],
    )
    pre_act, grads = pl.pallas_call(
        functools.partial(forward_kernel, direct=direct),
        grid_spec=grid_spec,
        out_shape=[
            jax.ShapeDtypeStruct((utts, frame_count, bottleneck), jnp.float32),
            jax.ShapeDtypeStruct(g_shape, jnp.bfloat16),
        ],
        compiler_params=pltpu.CompilerParams(
            dimension_semantics=("arbitrary",), vmem_limit_bytes=60 * 1024 * 1024
        ),
        cost_estimate=pl.CostEstimate(
            flops=4 * utts * frame_count * width * bottleneck,
            bytes_accessed=2 * frames.size * 2 + utts * width * bottleneck * 2,
            transcendentals=utts * frame_count * bottleneck,
        ),
    )(own_slot, own_lengths, frames, cotangent, gain.reshape(1, width), w_down,
      own_scale.reshape(slots, 1, 1))
    return pre_act, _to_send(grads, got_down.shape, direct)


def backward_pass(frames, cotangent, gain, got_down, got_up, pre_act, own_slot, own_lengths,
                  own_scale):
    utts, frame_count, width = frames.shape
    slots, bottleneck = got_down.shape[1], got_down.shape[3]
    direct, w_down, w_spec, g_shape, g_spec = _layouts(got_down)
    _, w_up, _, _, _ = _layouts(got_up)
    grid_spec = pltpu.PrefetchScalarGridSpec(
        num_scalar_prefetch=2,
        grid=(utts,),
        in_specs=[
            _utt_spec(frame_count, width),
            _utt_spec(frame_count, width),
            pl.BlockSpec((1, width), lambda u, sl, ln: (0, 0)),
            w_spec,
            w_spec,
            pl.BlockSpec((1, frame_count, bottleneck), lambda u, sl, ln: (u, 0, 0)),
            pl.BlockSpec((slots, 1, 1), lambda u, sl, ln: (0, 0, 0)),
        ],
        out_specs=[_utt_spec(frame_count, width), g_spec],
        scratch_shapes=[pltpu.VMEM((slots, width, bottleneck), jnp.float32)],
    )
    d_frames, grads = pl.pallas_call(
        functools.partial(backward_kernel, direct=direct),
        grid_spec=grid_spec,
        out_shape=[
            jax.ShapeDtypeStruct(frames.shape, jnp.bfloat16),
            jax.ShapeDtypeStruct(g_shape, jnp.bfloat16),
        ],
        compiler_params=pltpu.CompilerParams(
            dimension_semantics=("arbitrary",), vmem_limit_bytes=60 * 1024 * 1024
        ),
        cost_estimate=pl.CostEstimate(
            flops=6 * utts * frame_count * width * bottleneck,
            bytes_accessed=3 * frames.size * 2 + 2 * utts * width * bottleneck * 2,
            transcendentals=utts * frame_count * bottleneck,
        ),
    )(own_slot, own_lengths, frames, cotangent, gain.reshape(1, width), w_down, w_up, pre_act,
      own_scale.reshape(slots, 1, 1))
    return d_frames, _to_send(grads, got_down.shape, direct)


def on_device(frames, cotangent, gain, down_weight, up_weight, slot_lang, utt_slot, lengths):
    devices = lax.axis_size("dp")
    self_index = lax.axis_index("dp")
    per_device = frames.shape[0]
    slots = slot_lang.shape[1]
    lang_count, row_count, bottleneck = down_weight.shape
    owners = jnp.arange(utt_slot.shape[0], dtype=jnp.int32) // per_device
    utt_lang = slot_lang[owners, utt_slot]
    own_lengths = lax.dynamic_slice_in_dim(lengths, self_index * per_device, per_device)
    own_slot = lax.dynamic_slice_in_dim(utt_slot, self_index * per_device, per_device)
    lang_ids = jnp.arange(lang_count, dtype=jnp.int32)
    counts = jnp.sum(jnp.where(utt_lang[None, :] == lang_ids[:, None], lengths[None, :], 0), axis=1)
    scaling = lax.rsqrt(jnp.maximum(counts, 1).astype(jnp.float32))
    member_langs = slot_lang.reshape(-1)
    own_scale = jnp.take(scaling, lax.dynamic_index_in_dim(slot_lang, self_index, 0, False))
    def exchange(x):
        flat = x.reshape(x.shape[0], x.shape[1] * x.shape[2], x.shape[3])
        moved = lax.all_to_all(flat, "dp", split_axis=0, concat_axis=0, tiled=True)
        return moved.reshape(x.shape)

    got_down = exchange(gather_rows(slot_lang, down_weight))
    got_up = exchange(gather_rows(slot_lang, up_weight))
    pre_act, send_up = forward_pass(
        frames, cotangent, gain, got_down, own_slot, own_lengths, own_scale
    )
    back_up = exchange(send_up).reshape(devices * slots, row_count, bottleneck)
    d_frames, send_down = backward_pass(
        frames, cotangent, gain, got_down, got_up, pre_act, own_slot, own_lengths, own_scale
    )
    send_down, back_up = lax.optimization_barrier((send_down, back_up))
    back_down = exchange(send_down).reshape(devices * slots, row_count, bottleneck)
    plan = combine_plan(slot_lang, lang_count)
    up_grads, zeros = combine(plan, back_up, lang_count, with_zeros=True)
    down_grads = scatter_combine(plan, back_down, zeros)
    return (d_frames, down_grads, up_grads)


def solution(mesh):
    placed = (
        P(("groups", "dp"), None, None),
        P(("groups", "dp"), None, None),
        P(),
        P("groups", "dp", None),
        P("groups", "dp", None),
        P("groups", None),
        P("groups"),
        P("groups"),
    )
    return jax.shard_map(
        on_device,
        mesh=mesh,
        in_specs=placed,
        out_specs=(
            P(("groups", "dp"), None, None),
            P("groups", "dp", None),
            P("groups", "dp", None),
        ),
        check_vma=False,
    )
```

```python
import functools

import jax
import jax.numpy as jnp
from jax import lax
from jax.experimental import pallas as pl
from jax.experimental.pallas import tpu as pltpu
from jax.sharding import PartitionSpec as P


def _weights(ref, direct):
    if direct:
        devices, _, row_count, bottleneck = ref.shape
        return ref[:, 0].reshape(devices * row_count, bottleneck)
    return ref[0]


def _flush(acc_ref, scale_ref, out_ref, direct):
    if direct:
        devices, slots, row_count, _ = out_ref.shape
        for dev in range(devices):
            rows = pl.ds(dev * row_count, row_count)
            out_ref[dev] = (acc_ref[:, rows, :] * scale_ref[...]).astype(out_ref.dtype)
    else:
        out_ref[...] = (acc_ref[...] * scale_ref[...]).astype(out_ref.dtype)


def _normalize(frames_ref, gain):
    values = frames_ref[0].astype(jnp.float32)
    centre_mean = jnp.mean(values, axis=1, keepdims=True)
    mean_removed = values - centre_mean
    variance = jnp.mean(mean_removed * mean_removed, axis=1, keepdims=True)
    reciprocal_deviation = lax.rsqrt(variance + 1e-06)
    standardized_input = mean_removed * reciprocal_deviation
    layer_normed = (standardized_input * gain).astype(jnp.bfloat16)
    return reciprocal_deviation, standardized_input, layer_normed


def _masked(cot_ref, length):
    upstream = cot_ref[0]
    live = lax.broadcasted_iota(jnp.int32, (upstream.shape[0], 1), 0) < length
    return upstream, jnp.where(live, upstream, jnp.zeros_like(upstream))


CONTRACT_ROWS = (((0,), (0,)), ((), ()))


def forward_kernel(slot_ref, len_ref, frames_ref, cot_ref, gain_ref, wd_ref, scale_ref,
                   pre_ref, gu_out, gu_ref, *, direct):
    u = pl.program_id(0)

    @pl.when(u == 0)
    def _():
        gu_ref[...] = jnp.zeros_like(gu_ref)

    slot = slot_ref[u]
    _, _, layer_normed = _normalize(frames_ref, gain_ref[...])
    pre_act = jnp.dot(layer_normed, _weights(wd_ref, direct), preferred_element_type=jnp.float32)
    pre_ref[0] = pre_act
    sigmoid_pre = 1.0 / (1.0 + jnp.exp(-pre_act))
    hidden = (pre_act * sigmoid_pre).astype(jnp.bfloat16)
    _, masked_up = _masked(cot_ref, len_ref[u])
    gu_ref[slot] += lax.dot_general(
        masked_up, hidden, CONTRACT_ROWS, preferred_element_type=jnp.float32
    )

    @pl.when(u == pl.num_programs(0) - 1)
    def _():
        _flush(gu_ref, scale_ref, gu_out, direct)


def backward_kernel(slot_ref, len_ref, frames_ref, cot_ref, gain_ref, wd_ref, wu_ref, pre_ref,
                    scale_ref, out_ref, gd_out, gd_ref, *, direct):
    u = pl.program_id(0)

    @pl.when(u == 0)
    def _():
        gd_ref[...] = jnp.zeros_like(gd_ref)

    slot = slot_ref[u]
    gain = gain_ref[...]
    reciprocal_deviation, standardized_input, layer_normed = _normalize(frames_ref, gain)
    pre_act = pre_ref[0]
    sigmoid_pre = 1.0 / (1.0 + jnp.exp(-pre_act))
    upstream, masked_up = _masked(cot_ref, len_ref[u])
    d_hidden = jnp.dot(masked_up, _weights(wu_ref, direct), preferred_element_type=jnp.float32)
    d_pre = (d_hidden * sigmoid_pre * (1.0 + pre_act * (1.0 - sigmoid_pre))).astype(jnp.bfloat16)
    gd_ref[slot] += lax.dot_general(
        layer_normed, d_pre, CONTRACT_ROWS, preferred_element_type=jnp.float32
    )
    d_normed = lax.dot_general(
        d_pre, _weights(wd_ref, direct), (((1,), (1,)), ((), ())),
        preferred_element_type=jnp.float32,
    )
    scaled_rows = d_normed * gain
    inner_gradient = (
        scaled_rows
        - jnp.mean(scaled_rows, axis=1, keepdims=True)
        - standardized_input * jnp.mean(scaled_rows * standardized_input, axis=1, keepdims=True)
    ) * reciprocal_deviation
    out_ref[0] = (upstream.astype(jnp.float32) + inner_gradient).astype(out_ref.dtype)

    @pl.when(u == pl.num_programs(0) - 1)
    def _():
        _flush(gd_ref, scale_ref, gd_out, direct)


def combine_kernel(order_ref, lang_ref, start_ref, back_ref, out_ref, *rest):
    acc_ref = rest[-1]
    if len(rest) == 2:
        rest[0][...] = jnp.zeros_like(rest[0])
    block = out_ref.shape[0]
    b = pl.program_id(0)
    base = b * block
    out_ref[...] = jnp.zeros_like(out_ref)
    first_at = start_ref[b]
    end_at = start_ref[b + 1]
    last_member = lang_ref.shape[0] - 1

    def add_member(i, carry):
        m = order_ref[i]
        lang = lang_ref[i]
        first = (i == first_at) | (lang_ref[jnp.maximum(i - 1, 0)] != lang)
        last = (i == end_at - 1) | (lang_ref[jnp.minimum(i + 1, last_member)] != lang)
        val = back_ref[m].astype(jnp.float32)

        @pl.when(first)
        def _():
            acc_ref[...] = val

        @pl.when(jnp.logical_not(first))
        def _():
            acc_ref[...] += val

        @pl.when(last)
        def _():
            out_ref[lang - base] = acc_ref[...].astype(out_ref.dtype)

        return carry

    lax.fori_loop(first_at, end_at, add_member, 0)


def scatter_kernel(order_ref, lang_ref, back_ref, zeros_hbm, out_hbm, acc_ref, stage_ref, sems):
    del zeros_hbm
    members = lang_ref.shape[0]
    last_member = members - 1

    def run_end(i):
        return (i == last_member) | (lang_ref[jnp.minimum(i + 1, last_member)] != lang_ref[i])

    def copy(i):
        return pltpu.make_async_copy(stage_ref.at[i], out_hbm.at[lang_ref[i]], sems.at[i])

    def add_member(i, carry):
        first = (i == 0) | (lang_ref[jnp.maximum(i - 1, 0)] != lang_ref[i])
        val = back_ref[order_ref[i]].astype(jnp.float32)

        @pl.when(first)
        def _():
            acc_ref[...] = val

        @pl.when(jnp.logical_not(first))
        def _():
            acc_ref[...] += val

        @pl.when(run_end(i))
        def _():
            stage_ref[i] = acc_ref[...].astype(stage_ref.dtype)
            copy(i).start()

        return carry

    def finish(i, carry):
        @pl.when(run_end(i))
        def _():
            copy(i).wait()

        return carry

    lax.fori_loop(0, members, add_member, 0)
    lax.fori_loop(0, members, finish, 0)


def scatter_combine(plan, back, zeros):
    _, order, sorted_langs, _ = plan
    members, row_count, bottleneck = back.shape
    lang_count = zeros.shape[0]
    grid_spec = pltpu.PrefetchScalarGridSpec(
        num_scalar_prefetch=2,
        grid=(1,),
        in_specs=[
            pl.BlockSpec((members, row_count, bottleneck), lambda i, o, l: (0, 0, 0)),
            pl.BlockSpec(memory_space=pl.ANY),
        ],
        out_specs=pl.BlockSpec(memory_space=pl.ANY),
        scratch_shapes=[
            pltpu.VMEM((row_count, bottleneck), jnp.float32),
            pltpu.VMEM((members, row_count, bottleneck), jnp.bfloat16),
            pltpu.SemaphoreType.DMA((members,)),
        ],
    )
    return pl.pallas_call(
        scatter_kernel,
        grid_spec=grid_spec,
        out_shape=jax.ShapeDtypeStruct((lang_count, row_count, bottleneck), jnp.bfloat16),
        input_output_aliases={3: 0},
        compiler_params=pltpu.CompilerParams(vmem_limit_bytes=48 * 1024 * 1024),
        cost_estimate=pl.CostEstimate(
            flops=back.size, bytes_accessed=back.size * 4, transcendentals=0
        ),
    )(order, sorted_langs, back, zeros)


def combine_plan(slot_lang, lang_count):
    block = 32 if lang_count % 32 == 0 else (8 if lang_count % 8 == 0 else 1)
    langs = slot_lang.reshape(-1)
    order = jnp.argsort(langs, stable=True).astype(jnp.int32)
    sorted_langs = langs[order].astype(jnp.int32)
    edges = jnp.arange(lang_count // block + 1, dtype=jnp.int32) * block
    starts = jnp.sum((sorted_langs[None, :] < edges[:, None]).astype(jnp.int32), axis=1)
    return block, order, sorted_langs, starts


def combine(plan, back, lang_count, with_zeros=False):
    block, order, sorted_langs, starts = plan
    members, row_count, bottleneck = back.shape
    outputs = 2 if with_zeros else 1
    out_spec = pl.BlockSpec((block, row_count, bottleneck), lambda b, o, l, st: (b, 0, 0))
    out_shape = jax.ShapeDtypeStruct((lang_count, row_count, bottleneck), jnp.bfloat16)
    grid_spec = pltpu.PrefetchScalarGridSpec(
        num_scalar_prefetch=3,
        grid=(lang_count // block,),
        in_specs=[pl.BlockSpec((members, row_count, bottleneck), lambda b, o, l, st: (0, 0, 0))],
        out_specs=[out_spec] * outputs,
        scratch_shapes=[pltpu.VMEM((row_count, bottleneck), jnp.float32)],
    )
    result = pl.pallas_call(
        combine_kernel,
        grid_spec=grid_spec,
        out_shape=[out_shape] * outputs,
        compiler_params=pltpu.CompilerParams(
            dimension_semantics=("arbitrary",), vmem_limit_bytes=48 * 1024 * 1024
        ),
        cost_estimate=pl.CostEstimate(
            flops=back.size,
            bytes_accessed=back.size * 2 + outputs * lang_count * row_count * bottleneck * 2,
            transcendentals=0,
        ),
    )(order, sorted_langs, starts, back)
    return tuple(result) if with_zeros else result[0]


def gather_kernel(lang_ref, weight_hbm, out_ref, sems, *, slots):
    members = lang_ref.shape[0]

    def copy(m):
        return pltpu.make_async_copy(
            weight_hbm.at[lang_ref[m]], out_ref.at[m // slots, m % slots], sems.at[m]
        )

    def start(m, carry):
        copy(m).start()
        return carry

    def finish(m, carry):
        copy(m).wait()
        return carry

    lax.fori_loop(0, members, start, 0)
    lax.fori_loop(0, members, finish, 0)


def gather_rows(slot_lang, weight):
    devices, slots = slot_lang.shape
    _, row_count, bottleneck = weight.shape
    members = devices * slots
    grid_spec = pltpu.PrefetchScalarGridSpec(
        num_scalar_prefetch=1,
        grid=(1,),
        in_specs=[pl.BlockSpec(memory_space=pl.ANY)],
        out_specs=pl.BlockSpec((devices, slots, row_count, bottleneck), lambda i, ml: (0, 0, 0, 0)),
        scratch_shapes=[pltpu.SemaphoreType.DMA((members,))],
    )
    size = members * row_count * bottleneck * 2
    return pl.pallas_call(
        functools.partial(gather_kernel, slots=slots),
        grid_spec=grid_spec,
        out_shape=jax.ShapeDtypeStruct((devices, slots, row_count, bottleneck), jnp.bfloat16),
        compiler_params=pltpu.CompilerParams(vmem_limit_bytes=48 * 1024 * 1024),
        cost_estimate=pl.CostEstimate(flops=0, bytes_accessed=2 * size, transcendentals=0),
    )(slot_lang.reshape(-1), weight)


def _layouts(got):
    devices, slots, row_count, bottleneck = got.shape
    width = devices * row_count
    direct = row_count % 16 == 0
    if direct:
        weights = got
        w_spec = pl.BlockSpec((devices, 1, row_count, bottleneck), lambda u, sl, ln: (0, sl[u], 0, 0))
        g_shape = (devices, slots, row_count, bottleneck)
        g_spec = pl.BlockSpec(g_shape, lambda u, sl, ln: (0, 0, 0, 0))
    else:
        weights = got.transpose(1, 0, 2, 3).reshape(slots, width, bottleneck)
        w_spec = pl.BlockSpec((1, width, bottleneck), lambda u, sl, ln: (sl[u], 0, 0))
        g_shape = (slots, width, bottleneck)
        g_spec = pl.BlockSpec(g_shape, lambda u, sl, ln: (0, 0, 0))
    return direct, weights, w_spec, g_shape, g_spec


def _to_send(grads, got_shape, direct):
    if direct:
        return grads
    devices, slots, row_count, bottleneck = got_shape
    return grads.reshape(slots, devices, row_count, bottleneck).transpose(1, 0, 2, 3)


def _utt_spec(frame_count, width):
    return pl.BlockSpec((1, frame_count, width), lambda u, sl, ln: (u, 0, 0))


def forward_pass(frames, cotangent, gain, got_down, own_slot, own_lengths, own_scale):
    utts, frame_count, width = frames.shape
    slots, bottleneck = got_down.shape[1], got_down.shape[3]
    direct, w_down, w_spec, g_shape, g_spec = _layouts(got_down)
    grid_spec = pltpu.PrefetchScalarGridSpec(
        num_scalar_prefetch=2,
        grid=(utts,),
        in_specs=[
            _utt_spec(frame_count, width),
            _utt_spec(frame_count, width),
            pl.BlockSpec((1, width), lambda u, sl, ln: (0, 0)),
            w_spec,
            pl.BlockSpec((slots, 1, 1), lambda u, sl, ln: (0, 0, 0)),
        ],
        out_specs=[
            pl.BlockSpec((1, frame_count, bottleneck), lambda u, sl, ln: (u, 0, 0)),
            g_spec,
        ],
        scratch_shapes=[pltpu.VMEM((slots, width, bottleneck), jnp.float32)],
    )
    pre_act, grads = pl.pallas_call(
        functools.partial(forward_kernel, direct=direct),
        grid_spec=grid_spec,
        out_shape=[
            jax.ShapeDtypeStruct((utts, frame_count, bottleneck), jnp.float32),
            jax.ShapeDtypeStruct(g_shape, jnp.bfloat16),
        ],
        compiler_params=pltpu.CompilerParams(
            dimension_semantics=("arbitrary",), vmem_limit_bytes=60 * 1024 * 1024
        ),
        cost_estimate=pl.CostEstimate(
            flops=4 * utts * frame_count * width * bottleneck,
            bytes_accessed=2 * frames.size * 2 + utts * width * bottleneck * 2,
            transcendentals=utts * frame_count * bottleneck,
        ),
    )(own_slot, own_lengths, frames, cotangent, gain.reshape(1, width), w_down,
      own_scale.reshape(slots, 1, 1))
    return pre_act, _to_send(grads, got_down.shape, direct)


def backward_pass(frames, cotangent, gain, got_down, got_up, pre_act, own_slot, own_lengths,
                  own_scale):
    utts, frame_count, width = frames.shape
    slots, bottleneck = got_down.shape[1], got_down.shape[3]
    direct, w_down, w_spec, g_shape, g_spec = _layouts(got_down)
    _, w_up, _, _, _ = _layouts(got_up)
    grid_spec = pltpu.PrefetchScalarGridSpec(
        num_scalar_prefetch=2,
        grid=(utts,),
        in_specs=[
            _utt_spec(frame_count, width),
            _utt_spec(frame_count, width),
            pl.BlockSpec((1, width), lambda u, sl, ln: (0, 0)),
            w_spec,
            w_spec,
            pl.BlockSpec((1, frame_count, bottleneck), lambda u, sl, ln: (u, 0, 0)),
            pl.BlockSpec((slots, 1, 1), lambda u, sl, ln: (0, 0, 0)),
        ],
        out_specs=[_utt_spec(frame_count, width), g_spec],
        scratch_shapes=[pltpu.VMEM((slots, width, bottleneck), jnp.float32)],
    )
    d_frames, grads = pl.pallas_call(
        functools.partial(backward_kernel, direct=direct),
        grid_spec=grid_spec,
        out_shape=[
            jax.ShapeDtypeStruct(frames.shape, jnp.bfloat16),
            jax.ShapeDtypeStruct(g_shape, jnp.bfloat16),
        ],
        compiler_params=pltpu.CompilerParams(
            dimension_semantics=("arbitrary",), vmem_limit_bytes=60 * 1024 * 1024
        ),
        cost_estimate=pl.CostEstimate(
            flops=6 * utts * frame_count * width * bottleneck,
            bytes_accessed=3 * frames.size * 2 + 2 * utts * width * bottleneck * 2,
            transcendentals=utts * frame_count * bottleneck,
        ),
    )(own_slot, own_lengths, frames, cotangent, gain.reshape(1, width), w_down, w_up, pre_act,
      own_scale.reshape(slots, 1, 1))
    return d_frames, _to_send(grads, got_down.shape, direct)


def on_device(frames, cotangent, gain, down_weight, up_weight, slot_lang, utt_slot, lengths):
    devices = lax.axis_size("dp")
    self_index = lax.axis_index("dp")
    per_device = frames.shape[0]
    slots = slot_lang.shape[1]
    lang_count, row_count, bottleneck = down_weight.shape
    owners = jnp.arange(utt_slot.shape[0], dtype=jnp.int32) // per_device
    utt_lang = slot_lang[owners, utt_slot]
    own_lengths = lax.dynamic_slice_in_dim(lengths, self_index * per_device, per_device)
    own_slot = lax.dynamic_slice_in_dim(utt_slot, self_index * per_device, per_device)
    lang_ids = jnp.arange(lang_count, dtype=jnp.int32)
    counts = jnp.sum(jnp.where(utt_lang[None, :] == lang_ids[:, None], lengths[None, :], 0), axis=1)
    scaling = lax.rsqrt(jnp.maximum(counts, 1).astype(jnp.float32))
    member_langs = slot_lang.reshape(-1)
    own_scale = jnp.take(scaling, lax.dynamic_index_in_dim(slot_lang, self_index, 0, False))
    exchange = functools.partial(lax.all_to_all, axis_name="dp", split_axis=0, concat_axis=0, tiled=True)
    got = exchange(
        jnp.concatenate(
            [gather_rows(slot_lang, down_weight), gather_rows(slot_lang, up_weight)], axis=1
        )
    )
    got_down = got[:, :slots]
    got_up = got[:, slots:]
    pre_act, send_up = forward_pass(
        frames, cotangent, gain, got_down, own_slot, own_lengths, own_scale
    )
    back_up = exchange(send_up).reshape(devices * slots, row_count, bottleneck)
    d_frames, send_down = backward_pass(
        frames, cotangent, gain, got_down, got_up, pre_act, own_slot, own_lengths, own_scale
    )
    send_down, back_up = lax.optimization_barrier((send_down, back_up))
    back_down = exchange(send_down).reshape(devices * slots, row_count, bottleneck)
    plan = combine_plan(slot_lang, lang_count)
    up_grads, zeros = combine(plan, back_up, lang_count, with_zeros=True)
    down_grads = scatter_combine(plan, back_down, zeros)
    return (d_frames, down_grads, up_grads)


def solution(mesh):
    placed = (
        P(("groups", "dp"), None, None),
        P(("groups", "dp"), None, None),
        P(),
        P("groups", "dp", None),
        P("groups", "dp", None),
        P("groups", None),
        P("groups"),
        P("groups"),
    )
    return jax.shard_map(
        on_device,
        mesh=mesh,
        in_specs=placed,
        out_specs=(
            P(("groups", "dp"), None, None),
            P("groups", "dp", None),
            P("groups", "dp", None),
        ),
        check_vma=False,
    )
```
